32 devices in a mesh: slab: 2 (over y), frame: 4 (over z), coil: 4 (over x, core).
Axes of the slice: x: 2, y: 2, z: 4, core: 2. Of those that a mesh axis runs over, the one named last changes fastest.
Arguments:
- factors: float32 [4, 16, 256, 256], P('slab', None, 'coil', 'frame'), parts along dimension 0, may hold values from -3 to 3
- temporal: float32 [4, 4, 16], P('slab'), parts along dimension 0, may hold values from -3 to 3
- maps: bfloat16 [32, 512, 512], P('coil', 'slab'), parts along dimension 1, may hold values from -1 to 1
- kdata: bfloat16 [4, 32, 512, 512], P('frame', 'coil', 'slab'), parts along dimension 2, may hold values from -1.5 to 1.5
- masks: int32 [4, 32, 512], P('frame', 'coil', 'slab'), parts along dimension 2, may hold values 0 or 1
Outputs:
- new_factors: float32 [4, 16, 256, 256], P('slab', None, 'coil', 'frame'), parts along dimension 0
The draws below stay inside these ranges and needn't reach their ends.
There are 2 independent parts, one for each index of `slab`. The reference program is written for one: setup_inputs(seed, part) draws one part's arguments, and reference() takes and returns one part's arrays. A program takes and returns all parts, laid end to end along the dimension named above; each array names one. Nothing has to cross between parts.
All inputs are finite; a program needn't handle non-finite values. No bound on the sum of `masks` on one device may be relied on, other than what follows from the above.
Results may differ from the reference program's by a relative error of at most 0.0085.
Values may be sent and summed in bfloat16 or wider, within the bound.
No kernel may reach another device: no remote copies, remote signals or barrier semaphores. Data moves between devices by JAX's collectives and lax.ppermute only.
A program may use at most 64 MiB of HBM per device.

```python
import math
import jax
import jax.numpy as jnp
from jax import lax

NX = 256
NY = 256
COILS = 32
RANK = 16
FRAMES = 4


def with_ends(result, rng, smallest, high):
    spot = [jax.random.randint(jax.random.fold_in(rng, axis), (), 0, length) for axis, length in enumerate(result.shape)]
    main_axis = result.shape.index(max(result.shape))
    neighbour = spot[:main_axis] + [(spot[main_axis] + 1) % result.shape[main_axis]] + spot[main_axis + 1:]
    return result.at[tuple(spot)].set(smallest).at[tuple(neighbour)].set(high)


def level_of(rng, extent, pieces, least, high):
    def one(position, shards_of):
        heights = jax.random.uniform(jax.random.fold_in(jax.random.fold_in(rng, 6), position), (shards_of,), jnp.float32, least / len(pieces), high / len(pieces))
        return jnp.repeat(jnp.exp(heights), extent[position] // shards_of).reshape((-1,) + (1,) * (len(extent) - position - 1))

    loudness = one(*pieces[0])
    for cut in pieces[1:]:
        loudness = loudness * one(*cut)
    return loudness


def noise(own_key, dims, deviation, most, split=(), held_as=jnp.bfloat16):
    values = jax.random.normal(own_key, dims, jnp.float32) * deviation
    if len(split) > 0:
        values = level_of(own_key, dims, split, -0.22, 0.18) * values
    return jnp.clip(values, min=-most, max=most).astype(held_as)


def setup_inputs(seed: int = 0, part: int = 0) -> dict:
    key_list = jax.random.split(jax.random.key(seed), 6)
    own_keys = jax.random.split(jax.random.fold_in(key_list[5], part), 6)
    factors = noise(own_keys[0], (2, RANK, NY, NX), 0.5, 3.0, ((2, 4), (3, 4)), jnp.float32)
    temporal = noise(own_keys[1], (2, FRAMES, RANK), 0.5, 3.0, (), jnp.float32)
    maps = noise(own_keys[2], (COILS, NY, 2 * NX), COILS ** -0.5, 1.0, ((0, 4),))
    kdata = noise(own_keys[3], (FRAMES, COILS, NY, 2 * NX), 0.25, 1.5, ((0, 4), (1, 4)))
    masks = with_ends((jax.random.randint(own_keys[4], (FRAMES, COILS, NY), 0, 3) < 1).astype(jnp.int32), jax.random.fold_in(own_keys[4], 1), 0, 1)
    return dict(factors=factors, temporal=temporal, maps=maps, kdata=kdata, masks=masks)


def rounded(value):
    return lax.optimization_barrier(value.astype(jnp.bfloat16)).astype(jnp.float32)

def dft_table(length):
    index = jnp.arange(length, dtype=jnp.int32)
    phase = index[:, None] * index[None, :] % length
    angle = 2.0 * math.pi / length * phase.astype(jnp.float32)
    scale = 1.0 / math.sqrt(length)
    return (rounded(jnp.cos(angle) * scale), rounded(-jnp.sin(angle) * scale))

def product(form, first, second):
    return jnp.einsum(form, first, second, precision=lax.Precision.HIGHEST)

def reference(factors, temporal, maps, kdata, masks):
    left_re = factors[0]
    left_im = factors[1]
    time_re = temporal[0]
    time_im = temporal[1]
    image_re = rounded(product('tr,ryx->tyx', time_re, left_re) - product('tr,ryx->tyx', time_im, left_im))
    image_im = rounded(product('tr,ryx->tyx', time_im, left_re) + product('tr,ryx->tyx', time_re, left_im))
    table_x_re, table_x_im = dft_table(NX)
    table_y_re, table_y_im = dft_table(NY)
    maps_wide = maps.astype(jnp.float32)
    sens_re = maps_wide[:, :, :NX]
    sens_im = maps_wide[:, :, NX:]

    def one_frame(inputs):
        frame_re, frame_im, measured, sampled = inputs
        coil_re = rounded(sens_re * frame_re[None] - sens_im * frame_im[None])
        coil_im = rounded(sens_re * frame_im[None] + sens_im * frame_re[None])
        half_re = rounded(product('cyx,xk->cyk', coil_re, table_x_re) - product('cyx,xk->cyk', coil_im, table_x_im))
        half_im = rounded(product('cyx,xk->cyk', coil_re, table_x_im) + product('cyx,xk->cyk', coil_im, table_x_re))
        kspace_re = product('ky,cyn->ckn', table_y_re, half_re) - product('ky,cyn->ckn', table_y_im, half_im)
        kspace_im = product('ky,cyn->ckn', table_y_re, half_im) + product('ky,cyn->ckn', table_y_im, half_re)
        measured_wide = measured.astype(jnp.float32)
        weight = sampled.astype(jnp.float32)[:, :, None]
        resid_re = rounded(weight * (kspace_re - measured_wide[:, :, :NX]))
        resid_im = rounded(weight * (kspace_im - measured_wide[:, :, NX:]))
        back_re = rounded(product('ky,ckn->cyn', table_y_re, resid_re) + product('ky,ckn->cyn', table_y_im, resid_im))
        back_im = rounded(product('ky,ckn->cyn', table_y_re, resid_im) - product('ky,ckn->cyn', table_y_im, resid_re))
        coil_back_re = product('cyk,xk->cyx', back_re, table_x_re) + product('cyk,xk->cyx', back_im, table_x_im)
        coil_back_im = product('cyk,xk->cyx', back_im, table_x_re) - product('cyk,xk->cyx', back_re, table_x_im)
        summed_re = lax.optimization_barrier(jnp.sum(sens_re * coil_back_re + sens_im * coil_back_im, axis=0))
        summed_im = lax.optimization_barrier(jnp.sum(sens_re * coil_back_im - sens_im * coil_back_re, axis=0))
        return (summed_re, summed_im)
    back_re, back_im = lax.map(one_frame, (image_re, image_im, kdata, masks))
    grad_re = product('tr,tyx->ryx', time_re, back_re) + product('tr,tyx->ryx', time_im, back_im)
    grad_im = product('tr,tyx->ryx', time_re, back_im) - product('tr,tyx->ryx', time_im, back_re)
    return factors - 0.5 * jnp.stack([grad_re, grad_im])
```

```python
import math

import jax
import jax.numpy as jnp
from jax import lax
from jax.sharding import PartitionSpec as P


def dft_parts(length):
    index = jnp.arange(length, dtype=jnp.int32)
    phase = index[:, None] * index[None, :] % length
    angle = 2.0 * math.pi / length * phase.astype(jnp.float32)
    scale = 1.0 / math.sqrt(length)
    return (
        (jnp.cos(angle) * scale).astype(jnp.bfloat16),
        (-jnp.sin(angle) * scale).astype(jnp.bfloat16),
    )


def rotate_plus(values, half_width):
    return jnp.concatenate([-values[..., half_width:], values[..., :half_width]], axis=-1)


def rotate_minus(values, half_width):
    return jnp.concatenate([values[..., half_width:], -values[..., :half_width]], axis=-1)


def sens_times(sens, values, half_width):
    sens_re = sens[..., :half_width].astype(jnp.float32)
    sens_im = sens[..., half_width:].astype(jnp.float32)
    value_re = values[..., :half_width].astype(jnp.float32)
    value_im = values[..., half_width:].astype(jnp.float32)
    return jnp.concatenate(
        [sens_re * value_re - sens_im * value_im, sens_re * value_im + sens_im * value_re], axis=-1
    )


def conj_sens_times(sens, values, half_width):
    sens_re = sens[..., :half_width].astype(jnp.float32)
    sens_im = sens[..., half_width:].astype(jnp.float32)
    value_re = values[..., :half_width]
    value_im = values[..., half_width:]
    return jnp.concatenate(
        [sens_re * value_re + sens_im * value_im, sens_re * value_im - sens_im * value_re], axis=-1
    )


def precise(form, first, second):
    return jnp.einsum(form, first, second, precision=lax.Precision.HIGHEST)


PERMUTE_LIMIT = 8


def shifted(count, step):
    return [(source, (source + step) % count) for source in range(count)]


def by_sender(pieces, count, me):
    ring = jnp.stack([pieces[0]] + pieces[1:][::-1])
    doubled = jnp.concatenate([ring, ring], axis=0)
    return lax.dynamic_slice_in_dim(doubled, (count - me) % count, count, 0)


def gather_blocks(value, axis):
    count = lax.axis_size(axis)
    if count > PERMUTE_LIMIT:
        return lax.all_gather(value, axis)
    me = lax.axis_index(axis)
    pieces = [value] + [lax.ppermute(value, axis, shifted(count, step)) for step in range(1, count)]
    return by_sender(pieces, count, me)


def exchange_blocks(blocks, axis):
    count = lax.axis_size(axis)
    if count > PERMUTE_LIMIT:
        return lax.all_to_all(blocks, axis, 0, 0, tiled=True)
    me = lax.axis_index(axis)
    pieces = [lax.dynamic_index_in_dim(blocks, me, 0, keepdims=False)]
    for step in range(1, count):
        outgoing = lax.dynamic_index_in_dim(blocks, (me + step) % count, 0, keepdims=False)
        pieces.append(lax.ppermute(outgoing, axis, shifted(count, step)))
    return by_sender(pieces, count, me)


def reduce_blocks(blocks, axis):
    count = lax.axis_size(axis)
    if count > PERMUTE_LIMIT:
        return lax.psum_scatter(blocks.astype(jnp.bfloat16), axis, scatter_dimension=0).astype(jnp.float32)
    me = lax.axis_index(axis)
    total = lax.dynamic_index_in_dim(blocks, me, 0, keepdims=False)
    for step in range(1, count):
        outgoing = lax.dynamic_index_in_dim(blocks, (me + step) % count, 0, keepdims=False)
        total = total + lax.ppermute(outgoing.astype(jnp.bfloat16), axis, shifted(count, step)).astype(jnp.float32)
    return total


def on_device(factors, temporal, maps, kdata, masks):
    width_x = maps.shape[2] // 2
    width_y = maps.shape[1]
    rows_own = factors.shape[2]
    table_x_re, table_x_im = dft_parts(width_x)
    table_y_re, table_y_im = dft_parts(width_y)
    forward_x = jnp.concatenate(
        [
            jnp.concatenate([table_x_re, table_x_im], axis=1),
            jnp.concatenate([-table_x_im, table_x_re], axis=1),
        ],
        axis=0,
    )
    adjoint_x = jnp.concatenate(
        [
            jnp.concatenate([table_x_re, -table_x_im], axis=1),
            jnp.concatenate([table_x_im, table_x_re], axis=1),
        ],
        axis=0,
    )
    wide_y = jnp.concatenate([table_y_re, table_y_im], axis=1)
    left_re = factors[0]
    left_im = factors[1]
    time_re = temporal[0]
    time_im = temporal[1]
    image_re = precise("tr,ryx->tyx", time_re, left_re) - precise("tr,ryx->tyx", time_im, left_im)
    image_im = precise("tr,ryx->tyx", time_im, left_re) + precise("tr,ryx->tyx", time_re, left_im)
    images = jnp.stack([image_re, image_im], axis=2).astype(jnp.bfloat16)
    frames_here = images.shape[0]
    width_own = images.shape[3]
    pieces_x = exchange_blocks(images, "frame")
    own_rows = jnp.transpose(pieces_x, (1, 2, 0, 3)).reshape(rows_own, 2 * width_x)
    full_image = gather_blocks(own_rows, "coil").reshape(width_y, 2 * width_x)
    sens = maps
    coil_image = sens_times(sens, full_image[None], width_x).astype(jnp.bfloat16)
    half_k = jnp.einsum(
        "cyn,nm->cym", coil_image, forward_x, preferred_element_type=jnp.float32
    ).astype(jnp.bfloat16)
    stacked = jnp.concatenate([half_k, rotate_plus(half_k, width_x)], axis=1)
    kspace = jnp.einsum("kj,cjn->ckn", wide_y, stacked, preferred_element_type=jnp.float32)
    sampled = masks[0].astype(jnp.float32)[:, :, None]
    residual = (sampled * (kspace - kdata[0].astype(jnp.float32))).astype(jnp.bfloat16)
    resid_stack = jnp.concatenate([residual, rotate_minus(residual, width_x)], axis=1)
    back_half = jnp.einsum(
        "kj,cjn->ckn", wide_y, resid_stack, preferred_element_type=jnp.float32
    ).astype(jnp.bfloat16)
    coil_back = jnp.einsum("cyn,nm->cym", back_half, adjoint_x, preferred_element_type=jnp.float32)
    sens = maps
    combined = jnp.sum(conj_sens_times(sens, coil_back, width_x), axis=0)
    groups = width_y // rows_own
    own_share = reduce_blocks(combined.reshape(groups, rows_own, 2 * width_x), "coil")
    outgoing = jnp.transpose(
        own_share.reshape(rows_own, 2, frames_here, width_own), (2, 0, 1, 3)
    ).astype(jnp.bfloat16)
    returned = exchange_blocks(outgoing, "frame").astype(jnp.float32)
    back_re = returned[:, :, 0]
    back_im = returned[:, :, 1]
    grad_re = precise("tr,tyx->ryx", time_re, back_re) + precise("tr,tyx->ryx", time_im, back_im)
    grad_im = precise("tr,tyx->ryx", time_re, back_im) - precise("tr,tyx->ryx", time_im, back_re)
    return factors - 0.5 * jnp.stack([grad_re, grad_im])


def solution(mesh):
    placed = (
        P("slab", None, "coil", "frame"),
        P("slab", None, None),
        P("coil", "slab", None),
        P("frame", "coil", "slab", None),
        P("frame", "coil", "slab"),
    )
    return jax.shard_map(
        on_device,
        mesh=mesh,
        in_specs=placed,
        out_specs=P("slab", None, "coil", "frame"),
        check_vma=False,
    )
```

```python
import math

import jax
import jax.numpy as jnp
from jax import lax
from jax.sharding import PartitionSpec as P


def dft_parts(length):
    index = jnp.arange(length, dtype=jnp.int32)
    phase = index[:, None] * index[None, :] % length
    angle = 2.0 * math.pi / length * phase.astype(jnp.float32)
    scale = 1.0 / math.sqrt(length)
    return (
        (jnp.cos(angle) * scale).astype(jnp.bfloat16),
        (-jnp.sin(angle) * scale).astype(jnp.bfloat16),
    )


def rotate_plus(values, half_width):
    return jnp.concatenate([-values[..., half_width:], values[..., :half_width]], axis=-1)


def rotate_minus(values, half_width):
    return jnp.concatenate([values[..., half_width:], -values[..., :half_width]], axis=-1)


def sens_times(sens, values, half_width):
    sens_re = sens[..., :half_width].astype(jnp.float32)
    sens_im = sens[..., half_width:].astype(jnp.float32)
    value_re = values[..., :half_width].astype(jnp.float32)
    value_im = values[..., half_width:].astype(jnp.float32)
    return jnp.concatenate(
        [sens_re * value_re - sens_im * value_im, sens_re * value_im + sens_im * value_re], axis=-1
    )


def conj_sens_times(sens, values, half_width):
    sens_re = sens[..., :half_width].astype(jnp.float32)
    sens_im = sens[..., half_width:].astype(jnp.float32)
    value_re = values[..., :half_width]
    value_im = values[..., half_width:]
    return jnp.concatenate(
        [sens_re * value_re + sens_im * value_im, sens_re * value_im - sens_im * value_re], axis=-1
    )


def precise(form, first, second):
    return jnp.einsum(form, first, second, precision=lax.Precision.HIGHEST)


PERMUTE_LIMIT = 8


def shifted(count, step):
    return [(source, (source + step) % count) for source in range(count)]


def by_sender(pieces, count, me):
    ring = jnp.stack([pieces[0]] + pieces[1:][::-1])
    doubled = jnp.concatenate([ring, ring], axis=0)
    return lax.dynamic_slice_in_dim(doubled, (count - me) % count, count, 0)


def gather_blocks(value, axis):
    count = lax.axis_size(axis)
    if count > PERMUTE_LIMIT:
        return lax.all_gather(value, axis)
    me = lax.axis_index(axis)
    pieces = [value] + [lax.ppermute(value, axis, shifted(count, step)) for step in range(1, count)]
    return by_sender(pieces, count, me)


def exchange_blocks(blocks, axis):
    count = lax.axis_size(axis)
    if count > PERMUTE_LIMIT:
        return lax.all_to_all(blocks, axis, 0, 0, tiled=True)
    me = lax.axis_index(axis)
    pieces = [lax.dynamic_index_in_dim(blocks, me, 0, keepdims=False)]
    for step in range(1, count):
        outgoing = lax.dynamic_index_in_dim(blocks, (me + step) % count, 0, keepdims=False)
        pieces.append(lax.ppermute(outgoing, axis, shifted(count, step)))
    return by_sender(pieces, count, me)


def reduce_blocks(blocks, axis):
    count = lax.axis_size(axis)
    if count > PERMUTE_LIMIT:
        return lax.psum_scatter(blocks.astype(jnp.bfloat16), axis, scatter_dimension=0).astype(jnp.float32)
    me = lax.axis_index(axis)
    total = lax.dynamic_index_in_dim(blocks, me, 0, keepdims=False)
    for step in range(1, count):
        outgoing = lax.dynamic_index_in_dim(blocks, (me + step) % count, 0, keepdims=False)
        total = total + lax.ppermute(outgoing.astype(jnp.bfloat16), axis, shifted(count, step)).astype(jnp.float32)
    return total


def shifted_pair(frames, groups, step_f, step_c):
    pairs = []
    for frame in range(frames):
        for group in range(groups):
            target = ((frame + step_f) % frames) * groups + (group + step_c) % groups
            pairs.append((frame * groups + group, target))
    return pairs


def spread_image(images, frames, groups):
    me_f = lax.axis_index("frame")
    me_c = lax.axis_index("coil")
    outgoing = {}
    by_x = []
    for step_f in range(frames):
        block = lax.dynamic_index_in_dim(images, (me_f + step_f) % frames, 0, keepdims=False)
        pieces = []
        for step_c in range(groups):
            if step_f == 0 and step_c == 0:
                pieces.append(block)
            else:
                pieces.append(lax.ppermute(block, ("frame", "coil"), shifted_pair(frames, groups, step_f, step_c)))
        by_x.append(by_sender(pieces, groups, me_c))
    return by_sender(by_x, frames, me_f)


def collect_image(blocks, frames, groups):
    me_f = lax.axis_index("frame")
    me_c = lax.axis_index("coil")
    sums = []
    for step_f in range(frames):
        total = None
        for step_c in range(groups):
            block = lax.dynamic_index_in_dim(
                lax.dynamic_index_in_dim(blocks, (me_c + step_c) % groups, 0, keepdims=False),
                (me_f + step_f) % frames, 0, keepdims=False,
            )
            if step_f == 0 and step_c == 0:
                term = block
            else:
                term = lax.ppermute(
                    block.astype(jnp.bfloat16), ("frame", "coil"), shifted_pair(frames, groups, step_f, step_c)
                ).astype(jnp.float32)
            total = term if total is None else total + term
        sums.append(total)
    return by_sender(sums, frames, me_f)


def on_device(factors, temporal, maps, kdata, masks):
    width_x = maps.shape[2] // 2
    width_y = maps.shape[1]
    rows_own = factors.shape[2]
    table_x_re, table_x_im = dft_parts(width_x)
    table_y_re, table_y_im = dft_parts(width_y)
    forward_x = jnp.concatenate(
        [
            jnp.concatenate([table_x_re, table_x_im], axis=1),
            jnp.concatenate([-table_x_im, table_x_re], axis=1),
        ],
        axis=0,
    )
    adjoint_x = jnp.concatenate(
        [
            jnp.concatenate([table_x_re, -table_x_im], axis=1),
            jnp.concatenate([table_x_im, table_x_re], axis=1),
        ],
        axis=0,
    )
    wide_y = jnp.concatenate([table_y_re, table_y_im], axis=1)
    left_re = factors[0]
    left_im = factors[1]
    time_re = temporal[0]
    time_im = temporal[1]
    image_re = precise("tr,ryx->tyx", time_re, left_re) - precise("tr,ryx->tyx", time_im, left_im)
    image_im = precise("tr,ryx->tyx", time_im, left_re) + precise("tr,ryx->tyx", time_re, left_im)
    images = jnp.stack([image_re, image_im], axis=2).astype(jnp.bfloat16)
    frames_here = images.shape[0]
    width_own = images.shape[3]
    frames = lax.axis_size("frame")
    groups = lax.axis_size("coil")
    direct = frames * groups <= 2 * PERMUTE_LIMIT
    if direct:
        blocks = spread_image(images, frames, groups)
        full_image = jnp.transpose(blocks, (1, 2, 3, 0, 4)).reshape(width_y, 2 * width_x)
    else:
        pieces_x = exchange_blocks(images, "frame")
        own_rows = jnp.transpose(pieces_x, (1, 2, 0, 3)).reshape(rows_own, 2 * width_x)
        full_image = gather_blocks(own_rows, "coil").reshape(width_y, 2 * width_x)
    sens = maps
    coil_image = sens_times(sens, full_image[None], width_x).astype(jnp.bfloat16)
    half_k = jnp.einsum(
        "cyn,nm->cym", coil_image, forward_x, preferred_element_type=jnp.float32
    ).astype(jnp.bfloat16)
    stacked = jnp.concatenate([half_k, rotate_plus(half_k, width_x)], axis=1)
    kspace = jnp.einsum("kj,cjn->ckn", wide_y, stacked, preferred_element_type=jnp.float32)
    sampled = masks[0].astype(jnp.float32)[:, :, None]
    residual = (sampled * (kspace - kdata[0].astype(jnp.float32))).astype(jnp.bfloat16)
    resid_stack = jnp.concatenate([residual, rotate_minus(residual, width_x)], axis=1)
    back_half = jnp.einsum(
        "kj,cjn->ckn", wide_y, resid_stack, preferred_element_type=jnp.float32
    ).astype(jnp.bfloat16)
    coil_back = jnp.einsum("cyn,nm->cym", back_half, adjoint_x, preferred_element_type=jnp.float32)
    sens = maps
    combined = jnp.sum(conj_sens_times(sens, coil_back, width_x), axis=0)
    if direct:
        blocks = jnp.transpose(
            combined.reshape(groups, rows_own, 2, frames, width_own), (0, 3, 1, 2, 4)
        )
        returned = collect_image(blocks, frames, groups)
    else:
        own_share = reduce_blocks(combined.reshape(groups, rows_own, 2 * width_x), "coil")
        outgoing = jnp.transpose(
            own_share.reshape(rows_own, 2, frames_here, width_own), (2, 0, 1, 3)
        ).astype(jnp.bfloat16)
        returned = exchange_blocks(outgoing, "frame").astype(jnp.float32)
    back_re = returned[:, :, 0]
    back_im = returned[:, :, 1]
    grad_re = precise("tr,tyx->ryx", time_re, back_re) + precise("tr,tyx->ryx", time_im, back_im)
    grad_im = precise("tr,tyx->ryx", time_re, back_im) - precise("tr,tyx->ryx", time_im, back_re)
    return factors - 0.5 * jnp.stack([grad_re, grad_im])


def solution(mesh):
    placed = (
        P("slab", None, "coil", "frame"),
        P("slab", None, None),
        P("coil", "slab", None),
        P("frame", "coil", "slab", None),
        P("frame", "coil", "slab"),
    )
    return jax.shard_map(
        on_device,
        mesh=mesh,
        in_specs=placed,
        out_specs=P("slab", None, "coil", "frame"),
        check_vma=False,
    )
```

```python
import math

import jax
import jax.numpy as jnp
from jax import lax
from jax.sharding import PartitionSpec as P


def dft_parts(length):
    index = jnp.arange(length, dtype=jnp.int32)
    phase = index[:, None] * index[None, :] % length
    angle = 2.0 * math.pi / length * phase.astype(jnp.float32)
    scale = 1.0 / math.sqrt(length)
    return (
        (jnp.cos(angle) * scale).astype(jnp.bfloat16),
        (-jnp.sin(angle) * scale).astype(jnp.bfloat16),
    )


def rotate_plus(values, half_width):
    return jnp.concatenate([-values[..., half_width:], values[..., :half_width]], axis=-1)


def rotate_minus(values, half_width):
    return jnp.concatenate([values[..., half_width:], -values[..., :half_width]], axis=-1)


def sens_times(sens, values, half_width):
    sens_re = sens[..., :half_width].astype(jnp.float32)
    sens_im = sens[..., half_width:].astype(jnp.float32)
    value_re = values[..., :half_width].astype(jnp.float32)
    value_im = values[..., half_width:].astype(jnp.float32)
    return jnp.concatenate(
        [sens_re * value_re - sens_im * value_im, sens_re * value_im + sens_im * value_re], axis=-1
    )


def conj_sens_times(sens, values, half_width):
    sens_re = sens[..., :half_width].astype(jnp.float32)
    sens_im = sens[..., half_width:].astype(jnp.float32)
    value_re = values[..., :half_width]
    value_im = values[..., half_width:]
    return jnp.concatenate(
        [sens_re * value_re + sens_im * value_im, sens_re * value_im - sens_im * value_re], axis=-1
    )


def precise(form, first, second):
    return jnp.einsum(form, first, second, precision=lax.Precision.HIGHEST)


PERMUTE_LIMIT = 8


def shifted(count, step):
    return [(source, (source + step) % count) for source in range(count)]


def by_sender(pieces, count, me):
    ring = jnp.stack([pieces[0]] + pieces[1:][::-1])
    doubled = jnp.concatenate([ring, ring], axis=0)
    return lax.dynamic_slice_in_dim(doubled, (count - me) % count, count, 0)


def gather_blocks(value, axis):
    count = lax.axis_size(axis)
    if count > PERMUTE_LIMIT:
        return lax.all_gather(value, axis)
    me = lax.axis_index(axis)
    pieces = [value] + [lax.ppermute(value, axis, shifted(count, step)) for step in range(1, count)]
    return by_sender(pieces, count, me)


def exchange_blocks(blocks, axis):
    count = lax.axis_size(axis)
    if count > PERMUTE_LIMIT:
        return lax.all_to_all(blocks, axis, 0, 0, tiled=True)
    me = lax.axis_index(axis)
    pieces = [lax.dynamic_index_in_dim(blocks, me, 0, keepdims=False)]
    for step in range(1, count):
        outgoing = lax.dynamic_index_in_dim(blocks, (me + step) % count, 0, keepdims=False)
        pieces.append(lax.ppermute(outgoing, axis, shifted(count, step)))
    return by_sender(pieces, count, me)


def reduce_blocks(blocks, axis):
    count = lax.axis_size(axis)
    if count > PERMUTE_LIMIT:
        return lax.psum_scatter(blocks.astype(jnp.bfloat16), axis, scatter_dimension=0).astype(jnp.float32)
    me = lax.axis_index(axis)
    total = lax.dynamic_index_in_dim(blocks, me, 0, keepdims=False)
    for step in range(1, count):
        outgoing = lax.dynamic_index_in_dim(blocks, (me + step) % count, 0, keepdims=False)
        total = total + lax.ppermute(outgoing.astype(jnp.bfloat16), axis, shifted(count, step)).astype(jnp.float32)
    return total


def on_device(factors, temporal, maps, kdata, masks):
    width_x = maps.shape[2] // 2
    width_y = maps.shape[1]
    rows_own = factors.shape[2]
    table_x_re, table_x_im = dft_parts(width_x)
    table_y_re, table_y_im = dft_parts(width_y)
    forward_x = jnp.concatenate(
        [
            jnp.concatenate([table_x_re, table_x_im], axis=1),
            jnp.concatenate([-table_x_im, table_x_re], axis=1),
        ],
        axis=0,
    )
    adjoint_x = jnp.concatenate(
        [
            jnp.concatenate([table_x_re, -table_x_im], axis=1),
            jnp.concatenate([table_x_im, table_x_re], axis=1),
        ],
        axis=0,
    )
    wide_y = jnp.concatenate([table_y_re, table_y_im], axis=1)
    left_re = factors[0]
    left_im = factors[1]
    time_re = temporal[0]
    time_im = temporal[1]
    image_re = jnp.sum(
        time_re[:, :, None, None] * left_re[None] - time_im[:, :, None, None] * left_im[None], axis=1
    )
    image_im = jnp.sum(
        time_im[:, :, None, None] * left_re[None] + time_re[:, :, None, None] * left_im[None], axis=1
    )
    images = jnp.stack([image_re, image_im], axis=2).astype(jnp.bfloat16)
    frames_here = images.shape[0]
    width_own = images.shape[3]
    pieces_x = exchange_blocks(images, "frame")
    own_rows = jnp.transpose(pieces_x, (1, 2, 0, 3)).reshape(rows_own, 2 * width_x)
    full_image = gather_blocks(own_rows, "coil").reshape(width_y, 2 * width_x)
    sens = maps
    coil_image = sens_times(sens, full_image[None], width_x).astype(jnp.bfloat16)
    half_k = jnp.einsum(
        "cyn,nm->cym", coil_image, forward_x, preferred_element_type=jnp.float32
    ).astype(jnp.bfloat16)
    stacked = jnp.concatenate([half_k, rotate_plus(half_k, width_x)], axis=1)
    kspace = jnp.einsum("kj,cjn->ckn", wide_y, stacked, preferred_element_type=jnp.float32)
    sampled = masks[0].astype(jnp.float32)[:, :, None]
    residual = (sampled * (kspace - kdata[0].astype(jnp.float32))).astype(jnp.bfloat16)
    resid_stack = jnp.concatenate([residual, rotate_minus(residual, width_x)], axis=1)
    back_half = jnp.einsum(
        "kj,cjn->ckn", wide_y, resid_stack, preferred_element_type=jnp.float32
    ).astype(jnp.bfloat16)
    coil_back = jnp.einsum("cyn,nm->cym", back_half, adjoint_x, preferred_element_type=jnp.float32)
    sens = maps
    combined = jnp.sum(conj_sens_times(sens, coil_back, width_x), axis=0)
    groups = width_y // rows_own
    own_share = reduce_blocks(combined.reshape(groups, rows_own, 2 * width_x), "coil")
    outgoing = jnp.transpose(
        own_share.reshape(rows_own, 2, frames_here, width_own), (2, 0, 1, 3)
    ).astype(jnp.bfloat16)
    returned = exchange_blocks(outgoing, "frame").astype(jnp.float32)
    back_re = returned[:, :, 0]
    back_im = returned[:, :, 1]
    grad_re = jnp.sum(
        time_re[:, :, None, None] * back_re[:, None] + time_im[:, :, None, None] * back_im[:, None], axis=0
    )
    grad_im = jnp.sum(
        time_re[:, :, None, None] * back_im[:, None] - time_im[:, :, None, None] * back_re[:, None], axis=0
    )
    return factors - 0.5 * jnp.stack([grad_re, grad_im])


def solution(mesh):
    placed = (
        P("slab", None, "coil", "frame"),
        P("slab", None, None),
        P("coil", "slab", None),
        P("frame", "coil", "slab", None),
        P("frame", "coil", "slab"),
    )
    return jax.shard_map(
        on_device,
        mesh=mesh,
        in_specs=placed,
        out_specs=P("slab", None, "coil", "frame"),
        check_vma=False,
    )
```

```python
import math

import jax
import jax.numpy as jnp
from jax import lax
from jax.experimental import pallas as pl
from jax.experimental.pallas import tpu as pltpu
from jax.sharding import PartitionSpec as P


def dft_parts(length):
    index = jnp.arange(length, dtype=jnp.int32)
    phase = index[:, None] * index[None, :] % length
    angle = 2.0 * math.pi / length * phase.astype(jnp.float32)
    scale = 1.0 / math.sqrt(length)
    return (
        (jnp.cos(angle) * scale).astype(jnp.bfloat16),
        (-jnp.sin(angle) * scale).astype(jnp.bfloat16),
    )


def rotate_plus(values, half_width):
    return jnp.concatenate([-values[..., half_width:], values[..., :half_width]], axis=-1)


def rotate_minus(values, half_width):
    return jnp.concatenate([values[..., half_width:], -values[..., :half_width]], axis=-1)


def sens_times(sens, values, half_width):
    sens_re = sens[..., :half_width].astype(jnp.float32)
    sens_im = sens[..., half_width:].astype(jnp.float32)
    value_re = values[..., :half_width].astype(jnp.float32)
    value_im = values[..., half_width:].astype(jnp.float32)
    return jnp.concatenate(
        [sens_re * value_re - sens_im * value_im, sens_re * value_im + sens_im * value_re], axis=-1
    )


def conj_sens_times(sens, values, half_width):
    sens_re = sens[..., :half_width].astype(jnp.float32)
    sens_im = sens[..., half_width:].astype(jnp.float32)
    value_re = values[..., :half_width]
    value_im = values[..., half_width:]
    return jnp.concatenate(
        [sens_re * value_re + sens_im * value_im, sens_re * value_im - sens_im * value_re], axis=-1
    )


def precise(form, first, second):
    return jnp.einsum(form, first, second, precision=lax.Precision.HIGHEST)


PERMUTE_LIMIT = 8


def shifted(count, step):
    return [(source, (source + step) % count) for source in range(count)]


def by_sender(pieces, count, me):
    ring = jnp.stack([pieces[0]] + pieces[1:][::-1])
    doubled = jnp.concatenate([ring, ring], axis=0)
    return lax.dynamic_slice_in_dim(doubled, (count - me) % count, count, 0)


def gather_blocks(value, axis):
    count = lax.axis_size(axis)
    if count > PERMUTE_LIMIT:
        return lax.all_gather(value, axis)
    me = lax.axis_index(axis)
    pieces = [value] + [lax.ppermute(value, axis, shifted(count, step)) for step in range(1, count)]
    return by_sender(pieces, count, me)


def exchange_blocks(blocks, axis):
    count = lax.axis_size(axis)
    if count > PERMUTE_LIMIT:
        return lax.all_to_all(blocks, axis, 0, 0, tiled=True)
    me = lax.axis_index(axis)
    pieces = [lax.dynamic_index_in_dim(blocks, me, 0, keepdims=False)]
    for step in range(1, count):
        outgoing = lax.dynamic_index_in_dim(blocks, (me + step) % count, 0, keepdims=False)
        pieces.append(lax.ppermute(outgoing, axis, shifted(count, step)))
    return by_sender(pieces, count, me)


def reduce_blocks(blocks, axis):
    count = lax.axis_size(axis)
    if count > PERMUTE_LIMIT:
        return lax.psum_scatter(blocks.astype(jnp.bfloat16), axis, scatter_dimension=0).astype(jnp.float32)
    me = lax.axis_index(axis)
    total = lax.dynamic_index_in_dim(blocks, me, 0, keepdims=False)
    for step in range(1, count):
        outgoing = lax.dynamic_index_in_dim(blocks, (me + step) % count, 0, keepdims=False)
        total = total + lax.ppermute(outgoing.astype(jnp.bfloat16), axis, shifted(count, step)).astype(jnp.float32)
    return total


def swap_halves(values, half_width, negate_first):
    low = values[:, :half_width]
    high = values[:, half_width:]
    if negate_first:
        return jnp.concatenate([-high, low], axis=1)
    return jnp.concatenate([high, -low], axis=1)


def coil_chain_kernel(image_ref, sens_ref, measured_ref, sampled_ref, forward_ref, adjoint_ref,
                      table_re_ref, table_im_ref, out_ref):
    half_width = image_ref.shape[1] // 2
    sens = sens_ref[0].astype(jnp.float32)
    sens_re = sens[:, :half_width]
    sens_im = sens[:, half_width:]
    image = image_ref[...].astype(jnp.float32)
    image_re = image[:, :half_width]
    image_im = image[:, half_width:]
    coil = jnp.concatenate(
        [sens_re * image_re - sens_im * image_im, sens_re * image_im + sens_im * image_re], axis=1
    ).astype(jnp.bfloat16)
    half_k = jnp.dot(coil, forward_ref[...], preferred_element_type=jnp.float32).astype(jnp.bfloat16)
    table_re = table_re_ref[...]
    table_im = table_im_ref[...]
    kspace = jnp.dot(table_re, half_k, preferred_element_type=jnp.float32) + jnp.dot(
        table_im, swap_halves(half_k, half_width, True), preferred_element_type=jnp.float32
    )
    residual = (sampled_ref[0] * (kspace - measured_ref[0].astype(jnp.float32))).astype(jnp.bfloat16)
    back_half = (
        jnp.dot(table_re, residual, preferred_element_type=jnp.float32)
        + jnp.dot(table_im, swap_halves(residual, half_width, False), preferred_element_type=jnp.float32)
    ).astype(jnp.bfloat16)
    coil_back = jnp.dot(back_half, adjoint_ref[...], preferred_element_type=jnp.float32)
    back_re = coil_back[:, :half_width]
    back_im = coil_back[:, half_width:]
    term = jnp.concatenate(
        [sens_re * back_re + sens_im * back_im, sens_re * back_im - sens_im * back_re], axis=1
    )

    @pl.when(pl.program_id(0) == 0)
    def _():
        out_ref[...] = term

    @pl.when(pl.program_id(0) > 0)
    def _():
        out_ref[...] += term


def coil_chain(image, sens, measured, sampled, forward_x, adjoint_x, table_y_re, table_y_im):
    coils, rows, width = sens.shape
    whole = lambda c: (0, 0)
    per_coil = lambda c: (c, 0, 0)
    flops = coils * 8 * rows * width * width
    return pl.pallas_call(
        coil_chain_kernel,
        out_shape=jax.ShapeDtypeStruct((rows, width), jnp.float32),
        grid=(coils,),
        in_specs=[
            pl.BlockSpec((rows, width), whole),
            pl.BlockSpec((1, rows, width), per_coil),
            pl.BlockSpec((1, rows, width), per_coil),
            pl.BlockSpec((1, rows, 1), per_coil),
            pl.BlockSpec((width, width), whole),
            pl.BlockSpec((width, width), whole),
            pl.BlockSpec((rows, rows), whole),
            pl.BlockSpec((rows, rows), whole),
        ],
        out_specs=pl.BlockSpec((rows, width), whole),
        compiler_params=pltpu.CompilerParams(dimension_semantics=("arbitrary",)),
        cost_estimate=pl.CostEstimate(
            flops=flops, transcendentals=0, bytes_accessed=2 * 2 * coils * rows * width + 4 * rows * width
        ),
    )(image, sens, measured, sampled, forward_x, adjoint_x, table_y_re, table_y_im)


def on_device(factors, temporal, maps, kdata, masks):
    width_x = maps.shape[2] // 2
    width_y = maps.shape[1]
    rows_own = factors.shape[2]
    table_x_re, table_x_im = dft_parts(width_x)
    table_y_re, table_y_im = dft_parts(width_y)
    forward_x = jnp.concatenate(
        [
            jnp.concatenate([table_x_re, table_x_im], axis=1),
            jnp.concatenate([-table_x_im, table_x_re], axis=1),
        ],
        axis=0,
    )
    adjoint_x = jnp.concatenate(
        [
            jnp.concatenate([table_x_re, -table_x_im], axis=1),
            jnp.concatenate([table_x_im, table_x_re], axis=1),
        ],
        axis=0,
    )
    wide_y = jnp.concatenate([table_y_re, table_y_im], axis=1)
    left_re = factors[0]
    left_im = factors[1]
    time_re = temporal[0]
    time_im = temporal[1]
    image_re = jnp.sum(
        time_re[:, :, None, None] * left_re[None] - time_im[:, :, None, None] * left_im[None], axis=1
    )
    image_im = jnp.sum(
        time_im[:, :, None, None] * left_re[None] + time_re[:, :, None, None] * left_im[None], axis=1
    )
    images = jnp.stack([image_re, image_im], axis=2).astype(jnp.bfloat16)
    frames_here = images.shape[0]
    width_own = images.shape[3]
    pieces_x = exchange_blocks(images, "frame")
    own_rows = jnp.transpose(pieces_x, (1, 2, 0, 3)).reshape(rows_own, 2 * width_x)
    full_image = gather_blocks(own_rows, "coil").reshape(width_y, 2 * width_x)
    sampled = masks[0].astype(jnp.float32)[:, :, None]
    combined = coil_chain(full_image, maps, kdata[0], sampled, forward_x, adjoint_x, table_y_re, table_y_im)
    groups = width_y // rows_own
    own_share = reduce_blocks(combined.reshape(groups, rows_own, 2 * width_x), "coil")
    outgoing = jnp.transpose(
        own_share.reshape(rows_own, 2, frames_here, width_own), (2, 0, 1, 3)
    ).astype(jnp.bfloat16)
    returned = exchange_blocks(outgoing, "frame").astype(jnp.float32)
    back_re = returned[:, :, 0]
    back_im = returned[:, :, 1]
    grad_re = jnp.sum(
        time_re[:, :, None, None] * back_re[:, None] + time_im[:, :, None, None] * back_im[:, None], axis=0
    )
    grad_im = jnp.sum(
        time_re[:, :, None, None] * back_im[:, None] - time_im[:, :, None, None] * back_re[:, None], axis=0
    )
    return factors - 0.5 * jnp.stack([grad_re, grad_im])


def solution(mesh):
    placed = (
        P("slab", None, "coil", "frame"),
        P("slab", None, None),
        P("coil", "slab", None),
        P("frame", "coil", "slab", None),
        P("frame", "coil", "slab"),
    )
    return jax.shard_map(
        on_device,
        mesh=mesh,
        in_specs=placed,
        out_specs=P("slab", None, "coil", "frame"),
        check_vma=False,
    )
```

```python
import math

import jax
import jax.numpy as jnp
from jax import lax
from jax.experimental import pallas as pl
from jax.experimental.pallas import tpu as pltpu
from jax.sharding import PartitionSpec as P


def dft_parts(length):
    index = jnp.arange(length, dtype=jnp.int32)
    phase = index[:, None] * index[None, :] % length
    angle = 2.0 * math.pi / length * phase.astype(jnp.float32)
    scale = 1.0 / math.sqrt(length)
    return (
        (jnp.cos(angle) * scale).astype(jnp.bfloat16),
        (-jnp.sin(angle) * scale).astype(jnp.bfloat16),
    )


def rotate_plus(values, half_width):
    return jnp.concatenate([-values[..., half_width:], values[..., :half_width]], axis=-1)


def rotate_minus(values, half_width):
    return jnp.concatenate([values[..., half_width:], -values[..., :half_width]], axis=-1)


def sens_times(sens, values, half_width):
    sens_re = sens[..., :half_width].astype(jnp.float32)
    sens_im = sens[..., half_width:].astype(jnp.float32)
    value_re = values[..., :half_width].astype(jnp.float32)
    value_im = values[..., half_width:].astype(jnp.float32)
    return jnp.concatenate(
        [sens_re * value_re - sens_im * value_im, sens_re * value_im + sens_im * value_re], axis=-1
    )


def conj_sens_times(sens, values, half_width):
    sens_re = sens[..., :half_width].astype(jnp.float32)
    sens_im = sens[..., half_width:].astype(jnp.float32)
    value_re = values[..., :half_width]
    value_im = values[..., half_width:]
    return jnp.concatenate(
        [sens_re * value_re + sens_im * value_im, sens_re * value_im - sens_im * value_re], axis=-1
    )


def precise(form, first, second):
    return jnp.einsum(form, first, second, precision=lax.Precision.HIGHEST)


PERMUTE_LIMIT = 8


def paired(count, step):
    if count & (count - 1) == 0:
        return [(source, source ^ step) for source in range(count)]
    return [(source, (source + step) % count) for source in range(count)]


def partner(count, me, step):
    if count & (count - 1) == 0:
        return me ^ step
    return (me + step) % count


def by_sender(pieces, count, me):
    stacked = jnp.stack(pieces)
    if count & (count - 1) == 0:
        return jnp.take(stacked, me ^ jnp.arange(count), axis=0)
    ring = jnp.concatenate([stacked[:1], stacked[1:][::-1]], axis=0)
    doubled = jnp.concatenate([ring, ring], axis=0)
    return lax.dynamic_slice_in_dim(doubled, (count - me) % count, count, 0)


def gather_blocks(value, axis):
    count = lax.axis_size(axis)
    if count > PERMUTE_LIMIT:
        return lax.all_gather(value, axis)
    me = lax.axis_index(axis)
    pieces = [value] + [lax.ppermute(value, axis, paired(count, step)) for step in range(1, count)]
    return by_sender(pieces, count, me)


def exchange_blocks(blocks, axis):
    count = lax.axis_size(axis)
    if count > PERMUTE_LIMIT:
        return lax.all_to_all(blocks, axis, 0, 0, tiled=True)
    me = lax.axis_index(axis)
    pieces = [lax.dynamic_index_in_dim(blocks, me, 0, keepdims=False)]
    for step in range(1, count):
        outgoing = lax.dynamic_index_in_dim(blocks, partner(count, me, step), 0, keepdims=False)
        pieces.append(lax.ppermute(outgoing, axis, paired(count, step)))
    return by_sender(pieces, count, me)


def reduce_blocks(blocks, axis):
    count = lax.axis_size(axis)
    if count > PERMUTE_LIMIT:
        return lax.psum_scatter(blocks.astype(jnp.bfloat16), axis, scatter_dimension=0).astype(jnp.float32)
    me = lax.axis_index(axis)
    total = lax.dynamic_index_in_dim(blocks, me, 0, keepdims=False)
    for step in range(1, count):
        outgoing = lax.dynamic_index_in_dim(blocks, partner(count, me, step), 0, keepdims=False)
        total = total + lax.ppermute(outgoing.astype(jnp.bfloat16), axis, paired(count, step)).astype(jnp.float32)
    return total


def swap_halves(values, half_width, negate_first):
    low = values[:, :half_width]
    high = values[:, half_width:]
    if negate_first:
        return jnp.concatenate([-high, low], axis=1)
    return jnp.concatenate([high, -low], axis=1)


def coil_chain_kernel(image_ref, sens_ref, measured_ref, sampled_ref, forward_ref, adjoint_ref,
                      table_re_ref, table_im_ref, out_ref):
    half_width = image_ref.shape[1] // 2
    sens = sens_ref[0].astype(jnp.float32)
    sens_re = sens[:, :half_width]
    sens_im = sens[:, half_width:]
    image = image_ref[...].astype(jnp.float32)
    image_re = image[:, :half_width]
    image_im = image[:, half_width:]
    coil = jnp.concatenate(
        [sens_re * image_re - sens_im * image_im, sens_re * image_im + sens_im * image_re], axis=1
    ).astype(jnp.bfloat16)
    half_k = jnp.dot(coil, forward_ref[...], preferred_element_type=jnp.float32).astype(jnp.bfloat16)
    table_re = table_re_ref[...]
    table_im = table_im_ref[...]
    kspace = jnp.dot(table_re, half_k, preferred_element_type=jnp.float32) + jnp.dot(
        table_im, swap_halves(half_k, half_width, True), preferred_element_type=jnp.float32
    )
    residual = (sampled_ref[0] * (kspace - measured_ref[0].astype(jnp.float32))).astype(jnp.bfloat16)
    back_half = (
        jnp.dot(table_re, residual, preferred_element_type=jnp.float32)
        + jnp.dot(table_im, swap_halves(residual, half_width, False), preferred_element_type=jnp.float32)
    ).astype(jnp.bfloat16)
    coil_back = jnp.dot(back_half, adjoint_ref[...], preferred_element_type=jnp.float32)
    back_re = coil_back[:, :half_width]
    back_im = coil_back[:, half_width:]
    term = jnp.concatenate(
        [sens_re * back_re + sens_im * back_im, sens_re * back_im - sens_im * back_re], axis=1
    )

    @pl.when(pl.program_id(0) == 0)
    def _():
        out_ref[...] = term

    @pl.when(pl.program_id(0) > 0)
    def _():
        out_ref[...] += term


def coil_chain(image, sens, measured, sampled, forward_x, adjoint_x, table_y_re, table_y_im):
    coils, rows, width = sens.shape
    whole = lambda c: (0, 0)
    per_coil = lambda c: (c, 0, 0)
    flops = coils * 8 * rows * width * width
    return pl.pallas_call(
        coil_chain_kernel,
        out_shape=jax.ShapeDtypeStruct((rows, width), jnp.float32),
        grid=(coils,),
        in_specs=[
            pl.BlockSpec((rows, width), whole),
            pl.BlockSpec((1, rows, width), per_coil),
            pl.BlockSpec((1, rows, width), per_coil),
            pl.BlockSpec((1, rows, 1), per_coil),
            pl.BlockSpec((width, width), whole),
            pl.BlockSpec((width, width), whole),
            pl.BlockSpec((rows, rows), whole),
            pl.BlockSpec((rows, rows), whole),
        ],
        out_specs=pl.BlockSpec((rows, width), whole),
        compiler_params=pltpu.CompilerParams(dimension_semantics=("arbitrary",)),
        cost_estimate=pl.CostEstimate(
            flops=flops, transcendentals=0, bytes_accessed=2 * 2 * coils * rows * width + 4 * rows * width
        ),
    )(image, sens, measured, sampled, forward_x, adjoint_x, table_y_re, table_y_im)


def on_device(factors, temporal, maps, kdata, masks):
    width_x = maps.shape[2] // 2
    width_y = maps.shape[1]
    rows_own = factors.shape[2]
    table_x_re, table_x_im = dft_parts(width_x)
    table_y_re, table_y_im = dft_parts(width_y)
    forward_x = jnp.concatenate(
        [
            jnp.concatenate([table_x_re, table_x_im], axis=1),
            jnp.concatenate([-table_x_im, table_x_re], axis=1),
        ],
        axis=0,
    )
    adjoint_x = jnp.concatenate(
        [
            jnp.concatenate([table_x_re, -table_x_im], axis=1),
            jnp.concatenate([table_x_im, table_x_re], axis=1),
        ],
        axis=0,
    )
    wide_y = jnp.concatenate([table_y_re, table_y_im], axis=1)
    left_re = factors[0]
    left_im = factors[1]
    time_re = temporal[0]
    time_im = temporal[1]
    image_re = jnp.sum(
        time_re[:, :, None, None] * left_re[None] - time_im[:, :, None, None] * left_im[None], axis=1
    )
    image_im = jnp.sum(
        time_im[:, :, None, None] * left_re[None] + time_re[:, :, None, None] * left_im[None], axis=1
    )
    images = jnp.stack([image_re, image_im], axis=2).astype(jnp.bfloat16)
    frames_here = images.shape[0]
    width_own = images.shape[3]
    pieces_x = exchange_blocks(images, "frame")
    own_rows = jnp.transpose(pieces_x, (1, 2, 0, 3)).reshape(rows_own, 2 * width_x)
    full_image = gather_blocks(own_rows, "coil").reshape(width_y, 2 * width_x)
    sampled = masks[0].astype(jnp.float32)[:, :, None]
    combined = coil_chain(full_image, maps, kdata[0], sampled, forward_x, adjoint_x, table_y_re, table_y_im)
    groups = width_y // rows_own
    own_share = reduce_blocks(combined.reshape(groups, rows_own, 2 * width_x), "coil")
    outgoing = jnp.transpose(
        own_share.reshape(rows_own, 2, frames_here, width_own), (2, 0, 1, 3)
    ).astype(jnp.bfloat16)
    returned = exchange_blocks(outgoing, "frame").astype(jnp.float32)
    back_re = returned[:, :, 0]
    back_im = returned[:, :, 1]
    grad_re = jnp.sum(
        time_re[:, :, None, None] * back_re[:, None] + time_im[:, :, None, None] * back_im[:, None], axis=0
    )
    grad_im = jnp.sum(
        time_re[:, :, None, None] * back_im[:, None] - time_im[:, :, None, None] * back_re[:, None], axis=0
    )
    return factors - 0.5 * jnp.stack([grad_re, grad_im])


def solution(mesh):
    placed = (
        P("slab", None, "coil", "frame"),
        P("slab", None, None),
        P("coil", "slab", None),
        P("frame", "coil", "slab", None),
        P("frame", "coil", "slab"),
    )
    return jax.shard_map(
        on_device,
        mesh=mesh,
        in_specs=placed,
        out_specs=P("slab", None, "coil", "frame"),
        check_vma=False,
    )
```

```python
import math

import jax
import ml_dtypes
import numpy as np
import jax.numpy as jnp
from jax import lax
from jax.experimental import pallas as pl
from jax.experimental.pallas import tpu as pltpu
from jax.sharding import PartitionSpec as P


def dft_parts(length):
    index = np.arange(length, dtype=np.int64)
    phase = (index[:, None] * index[None, :]) % length
    angle = np.float32(2.0 * math.pi / length) * phase.astype(np.float32)
    scale = np.float32(1.0 / math.sqrt(length))
    real = (np.cos(angle.astype(np.float64)).astype(np.float32) * scale).astype(ml_dtypes.bfloat16)
    imag = (-np.sin(angle.astype(np.float64)).astype(np.float32) * scale).astype(ml_dtypes.bfloat16)
    return real, imag


def rotate_plus(values, half_width):
    return jnp.concatenate([-values[..., half_width:], values[..., :half_width]], axis=-1)


def rotate_minus(values, half_width):
    return jnp.concatenate([values[..., half_width:], -values[..., :half_width]], axis=-1)


def sens_times(sens, values, half_width):
    sens_re = sens[..., :half_width].astype(jnp.float32)
    sens_im = sens[..., half_width:].astype(jnp.float32)
    value_re = values[..., :half_width].astype(jnp.float32)
    value_im = values[..., half_width:].astype(jnp.float32)
    return jnp.concatenate(
        [sens_re * value_re - sens_im * value_im, sens_re * value_im + sens_im * value_re], axis=-1
    )


def conj_sens_times(sens, values, half_width):
    sens_re = sens[..., :half_width].astype(jnp.float32)
    sens_im = sens[..., half_width:].astype(jnp.float32)
    value_re = values[..., :half_width]
    value_im = values[..., half_width:]
    return jnp.concatenate(
        [sens_re * value_re + sens_im * value_im, sens_re * value_im - sens_im * value_re], axis=-1
    )


def precise(form, first, second):
    return jnp.einsum(form, first, second, precision=lax.Precision.HIGHEST)


PERMUTE_LIMIT = 8


def shifted(count, step):
    return [(source, (source + step) % count) for source in range(count)]


def by_sender(pieces, count, me):
    ring = jnp.stack([pieces[0]] + pieces[1:][::-1])
    doubled = jnp.concatenate([ring, ring], axis=0)
    return lax.dynamic_slice_in_dim(doubled, (count - me) % count, count, 0)


def gather_blocks(value, axis):
    count = lax.axis_size(axis)
    if count > PERMUTE_LIMIT:
        return lax.all_gather(value, axis)
    me = lax.axis_index(axis)
    pieces = [value] + [lax.ppermute(value, axis, shifted(count, step)) for step in range(1, count)]
    return by_sender(pieces, count, me)


def exchange_blocks(blocks, axis):
    count = lax.axis_size(axis)
    if count > PERMUTE_LIMIT:
        return lax.all_to_all(blocks, axis, 0, 0, tiled=True)
    me = lax.axis_index(axis)
    pieces = [lax.dynamic_index_in_dim(blocks, me, 0, keepdims=False)]
    for step in range(1, count):
        outgoing = lax.dynamic_index_in_dim(blocks, (me + step) % count, 0, keepdims=False)
        pieces.append(lax.ppermute(outgoing, axis, shifted(count, step)))
    return by_sender(pieces, count, me)


def reduce_blocks(blocks, axis):
    count = lax.axis_size(axis)
    if count > PERMUTE_LIMIT:
        return lax.psum_scatter(blocks.astype(jnp.bfloat16), axis, scatter_dimension=0).astype(jnp.float32)
    me = lax.axis_index(axis)
    total = lax.dynamic_index_in_dim(blocks, me, 0, keepdims=False)
    for step in range(1, count):
        outgoing = lax.dynamic_index_in_dim(blocks, (me + step) % count, 0, keepdims=False)
        total = total + lax.ppermute(outgoing.astype(jnp.bfloat16), axis, shifted(count, step)).astype(jnp.float32)
    return total


def swap_halves(values, half_width, negate_first):
    low = values[:, :half_width]
    high = values[:, half_width:]
    if negate_first:
        return jnp.concatenate([-high, low], axis=1)
    return jnp.concatenate([high, -low], axis=1)


def coil_chain_kernel(*refs):
    groups = len(refs) - 12
    pieces = refs[:groups]
    place_ref, sens_ref, measured_ref, sampled_ref, forward_ref, adjoint_ref, table_re_ref, table_im_ref = refs[
        groups:groups + 8
    ]
    own_ref, send_ref = refs[groups + 8:groups + 10]
    image_ref, total_ref = refs[groups + 10:]
    rows = pieces[0].shape[0]
    half_width = image_ref.shape[1] // 2
    me = place_ref[0]
    step = pl.program_id(0)

    @pl.when(step == 0)
    def _():
        for block in range(groups):
            source = (me - block + groups) % groups
            value = pieces[0][...]
            for other in range(1, groups):
                value = jnp.where(source == other, pieces[other][...], value)
            image_ref[block * rows:(block + 1) * rows, :] = value

    sens = sens_ref[0].astype(jnp.float32)
    sens_re = sens[:, :half_width]
    sens_im = sens[:, half_width:]
    image = image_ref[...].astype(jnp.float32)
    image_re = image[:, :half_width]
    image_im = image[:, half_width:]
    coil = jnp.concatenate(
        [sens_re * image_re - sens_im * image_im, sens_re * image_im + sens_im * image_re], axis=1
    ).astype(jnp.bfloat16)
    half_k = jnp.dot(coil, forward_ref[...], preferred_element_type=jnp.float32).astype(jnp.bfloat16)
    table_re = table_re_ref[...]
    table_im = table_im_ref[...]
    kspace = jnp.dot(table_re, half_k, preferred_element_type=jnp.float32) + jnp.dot(
        table_im, swap_halves(half_k, half_width, True), preferred_element_type=jnp.float32
    )
    residual = (kspace - measured_ref[0].astype(jnp.float32)).astype(jnp.bfloat16)
    sampled = sampled_ref[0].astype(jnp.bfloat16)
    back_half = (
        jnp.dot(table_re * sampled, residual, preferred_element_type=jnp.float32)
        + jnp.dot(table_im * sampled, swap_halves(residual, half_width, False), preferred_element_type=jnp.float32)
    ).astype(jnp.bfloat16)
    coil_back = jnp.dot(back_half, adjoint_ref[...], preferred_element_type=jnp.float32)
    back_re = coil_back[:, :half_width]
    back_im = coil_back[:, half_width:]
    term = jnp.concatenate(
        [sens_re * back_re + sens_im * back_im, sens_re * back_im - sens_im * back_re], axis=1
    )

    @pl.when(step == 0)
    def _():
        total_ref[...] = term

    @pl.when(step > 0)
    def _():
        total_ref[...] += term

    @pl.when(step == pl.num_programs(0) - 1)
    def _():
        start = pl.multiple_of(me * rows, rows)
        own_ref[...] = total_ref[pl.ds(start, rows), :]
        for shift in range(1, groups):
            start = pl.multiple_of(((me + shift) % groups) * rows, rows)
            send_ref[shift - 1] = total_ref[pl.ds(start, rows), :].astype(jnp.bfloat16)


def coil_chain(pieces, place, sens, measured, sampled, forward_x, adjoint_x, table_y_re, table_y_im):
    coils, height, width = sens.shape
    groups = len(pieces)
    rows = pieces[0].shape[0]
    whole = lambda c: (0, 0)
    per_coil = lambda c: (c, 0, 0)
    flops = coils * 8 * height * width * width
    return pl.pallas_call(
        coil_chain_kernel,
        out_shape=(
            jax.ShapeDtypeStruct((rows, width), jnp.float32),
            jax.ShapeDtypeStruct((groups - 1, rows, width), jnp.bfloat16),
        ),
        grid=(coils,),
        in_specs=[pl.BlockSpec((rows, width), whole)] * groups
        + [
            pl.BlockSpec(memory_space=pltpu.SMEM),
            pl.BlockSpec((1, height, width), per_coil),
            pl.BlockSpec((1, height, width), per_coil),
            pl.BlockSpec((1, 1, height), per_coil),
            pl.BlockSpec((width, width), whole),
            pl.BlockSpec((width, width), whole),
            pl.BlockSpec((height, height), whole),
            pl.BlockSpec((height, height), whole),
        ],
        out_specs=(
            pl.BlockSpec((rows, width), whole),
            pl.BlockSpec((groups - 1, rows, width), lambda c: (0, 0, 0)),
        ),
        scratch_shapes=[pltpu.VMEM((height, width), jnp.bfloat16), pltpu.VMEM((height, width), jnp.float32)],
        compiler_params=pltpu.CompilerParams(dimension_semantics=("arbitrary",)),
        cost_estimate=pl.CostEstimate(
            flops=flops, transcendentals=0, bytes_accessed=2 * 2 * coils * height * width + 4 * height * width
        ),
    )(*pieces, place, sens, measured, sampled, forward_x, adjoint_x, table_y_re, table_y_im)


def on_device(factors, temporal, maps, kdata, masks):
    width_x = maps.shape[2] // 2
    width_y = maps.shape[1]
    rows_own = factors.shape[2]
    table_x_re, table_x_im = dft_parts(width_x)
    table_y_re, table_y_im = dft_parts(width_y)
    forward_x = jnp.asarray(np.block([[table_x_re, table_x_im], [-table_x_im, table_x_re]]))
    adjoint_x = jnp.asarray(np.block([[table_x_re, -table_x_im], [table_x_im, table_x_re]]))
    table_y_re = jnp.asarray(table_y_re)
    table_y_im = jnp.asarray(table_y_im)
    time_re = temporal[0]
    time_im = temporal[1]
    mixing = jnp.stack(
        [jnp.stack([time_re, -time_im], axis=1), jnp.stack([time_im, time_re], axis=1)], axis=1
    )
    images = jnp.sum(
        mixing[:, :, :, :, None, None] * factors[None, None], axis=(2, 3)
    ).astype(jnp.bfloat16)
    frames_here = images.shape[0]
    width_own = images.shape[3]
    pieces_x = exchange_blocks(images, "frame")
    own_rows = jnp.transpose(pieces_x, (2, 1, 0, 3)).reshape(rows_own, 2 * width_x)
    groups = lax.axis_size("coil")
    me_c = lax.axis_index("coil")
    pieces = [own_rows] + [lax.ppermute(own_rows, "coil", shifted(groups, step)) for step in range(1, groups)]
    sampled = masks[0].astype(jnp.float32)[:, None, :]
    place = jnp.reshape(me_c, (1,)).astype(jnp.int32)
    own_total, outgoing = coil_chain(
        pieces, place, maps, kdata[0], sampled, forward_x, adjoint_x, table_y_re, table_y_im
    )
    own_share = own_total
    for step in range(1, groups):
        own_share = own_share + lax.ppermute(outgoing[step - 1], "coil", shifted(groups, step)).astype(jnp.float32)
    outgoing = jnp.transpose(
        own_share.reshape(rows_own, 2, frames_here, width_own), (2, 0, 1, 3)
    ).astype(jnp.bfloat16)
    returned = exchange_blocks(outgoing, "frame").astype(jnp.float32)
    weights = jnp.stack(
        [jnp.stack([time_re.T, time_im.T], axis=2), jnp.stack([-time_im.T, time_re.T], axis=2)], axis=0
    )
    gradient = jnp.sum(
        weights[:, :, :, None, :, None] * returned[None, None], axis=(2, 4)
    )
    return factors - 0.5 * gradient


def solution(mesh):
    placed = (
        P("slab", None, "coil", "frame"),
        P("slab", None, None),
        P("coil", "slab", None),
        P("frame", "coil", "slab", None),
        P("frame", "coil", "slab"),
    )
    return jax.shard_map(
        on_device,
        mesh=mesh,
        in_specs=placed,
        out_specs=P("slab", None, "coil", "frame"),
        check_vma=False,
    )
```

```python
import math

import jax
import ml_dtypes
import numpy as np
import jax.numpy as jnp
from jax import lax
from jax.experimental import pallas as pl
from jax.experimental.pallas import tpu as pltpu
from jax.sharding import PartitionSpec as P


def dft_parts(length):
    index = np.arange(length, dtype=np.int64)
    phase = (index[:, None] * index[None, :]) % length
    angle = np.float32(2.0 * math.pi / length) * phase.astype(np.float32)
    scale = np.float32(1.0 / math.sqrt(length))
    real = (np.cos(angle.astype(np.float64)).astype(np.float32) * scale).astype(ml_dtypes.bfloat16)
    imag = (-np.sin(angle.astype(np.float64)).astype(np.float32) * scale).astype(ml_dtypes.bfloat16)
    return real, imag


def rotate_plus(values, half_width):
    return jnp.concatenate([-values[..., half_width:], values[..., :half_width]], axis=-1)


def rotate_minus(values, half_width):
    return jnp.concatenate([values[..., half_width:], -values[..., :half_width]], axis=-1)


def sens_times(sens, values, half_width):
    sens_re = sens[..., :half_width].astype(jnp.float32)
    sens_im = sens[..., half_width:].astype(jnp.float32)
    value_re = values[..., :half_width].astype(jnp.float32)
    value_im = values[..., half_width:].astype(jnp.float32)
    return jnp.concatenate(
        [sens_re * value_re - sens_im * value_im, sens_re * value_im + sens_im * value_re], axis=-1
    )


def conj_sens_times(sens, values, half_width):
    sens_re = sens[..., :half_width].astype(jnp.float32)
    sens_im = sens[..., half_width:].astype(jnp.float32)
    value_re = values[..., :half_width]
    value_im = values[..., half_width:]
    return jnp.concatenate(
        [sens_re * value_re + sens_im * value_im, sens_re * value_im - sens_im * value_re], axis=-1
    )


def precise(form, first, second):
    return jnp.einsum(form, first, second, precision=lax.Precision.HIGHEST)


PERMUTE_LIMIT = 8


def shifted(count, step):
    return [(source, (source + step) % count) for source in range(count)]


def by_sender(pieces, count, me):
    ring = jnp.stack([pieces[0]] + pieces[1:][::-1])
    doubled = jnp.concatenate([ring, ring], axis=0)
    return lax.dynamic_slice_in_dim(doubled, (count - me) % count, count, 0)


def gather_blocks(value, axis):
    count = lax.axis_size(axis)
    if count > PERMUTE_LIMIT:
        return lax.all_gather(value, axis)
    me = lax.axis_index(axis)
    pieces = [value] + [lax.ppermute(value, axis, shifted(count, step)) for step in range(1, count)]
    return by_sender(pieces, count, me)


def exchange_blocks(blocks, axis):
    count = lax.axis_size(axis)
    if count > PERMUTE_LIMIT:
        return lax.all_to_all(blocks, axis, 0, 0, tiled=True)
    me = lax.axis_index(axis)
    pieces = [lax.dynamic_index_in_dim(blocks, me, 0, keepdims=False)]
    for step in range(1, count):
        outgoing = lax.dynamic_index_in_dim(blocks, (me + step) % count, 0, keepdims=False)
        pieces.append(lax.ppermute(outgoing, axis, shifted(count, step)))
    return by_sender(pieces, count, me)


def reduce_blocks(blocks, axis):
    count = lax.axis_size(axis)
    if count > PERMUTE_LIMIT:
        return lax.psum_scatter(blocks.astype(jnp.bfloat16), axis, scatter_dimension=0).astype(jnp.float32)
    me = lax.axis_index(axis)
    total = lax.dynamic_index_in_dim(blocks, me, 0, keepdims=False)
    for step in range(1, count):
        outgoing = lax.dynamic_index_in_dim(blocks, (me + step) % count, 0, keepdims=False)
        total = total + lax.ppermute(outgoing.astype(jnp.bfloat16), axis, shifted(count, step)).astype(jnp.float32)
    return total


def swap_halves(values, half_width, negate_first):
    low = values[:, :half_width]
    high = values[:, half_width:]
    if negate_first:
        return jnp.concatenate([-high, low], axis=1)
    return jnp.concatenate([high, -low], axis=1)


def coil_chain_kernel(*refs):
    groups = len(refs) - 12
    pieces = refs[:groups]
    place_ref, sens_ref, measured_ref, sampled_ref, forward_ref, adjoint_ref, table_re_ref, table_im_ref = refs[
        groups:groups + 8
    ]
    own_ref, send_ref = refs[groups + 8:groups + 10]
    image_ref, total_ref = refs[groups + 10:]
    rows = pieces[0].shape[0]
    half_width = image_ref.shape[1] // 2
    me = place_ref[0]
    step = pl.program_id(0)

    @pl.when(step == 0)
    def _():
        for block in range(groups):
            source = (me - block + groups) % groups
            value = pieces[0][...]
            for other in range(1, groups):
                value = jnp.where(source == other, pieces[other][...], value)
            image_ref[block * rows:(block + 1) * rows, :] = value

    sens = sens_ref[0].astype(jnp.float32)
    sens_re = sens[:, :half_width]
    sens_im = sens[:, half_width:]
    image = image_ref[...].astype(jnp.float32)
    image_re = image[:, :half_width]
    image_im = image[:, half_width:]
    coil = jnp.concatenate(
        [sens_re * image_re - sens_im * image_im, sens_re * image_im + sens_im * image_re], axis=1
    ).astype(jnp.bfloat16)
    half_k = jnp.dot(coil, forward_ref[...], preferred_element_type=jnp.float32).astype(jnp.bfloat16)
    table_re = table_re_ref[...]
    table_im = table_im_ref[...]
    kspace = jnp.dot(table_re, half_k, preferred_element_type=jnp.float32) + jnp.dot(
        table_im, swap_halves(half_k, half_width, True), preferred_element_type=jnp.float32
    )
    residual = (kspace - measured_ref[0].astype(jnp.float32)).astype(jnp.bfloat16)
    sampled = sampled_ref[0].astype(jnp.bfloat16)
    back_half = (
        jnp.dot(table_re * sampled, residual, preferred_element_type=jnp.float32)
        + jnp.dot(table_im * sampled, swap_halves(residual, half_width, False), preferred_element_type=jnp.float32)
    ).astype(jnp.bfloat16)
    coil_back = jnp.dot(back_half, adjoint_ref[...], preferred_element_type=jnp.float32)
    back_re = coil_back[:, :half_width]
    back_im = coil_back[:, half_width:]
    term = jnp.concatenate(
        [sens_re * back_re + sens_im * back_im, sens_re * back_im - sens_im * back_re], axis=1
    )

    @pl.when(step == 0)
    def _():
        total_ref[...] = term

    @pl.when(step > 0)
    def _():
        total_ref[...] += term

    @pl.when(step == pl.num_programs(0) - 1)
    def _():
        start = pl.multiple_of(me * rows, rows)
        own_ref[...] = total_ref[pl.ds(start, rows), :]
        for shift in range(1, groups):
            start = pl.multiple_of(((me + shift) % groups) * rows, rows)
            send_ref[shift - 1] = total_ref[pl.ds(start, rows), :].astype(jnp.bfloat16)


def coil_chain(pieces, place, sens, measured, sampled, forward_x, adjoint_x, table_y_re, table_y_im):
    coils, height, width = sens.shape
    groups = len(pieces)
    rows = pieces[0].shape[0]
    whole = lambda c: (0, 0)
    per_coil = lambda c: (c, 0, 0)
    flops = coils * 8 * height * width * width
    return pl.pallas_call(
        coil_chain_kernel,
        out_shape=(
            jax.ShapeDtypeStruct((rows, width), jnp.float32),
            jax.ShapeDtypeStruct((groups - 1, rows, width), jnp.bfloat16),
        ),
        grid=(coils,),
        in_specs=[pl.BlockSpec((rows, width), whole)] * groups
        + [
            pl.BlockSpec(memory_space=pltpu.SMEM),
            pl.BlockSpec((1, height, width), per_coil),
            pl.BlockSpec((1, height, width), per_coil),
            pl.BlockSpec((1, 1, height), per_coil),
            pl.BlockSpec((width, width), whole),
            pl.BlockSpec((width, width), whole),
            pl.BlockSpec((height, height), whole),
            pl.BlockSpec((height, height), whole),
        ],
        out_specs=(
            pl.BlockSpec((rows, width), whole),
            pl.BlockSpec((groups - 1, rows, width), lambda c: (0, 0, 0)),
        ),
        scratch_shapes=[pltpu.VMEM((height, width), jnp.bfloat16), pltpu.VMEM((height, width), jnp.float32)],
        compiler_params=pltpu.CompilerParams(dimension_semantics=("arbitrary",)),
        cost_estimate=pl.CostEstimate(
            flops=flops, transcendentals=0, bytes_accessed=2 * 2 * coils * height * width + 4 * height * width
        ),
    )(*pieces, place, sens, measured, sampled, forward_x, adjoint_x, table_y_re, table_y_im)


def on_device(factors, temporal, maps, kdata, masks):
    width_x = maps.shape[2] // 2
    width_y = maps.shape[1]
    rows_own = factors.shape[2]
    table_x_re, table_x_im = dft_parts(width_x)
    table_y_re, table_y_im = dft_parts(width_y)
    forward_x = jnp.asarray(np.block([[table_x_re, table_x_im], [-table_x_im, table_x_re]]))
    adjoint_x = jnp.asarray(np.block([[table_x_re, -table_x_im], [table_x_im, table_x_re]]))
    table_y_re = jnp.asarray(table_y_re)
    table_y_im = jnp.asarray(table_y_im)
    time_re = temporal[0]
    time_im = temporal[1]
    mixing = jnp.stack(
        [jnp.stack([time_re, -time_im], axis=1), jnp.stack([time_im, time_re], axis=1)], axis=1
    )
    images = jnp.sum(
        mixing[:, :, :, :, None, None] * factors[None, None], axis=(2, 3)
    ).astype(jnp.bfloat16)
    frames_here = images.shape[0]
    width_own = images.shape[3]
    groups = lax.axis_size("coil")
    frames = lax.axis_size("frame")
    me_c = lax.axis_index("coil")
    spread = jnp.broadcast_to(images[:, None], (frames, groups) + images.shape[1:]).reshape(
        (frames * groups,) + images.shape[1:]
    )
    arrived = lax.all_to_all(spread, ("frame", "coil"), 0, 0, tiled=True)
    full_rows = jnp.transpose(arrived.reshape((frames, groups) + images.shape[1:]), (1, 3, 2, 0, 4))
    full_rows = full_rows.reshape(groups, rows_own, 2 * width_x)
    pieces = [lax.dynamic_index_in_dim(full_rows, (me_c - step) % groups, 0, keepdims=False) for step in range(groups)]
    sampled = masks[0].astype(jnp.float32)[:, None, :]
    place = jnp.reshape(me_c, (1,)).astype(jnp.int32)
    own_total, outgoing = coil_chain(
        pieces, place, maps, kdata[0], sampled, forward_x, adjoint_x, table_y_re, table_y_im
    )
    total_rows = [None] * groups
    total_rows[0] = own_total
    for step in range(1, groups):
        total_rows[step] = outgoing[step - 1].astype(jnp.float32)
    ordered = jnp.take(jnp.stack(total_rows), (jnp.arange(groups) - me_c) % groups, axis=0)
    terms = jnp.transpose(
        ordered.reshape(groups, rows_own, 2, frames, width_own), (3, 0, 1, 2, 4)
    ).reshape((frames * groups, rows_own, 2, width_own))
    received = lax.all_to_all(terms.astype(jnp.bfloat16), ("frame", "coil"), 0, 0, tiled=True)
    returned = jnp.sum(
        received.reshape((frames, groups, rows_own, 2, width_own)).astype(jnp.float32), axis=1
    )
    weights = jnp.stack(
        [jnp.stack([time_re.T, time_im.T], axis=2), jnp.stack([-time_im.T, time_re.T], axis=2)], axis=0
    )
    gradient = jnp.sum(
        weights[:, :, :, None, :, None] * returned[None, None], axis=(2, 4)
    )
    return factors - 0.5 * gradient


def solution(mesh):
    placed = (
        P("slab", None, "coil", "frame"),
        P("slab", None, None),
        P("coil", "slab", None),
        P("frame", "coil", "slab", None),
        P("frame", "coil", "slab"),
    )
    return jax.shard_map(
        on_device,
        mesh=mesh,
        in_specs=placed,
        out_specs=P("slab", None, "coil", "frame"),
        check_vma=False,
    )
```

```python
import math

import jax
import ml_dtypes
import numpy as np
import jax.numpy as jnp
from jax import lax
from jax.experimental import pallas as pl
from jax.experimental.pallas import tpu as pltpu
from jax.sharding import PartitionSpec as P


def dft_parts(length):
    index = np.arange(length, dtype=np.int64)
    phase = (index[:, None] * index[None, :]) % length
    angle = np.float32(2.0 * math.pi / length) * phase.astype(np.float32)
    scale = np.float32(1.0 / math.sqrt(length))
    real = (np.cos(angle.astype(np.float64)).astype(np.float32) * scale).astype(ml_dtypes.bfloat16)
    imag = (-np.sin(angle.astype(np.float64)).astype(np.float32) * scale).astype(ml_dtypes.bfloat16)
    return real, imag


def rotate_plus(values, half_width):
    return jnp.concatenate([-values[..., half_width:], values[..., :half_width]], axis=-1)


def rotate_minus(values, half_width):
    return jnp.concatenate([values[..., half_width:], -values[..., :half_width]], axis=-1)


def sens_times(sens, values, half_width):
    sens_re = sens[..., :half_width].astype(jnp.float32)
    sens_im = sens[..., half_width:].astype(jnp.float32)
    value_re = values[..., :half_width].astype(jnp.float32)
    value_im = values[..., half_width:].astype(jnp.float32)
    return jnp.concatenate(
        [sens_re * value_re - sens_im * value_im, sens_re * value_im + sens_im * value_re], axis=-1
    )


def conj_sens_times(sens, values, half_width):
    sens_re = sens[..., :half_width].astype(jnp.float32)
    sens_im = sens[..., half_width:].astype(jnp.float32)
    value_re = values[..., :half_width]
    value_im = values[..., half_width:]
    return jnp.concatenate(
        [sens_re * value_re + sens_im * value_im, sens_re * value_im - sens_im * value_re], axis=-1
    )


def precise(form, first, second):
    return jnp.einsum(form, first, second, precision=lax.Precision.HIGHEST)


PERMUTE_LIMIT = 8


def shifted(count, step):
    return [(source, (source + step) % count) for source in range(count)]


def by_sender(pieces, count, me):
    ring = jnp.stack([pieces[0]] + pieces[1:][::-1])
    doubled = jnp.concatenate([ring, ring], axis=0)
    return lax.dynamic_slice_in_dim(doubled, (count - me) % count, count, 0)


def gather_blocks(value, axis):
    count = lax.axis_size(axis)
    if count > PERMUTE_LIMIT:
        return lax.all_gather(value, axis)
    me = lax.axis_index(axis)
    pieces = [value] + [lax.ppermute(value, axis, shifted(count, step)) for step in range(1, count)]
    return by_sender(pieces, count, me)


def exchange_blocks(blocks, axis):
    count = lax.axis_size(axis)
    if count > PERMUTE_LIMIT:
        return lax.all_to_all(blocks, axis, 0, 0, tiled=True)
    me = lax.axis_index(axis)
    pieces = [lax.dynamic_index_in_dim(blocks, me, 0, keepdims=False)]
    for step in range(1, count):
        outgoing = lax.dynamic_index_in_dim(blocks, (me + step) % count, 0, keepdims=False)
        pieces.append(lax.ppermute(outgoing, axis, shifted(count, step)))
    return by_sender(pieces, count, me)


def reduce_blocks(blocks, axis):
    count = lax.axis_size(axis)
    if count > PERMUTE_LIMIT:
        return lax.psum_scatter(blocks.astype(jnp.bfloat16), axis, scatter_dimension=0).astype(jnp.float32)
    me = lax.axis_index(axis)
    total = lax.dynamic_index_in_dim(blocks, me, 0, keepdims=False)
    for step in range(1, count):
        outgoing = lax.dynamic_index_in_dim(blocks, (me + step) % count, 0, keepdims=False)
        total = total + lax.ppermute(outgoing.astype(jnp.bfloat16), axis, shifted(count, step)).astype(jnp.float32)
    return total


def swap_halves(values, half_width, negate_first):
    low = values[:, :half_width]
    high = values[:, half_width:]
    if negate_first:
        return jnp.concatenate([-high, low], axis=1)
    return jnp.concatenate([high, -low], axis=1)


def coil_chain_kernel(*refs):
    groups = len(refs) - 13
    pieces = refs[:groups]
    place_ref, sens_ref, measured_ref, sampled_ref, forward_ref, adjoint_ref, table_ref = refs[groups:groups + 7]
    own_ref, send_ref = refs[groups + 7:groups + 9]
    image_re_ref, image_im_ref, total_re_ref, total_im_ref = refs[groups + 9:]
    rows = pieces[0].shape[0]
    half_width = image_re_ref.shape[1]
    height = image_re_ref.shape[0]
    me = place_ref[0]
    step = pl.program_id(0)

    @pl.when(step == 0)
    def _():
        for block in range(groups):
            source = (me - block + groups) % groups
            value = pieces[0][...]
            for other in range(1, groups):
                value = jnp.where(source == other, pieces[other][...], value)
            value = value.astype(jnp.float32)
            image_re_ref[block * rows:(block + 1) * rows, :] = value[:, :half_width]
            image_im_ref[block * rows:(block + 1) * rows, :] = value[:, half_width:]

    sens_re = sens_ref[0, :, :half_width].astype(jnp.float32)
    sens_im = sens_ref[0, :, half_width:].astype(jnp.float32)
    image_re = image_re_ref[...]
    image_im = image_im_ref[...]
    coil_re = (sens_re * image_re - sens_im * image_im).astype(jnp.bfloat16)
    coil_im = (sens_re * image_im + sens_im * image_re).astype(jnp.bfloat16)
    half_k = (
        jnp.dot(coil_re, forward_ref[:half_width, :], preferred_element_type=jnp.float32)
        + jnp.dot(coil_im, forward_ref[half_width:, :], preferred_element_type=jnp.float32)
    ).astype(jnp.bfloat16)
    table = table_ref[...]
    parts = jnp.dot(table, half_k, preferred_element_type=jnp.float32)
    kspace_re = parts[:height, :half_width] - parts[height:, half_width:]
    kspace_im = parts[:height, half_width:] + parts[height:, :half_width]
    residual = jnp.concatenate(
        [
            (kspace_re - measured_ref[0, :, :half_width].astype(jnp.float32)).astype(jnp.bfloat16),
            (kspace_im - measured_ref[0, :, half_width:].astype(jnp.float32)).astype(jnp.bfloat16),
        ],
        axis=1,
    )
    masked = table * sampled_ref[0].astype(jnp.bfloat16)
    parts = jnp.dot(masked, residual, preferred_element_type=jnp.float32)
    back_re = (parts[:height, :half_width] + parts[height:, half_width:]).astype(jnp.bfloat16)
    back_im = (parts[:height, half_width:] - parts[height:, :half_width]).astype(jnp.bfloat16)
    coil_back = jnp.dot(back_re, adjoint_ref[:half_width, :], preferred_element_type=jnp.float32) + jnp.dot(
        back_im, adjoint_ref[half_width:, :], preferred_element_type=jnp.float32
    )
    cb_re = coil_back[:, :half_width]
    cb_im = coil_back[:, half_width:]
    term_re = sens_re * cb_re + sens_im * cb_im
    term_im = sens_re * cb_im - sens_im * cb_re

    @pl.when(step == 0)
    def _():
        total_re_ref[...] = term_re
        total_im_ref[...] = term_im

    @pl.when(step > 0)
    def _():
        total_re_ref[...] += term_re
        total_im_ref[...] += term_im

    @pl.when(step == pl.num_programs(0) - 1)
    def _():
        start = pl.multiple_of(me * rows, rows)
        own_ref[:, :half_width] = total_re_ref[pl.ds(start, rows), :]
        own_ref[:, half_width:] = total_im_ref[pl.ds(start, rows), :]
        for shift in range(1, groups):
            start = pl.multiple_of(((me + shift) % groups) * rows, rows)
            send_ref[shift - 1, :, :half_width] = total_re_ref[pl.ds(start, rows), :].astype(jnp.bfloat16)
            send_ref[shift - 1, :, half_width:] = total_im_ref[pl.ds(start, rows), :].astype(jnp.bfloat16)


def coil_chain(pieces, place, sens, measured, sampled, forward_x, adjoint_x, table_y):
    coils, height, width = sens.shape
    groups = len(pieces)
    rows = pieces[0].shape[0]
    whole = lambda c: (0, 0)
    per_coil = lambda c: (c, 0, 0)
    flops = coils * 8 * height * width * width
    return pl.pallas_call(
        coil_chain_kernel,
        out_shape=(
            jax.ShapeDtypeStruct((rows, width), jnp.float32),
            jax.ShapeDtypeStruct((groups - 1, rows, width), jnp.bfloat16),
        ),
        grid=(coils,),
        in_specs=[pl.BlockSpec((rows, width), whole)] * groups
        + [
            pl.BlockSpec(memory_space=pltpu.SMEM),
            pl.BlockSpec((1, height, width), per_coil),
            pl.BlockSpec((1, height, width), per_coil),
            pl.BlockSpec((1, 1, height), per_coil),
            pl.BlockSpec((width, width), whole),
            pl.BlockSpec((width, width), whole),
            pl.BlockSpec((2 * height, height), whole),
        ],
        out_specs=(
            pl.BlockSpec((rows, width), whole),
            pl.BlockSpec((groups - 1, rows, width), lambda c: (0, 0, 0)),
        ),
        scratch_shapes=[pltpu.VMEM((height, width // 2), jnp.float32)] * 4,
        compiler_params=pltpu.CompilerParams(dimension_semantics=("arbitrary",)),
        cost_estimate=pl.CostEstimate(
            flops=flops, transcendentals=0, bytes_accessed=2 * 2 * coils * height * width + 4 * height * width
        ),
    )(*pieces, place, sens, measured, sampled, forward_x, adjoint_x, table_y)


def on_device(factors, temporal, maps, kdata, masks):
    width_x = maps.shape[2] // 2
    width_y = maps.shape[1]
    rows_own = factors.shape[2]
    table_x_re, table_x_im = dft_parts(width_x)
    table_y_re, table_y_im = dft_parts(width_y)
    forward_x = jnp.asarray(np.block([[table_x_re, table_x_im], [-table_x_im, table_x_re]]))
    adjoint_x = jnp.asarray(np.block([[table_x_re, -table_x_im], [table_x_im, table_x_re]]))
    table_y = jnp.asarray(np.concatenate([table_y_re, table_y_im], axis=0))
    time_re = temporal[0]
    time_im = temporal[1]
    mixing = jnp.stack(
        [jnp.stack([time_re, -time_im], axis=1), jnp.stack([time_im, time_re], axis=1)], axis=1
    )
    images = jnp.sum(
        mixing[:, :, :, :, None, None] * factors[None, None], axis=(2, 3)
    ).astype(jnp.bfloat16)
    frames_here = images.shape[0]
    width_own = images.shape[3]
    pieces_x = exchange_blocks(images, "frame")
    own_rows = jnp.transpose(pieces_x, (2, 1, 0, 3)).reshape(rows_own, 2 * width_x)
    groups = lax.axis_size("coil")
    me_c = lax.axis_index("coil")
    pieces = [own_rows] + [lax.ppermute(own_rows, "coil", shifted(groups, step)) for step in range(1, groups)]
    sampled = masks[0].astype(jnp.float32)[:, None, :]
    place = jnp.reshape(me_c, (1,)).astype(jnp.int32)
    own_total, outgoing = coil_chain(
        pieces, place, maps, kdata[0], sampled, forward_x, adjoint_x, table_y
    )
    own_share = own_total
    for step in range(1, groups):
        own_share = own_share + lax.ppermute(outgoing[step - 1], "coil", shifted(groups, step)).astype(jnp.float32)
    outgoing = jnp.transpose(
        own_share.reshape(rows_own, 2, frames_here, width_own), (2, 0, 1, 3)
    ).astype(jnp.bfloat16)
    returned = exchange_blocks(outgoing, "frame").astype(jnp.float32)
    weights = jnp.stack(
        [jnp.stack([time_re.T, time_im.T], axis=2), jnp.stack([-time_im.T, time_re.T], axis=2)], axis=0
    )
    gradient = jnp.sum(
        weights[:, :, :, None, :, None] * returned[None, None], axis=(2, 4)
    )
    return factors - 0.5 * gradient


def solution(mesh):
    placed = (
        P("slab", None, "coil", "frame"),
        P("slab", None, None),
        P("coil", "slab", None),
        P("frame", "coil", "slab", None),
        P("frame", "coil", "slab"),
    )
    return jax.shard_map(
        on_device,
        mesh=mesh,
        in_specs=placed,
        out_specs=P("slab", None, "coil", "frame"),
        check_vma=False,
    )
```

```python
import math

import jax
import ml_dtypes
import numpy as np
import jax.numpy as jnp
from jax import lax
from jax.experimental import pallas as pl
from jax.experimental.pallas import tpu as pltpu
from jax.sharding import PartitionSpec as P


def dft_parts(length):
    index = np.arange(length, dtype=np.int64)
    phase = (index[:, None] * index[None, :]) % length
    angle = np.float32(2.0 * math.pi / length) * phase.astype(np.float32)
    scale = np.float32(1.0 / math.sqrt(length))
    real = (np.cos(angle.astype(np.float64)).astype(np.float32) * scale).astype(ml_dtypes.bfloat16)
    imag = (-np.sin(angle.astype(np.float64)).astype(np.float32) * scale).astype(ml_dtypes.bfloat16)
    return real, imag


def rotate_plus(values, half_width):
    return jnp.concatenate([-values[..., half_width:], values[..., :half_width]], axis=-1)


def rotate_minus(values, half_width):
    return jnp.concatenate([values[..., half_width:], -values[..., :half_width]], axis=-1)


def sens_times(sens, values, half_width):
    sens_re = sens[..., :half_width].astype(jnp.float32)
    sens_im = sens[..., half_width:].astype(jnp.float32)
    value_re = values[..., :half_width].astype(jnp.float32)
    value_im = values[..., half_width:].astype(jnp.float32)
    return jnp.concatenate(
        [sens_re * value_re - sens_im * value_im, sens_re * value_im + sens_im * value_re], axis=-1
    )


def conj_sens_times(sens, values, half_width):
    sens_re = sens[..., :half_width].astype(jnp.float32)
    sens_im = sens[..., half_width:].astype(jnp.float32)
    value_re = values[..., :half_width]
    value_im = values[..., half_width:]
    return jnp.concatenate(
        [sens_re * value_re + sens_im * value_im, sens_re * value_im - sens_im * value_re], axis=-1
    )


def precise(form, first, second):
    return jnp.einsum(form, first, second, precision=lax.Precision.HIGHEST)


PERMUTE_LIMIT = 8


def shifted(count, step):
    return [(source, (source + step) % count) for source in range(count)]


def by_sender(pieces, count, me):
    ring = jnp.stack([pieces[0]] + pieces[1:][::-1])
    doubled = jnp.concatenate([ring, ring], axis=0)
    return lax.dynamic_slice_in_dim(doubled, (count - me) % count, count, 0)


def gather_blocks(value, axis):
    count = lax.axis_size(axis)
    if count > PERMUTE_LIMIT:
        return lax.all_gather(value, axis)
    me = lax.axis_index(axis)
    pieces = [value] + [lax.ppermute(value, axis, shifted(count, step)) for step in range(1, count)]
    return by_sender(pieces, count, me)


def exchange_blocks(blocks, axis):
    count = lax.axis_size(axis)
    if count > PERMUTE_LIMIT:
        return lax.all_to_all(blocks, axis, 0, 0, tiled=True)
    me = lax.axis_index(axis)
    pieces = [lax.dynamic_index_in_dim(blocks, me, 0, keepdims=False)]
    for step in range(1, count):
        outgoing = lax.dynamic_index_in_dim(blocks, (me + step) % count, 0, keepdims=False)
        pieces.append(lax.ppermute(outgoing, axis, shifted(count, step)))
    return by_sender(pieces, count, me)


def reduce_blocks(blocks, axis):
    count = lax.axis_size(axis)
    if count > PERMUTE_LIMIT:
        return lax.psum_scatter(blocks.astype(jnp.bfloat16), axis, scatter_dimension=0).astype(jnp.float32)
    me = lax.axis_index(axis)
    total = lax.dynamic_index_in_dim(blocks, me, 0, keepdims=False)
    for step in range(1, count):
        outgoing = lax.dynamic_index_in_dim(blocks, (me + step) % count, 0, keepdims=False)
        total = total + lax.ppermute(outgoing.astype(jnp.bfloat16), axis, shifted(count, step)).astype(jnp.float32)
    return total


def swap_halves(values, half_width, negate_first):
    low = values[:, :half_width]
    high = values[:, half_width:]
    if negate_first:
        return jnp.concatenate([-high, low], axis=1)
    return jnp.concatenate([high, -low], axis=1)


def coil_term(coil_index, image_ref, sens_ref, measured_ref, sampled_ref, forward_ref, adjoint_ref,
              table_re_ref, table_im_ref):
    half_width = image_ref.shape[1] // 2
    sens = sens_ref[coil_index].astype(jnp.float32)
    sens_re = sens[:, :half_width]
    sens_im = sens[:, half_width:]
    image = image_ref[...].astype(jnp.float32)
    image_re = image[:, :half_width]
    image_im = image[:, half_width:]
    coil = jnp.concatenate(
        [sens_re * image_re - sens_im * image_im, sens_re * image_im + sens_im * image_re], axis=1
    ).astype(jnp.bfloat16)
    half_k = jnp.dot(coil, forward_ref[...], preferred_element_type=jnp.float32).astype(jnp.bfloat16)
    table_re = table_re_ref[...]
    table_im = table_im_ref[...]
    kspace = jnp.dot(table_re, half_k, preferred_element_type=jnp.float32) + jnp.dot(
        table_im, swap_halves(half_k, half_width, True), preferred_element_type=jnp.float32
    )
    residual = (kspace - measured_ref[coil_index].astype(jnp.float32)).astype(jnp.bfloat16)
    sampled = sampled_ref[coil_index].astype(jnp.bfloat16)
    back_half = (
        jnp.dot(table_re * sampled, residual, preferred_element_type=jnp.float32)
        + jnp.dot(table_im * sampled, swap_halves(residual, half_width, False), preferred_element_type=jnp.float32)
    ).astype(jnp.bfloat16)
    coil_back = jnp.dot(back_half, adjoint_ref[...], preferred_element_type=jnp.float32)
    back_re = coil_back[:, :half_width]
    back_im = coil_back[:, half_width:]
    term = jnp.concatenate(
        [sens_re * back_re + sens_im * back_im, sens_re * back_im - sens_im * back_re], axis=1
    )

    return term


def coil_chain_kernel(*refs):
    groups = len(refs) - 12
    pieces = refs[:groups]
    place_ref, sens_ref, measured_ref, sampled_ref, forward_ref, adjoint_ref, table_re_ref, table_im_ref = refs[
        groups:groups + 8
    ]
    own_ref, send_ref = refs[groups + 8:groups + 10]
    image_ref, total_ref = refs[groups + 10:]
    rows = pieces[0].shape[0]
    half_width = image_ref.shape[1] // 2
    me = place_ref[0]
    step = pl.program_id(0)

    @pl.when(step == 0)
    def _():
        for block in range(groups):
            source = (me - block + groups) % groups
            value = pieces[0][...]
            for other in range(1, groups):
                value = jnp.where(source == other, pieces[other][...], value)
            image_ref[block * rows:(block + 1) * rows, :] = value

    term = None
    for coil_index in range(sens_ref.shape[0]):
        one = coil_term(coil_index, image_ref, sens_ref, measured_ref, sampled_ref, forward_ref, adjoint_ref,
                        table_re_ref, table_im_ref)
        term = one if term is None else term + one

    @pl.when(step == 0)
    def _():
        total_ref[...] = term

    @pl.when(step > 0)
    def _():
        total_ref[...] += term

    @pl.when(step == pl.num_programs(0) - 1)
    def _():
        start = pl.multiple_of(me * rows, rows)
        own_ref[...] = total_ref[pl.ds(start, rows), :]
        for shift in range(1, groups):
            start = pl.multiple_of(((me + shift) % groups) * rows, rows)
            send_ref[shift - 1] = total_ref[pl.ds(start, rows), :].astype(jnp.bfloat16)


def coil_chain(pieces, place, sens, measured, sampled, forward_x, adjoint_x, table_y_re, table_y_im):
    coils, height, width = sens.shape
    groups = len(pieces)
    rows = pieces[0].shape[0]
    whole = lambda c: (0, 0)
    per_coil = lambda c: (c, 0, 0)
    step_coils = 2 if coils % 2 == 0 else 1
    flops = coils * 8 * height * width * width
    return pl.pallas_call(
        coil_chain_kernel,
        out_shape=(
            jax.ShapeDtypeStruct((rows, width), jnp.float32),
            jax.ShapeDtypeStruct((groups - 1, rows, width), jnp.bfloat16),
        ),
        grid=(coils // step_coils,),
        in_specs=[pl.BlockSpec((rows, width), whole)] * groups
        + [
            pl.BlockSpec(memory_space=pltpu.SMEM),
            pl.BlockSpec((step_coils, height, width), per_coil),
            pl.BlockSpec((step_coils, height, width), per_coil),
            pl.BlockSpec((step_coils, 1, height), per_coil),
            pl.BlockSpec((width, width), whole),
            pl.BlockSpec((width, width), whole),
            pl.BlockSpec((height, height), whole),
            pl.BlockSpec((height, height), whole),
        ],
        out_specs=(
            pl.BlockSpec((rows, width), whole),
            pl.BlockSpec((groups - 1, rows, width), lambda c: (0, 0, 0)),
        ),
        scratch_shapes=[pltpu.VMEM((height, width), jnp.bfloat16), pltpu.VMEM((height, width), jnp.float32)],
        compiler_params=pltpu.CompilerParams(dimension_semantics=("arbitrary",)),
        cost_estimate=pl.CostEstimate(
            flops=flops, transcendentals=0, bytes_accessed=2 * 2 * coils * height * width + 4 * height * width
        ),
    )(*pieces, place, sens, measured, sampled, forward_x, adjoint_x, table_y_re, table_y_im)


def on_device(factors, temporal, maps, kdata, masks):
    width_x = maps.shape[2] // 2
    width_y = maps.shape[1]
    rows_own = factors.shape[2]
    table_x_re, table_x_im = dft_parts(width_x)
    table_y_re, table_y_im = dft_parts(width_y)
    forward_x = jnp.asarray(np.block([[table_x_re, table_x_im], [-table_x_im, table_x_re]]))
    adjoint_x = jnp.asarray(np.block([[table_x_re, -table_x_im], [table_x_im, table_x_re]]))
    table_y_re = jnp.asarray(table_y_re)
    table_y_im = jnp.asarray(table_y_im)
    time_re = temporal[0]
    time_im = temporal[1]
    mixing = jnp.stack(
        [jnp.stack([time_re, -time_im], axis=1), jnp.stack([time_im, time_re], axis=1)], axis=1
    )
    images = jnp.sum(
        mixing[:, :, :, :, None, None] * factors[None, None], axis=(2, 3)
    ).astype(jnp.bfloat16)
    frames_here = images.shape[0]
    width_own = images.shape[3]
    pieces_x = exchange_blocks(images, "frame")
    own_rows = jnp.transpose(pieces_x, (2, 1, 0, 3)).reshape(rows_own, 2 * width_x)
    groups = lax.axis_size("coil")
    me_c = lax.axis_index("coil")
    pieces = [own_rows] + [lax.ppermute(own_rows, "coil", shifted(groups, step)) for step in range(1, groups)]
    sampled = masks[0].astype(jnp.float32)[:, None, :]
    place = jnp.reshape(me_c, (1,)).astype(jnp.int32)
    own_total, outgoing = coil_chain(
        pieces, place, maps, kdata[0], sampled, forward_x, adjoint_x, table_y_re, table_y_im
    )
    own_share = own_total
    for step in range(1, groups):
        own_share = own_share + lax.ppermute(outgoing[step - 1], "coil", shifted(groups, step)).astype(jnp.float32)
    outgoing = jnp.transpose(
        own_share.reshape(rows_own, 2, frames_here, width_own), (2, 0, 1, 3)
    ).astype(jnp.bfloat16)
    returned = exchange_blocks(outgoing, "frame").astype(jnp.float32)
    weights = jnp.stack(
        [jnp.stack([time_re.T, time_im.T], axis=2), jnp.stack([-time_im.T, time_re.T], axis=2)], axis=0
    )
    gradient = jnp.sum(
        weights[:, :, :, None, :, None] * returned[None, None], axis=(2, 4)
    )
    return factors - 0.5 * gradient


def solution(mesh):
    placed = (
        P("slab", None, "coil", "frame"),
        P("slab", None, None),
        P("coil", "slab", None),
        P("frame", "coil", "slab", None),
        P("frame", "coil", "slab"),
    )
    return jax.shard_map(
        on_device,
        mesh=mesh,
        in_specs=placed,
        out_specs=P("slab", None, "coil", "frame"),
        check_vma=False,
    )
```

```python
import math

import jax
import ml_dtypes
import numpy as np
import jax.numpy as jnp
from jax import lax
from jax.experimental import pallas as pl
from jax.experimental.pallas import tpu as pltpu
from jax.sharding import PartitionSpec as P


def dft_parts(length):
    index = np.arange(length, dtype=np.int64)
    phase = (index[:, None] * index[None, :]) % length
    angle = np.float32(2.0 * math.pi / length) * phase.astype(np.float32)
    scale = np.float32(1.0 / math.sqrt(length))
    real = (np.cos(angle.astype(np.float64)).astype(np.float32) * scale).astype(ml_dtypes.bfloat16)
    imag = (-np.sin(angle.astype(np.float64)).astype(np.float32) * scale).astype(ml_dtypes.bfloat16)
    return real, imag


def rotate_plus(values, half_width):
    return jnp.concatenate([-values[..., half_width:], values[..., :half_width]], axis=-1)


def rotate_minus(values, half_width):
    return jnp.concatenate([values[..., half_width:], -values[..., :half_width]], axis=-1)


def sens_times(sens, values, half_width):
    sens_re = sens[..., :half_width].astype(jnp.float32)
    sens_im = sens[..., half_width:].astype(jnp.float32)
    value_re = values[..., :half_width].astype(jnp.float32)
    value_im = values[..., half_width:].astype(jnp.float32)
    return jnp.concatenate(
        [sens_re * value_re - sens_im * value_im, sens_re * value_im + sens_im * value_re], axis=-1
    )


def conj_sens_times(sens, values, half_width):
    sens_re = sens[..., :half_width].astype(jnp.float32)
    sens_im = sens[..., half_width:].astype(jnp.float32)
    value_re = values[..., :half_width]
    value_im = values[..., half_width:]
    return jnp.concatenate(
        [sens_re * value_re + sens_im * value_im, sens_re * value_im - sens_im * value_re], axis=-1
    )


def precise(form, first, second):
    return jnp.einsum(form, first, second, precision=lax.Precision.HIGHEST)


PERMUTE_LIMIT = 8


def shifted(count, step):
    return [(source, (source + step) % count) for source in range(count)]


def by_sender(pieces, count, me):
    ring = jnp.stack([pieces[0]] + pieces[1:][::-1])
    doubled = jnp.concatenate([ring, ring], axis=0)
    return lax.dynamic_slice_in_dim(doubled, (count - me) % count, count, 0)


def gather_blocks(value, axis):
    count = lax.axis_size(axis)
    if count > PERMUTE_LIMIT:
        return lax.all_gather(value, axis)
    me = lax.axis_index(axis)
    pieces = [value] + [lax.ppermute(value, axis, shifted(count, step)) for step in range(1, count)]
    return by_sender(pieces, count, me)


def exchange_blocks(blocks, axis):
    count = lax.axis_size(axis)
    if count > PERMUTE_LIMIT:
        return lax.all_to_all(blocks, axis, 0, 0, tiled=True)
    me = lax.axis_index(axis)
    pieces = [lax.dynamic_index_in_dim(blocks, me, 0, keepdims=False)]
    for step in range(1, count):
        outgoing = lax.dynamic_index_in_dim(blocks, (me + step) % count, 0, keepdims=False)
        pieces.append(lax.ppermute(outgoing, axis, shifted(count, step)))
    return by_sender(pieces, count, me)


def reduce_blocks(blocks, axis):
    count = lax.axis_size(axis)
    if count > PERMUTE_LIMIT:
        return lax.psum_scatter(blocks.astype(jnp.bfloat16), axis, scatter_dimension=0).astype(jnp.float32)
    me = lax.axis_index(axis)
    total = lax.dynamic_index_in_dim(blocks, me, 0, keepdims=False)
    for step in range(1, count):
        outgoing = lax.dynamic_index_in_dim(blocks, (me + step) % count, 0, keepdims=False)
        total = total + lax.ppermute(outgoing.astype(jnp.bfloat16), axis, shifted(count, step)).astype(jnp.float32)
    return total


def swap_halves(values, half_width, negate_first):
    low = values[:, :half_width]
    high = values[:, half_width:]
    if negate_first:
        return jnp.concatenate([-high, low], axis=1)
    return jnp.concatenate([high, -low], axis=1)


def coil_term(coil_index, image_ref, sens_ref, measured_ref, sampled_ref, forward_ref, adjoint_ref,
              table_re_ref, table_im_ref):
    half_width = image_ref.shape[1] // 2
    sens = sens_ref[coil_index].astype(jnp.float32)
    sens_re = sens[:, :half_width]
    sens_im = sens[:, half_width:]
    image = image_ref[...].astype(jnp.float32)
    image_re = image[:, :half_width]
    image_im = image[:, half_width:]
    coil = jnp.concatenate(
        [sens_re * image_re - sens_im * image_im, sens_re * image_im + sens_im * image_re], axis=1
    ).astype(jnp.bfloat16)
    half_k = jnp.dot(coil, forward_ref[...], preferred_element_type=jnp.float32).astype(jnp.bfloat16)
    table_re = table_re_ref[...]
    table_im = table_im_ref[...]
    kspace = jnp.dot(table_re, half_k, preferred_element_type=jnp.float32) + jnp.dot(
        table_im, swap_halves(half_k, half_width, True), preferred_element_type=jnp.float32
    )
    residual = (kspace - measured_ref[coil_index].astype(jnp.float32)).astype(jnp.bfloat16)
    sampled = sampled_ref[coil_index].astype(jnp.bfloat16)
    back_half = (
        jnp.dot(table_re * sampled, residual, preferred_element_type=jnp.float32)
        + jnp.dot(table_im * sampled, swap_halves(residual, half_width, False), preferred_element_type=jnp.float32)
    ).astype(jnp.bfloat16)
    coil_back = jnp.dot(back_half, adjoint_ref[...], preferred_element_type=jnp.float32)
    back_re = coil_back[:, :half_width]
    back_im = coil_back[:, half_width:]
    term = jnp.concatenate(
        [sens_re * back_re + sens_im * back_im, sens_re * back_im - sens_im * back_re], axis=1
    )

    return term


def coil_chain_kernel(image_ref, sens_ref, measured_ref, sampled_ref, forward_ref, adjoint_ref,
                      table_re_ref, table_im_ref, total_ref):
    step = pl.program_id(0)
    term = None
    for coil_index in range(sens_ref.shape[0]):
        one = coil_term(coil_index, image_ref, sens_ref, measured_ref, sampled_ref, forward_ref, adjoint_ref,
                        table_re_ref, table_im_ref)
        term = one if term is None else term + one

    @pl.when(step == 0)
    def _():
        total_ref[...] = term

    @pl.when(step > 0)
    def _():
        total_ref[...] += term


def coil_chain(image, sens, measured, sampled, forward_x, adjoint_x, table_y_re, table_y_im):
    coils, height, width = sens.shape
    whole = lambda c: (0, 0)
    per_coil = lambda c: (c, 0, 0)
    step_coils = 2 if coils % 2 == 0 else 1
    flops = coils * 8 * height * width * width
    return pl.pallas_call(
        coil_chain_kernel,
        out_shape=jax.ShapeDtypeStruct((height, width), jnp.float32),
        grid=(coils // step_coils,),
        in_specs=[
            pl.BlockSpec((height, width), whole),
            pl.BlockSpec((step_coils, height, width), per_coil),
            pl.BlockSpec((step_coils, height, width), per_coil),
            pl.BlockSpec((step_coils, 1, height), per_coil),
            pl.BlockSpec((width, width), whole),
            pl.BlockSpec((width, width), whole),
            pl.BlockSpec((height, height), whole),
            pl.BlockSpec((height, height), whole),
        ],
        out_specs=pl.BlockSpec((height, width), whole),
        compiler_params=pltpu.CompilerParams(dimension_semantics=("arbitrary",)),
        cost_estimate=pl.CostEstimate(
            flops=flops, transcendentals=0, bytes_accessed=2 * 2 * coils * height * width + 4 * height * width
        ),
    )(image, sens, measured, sampled, forward_x, adjoint_x, table_y_re, table_y_im)


def doubling_gather(value, axis):
    count = lax.axis_size(axis)
    me = lax.axis_index(axis)
    span = 1
    while span < count:
        other = lax.ppermute(value, axis, [(i, i ^ span) for i in range(count)])
        upper = (me & span) != 0
        value = jnp.concatenate([jnp.where(upper, other, value), jnp.where(upper, value, other)], axis=0)
        span *= 2
    return value


def halving_reduce(total, axis):
    count = lax.axis_size(axis)
    me = lax.axis_index(axis)
    span = count // 2
    while span >= 1:
        size = total.shape[0] // 2
        low = total[:size]
        high = total[size:]
        upper = (me & span) != 0
        keep = jnp.where(upper, high, low)
        give = jnp.where(upper, low, high)
        other = lax.ppermute(give.astype(jnp.bfloat16), axis, [(i, i ^ span) for i in range(count)])
        total = keep + other.astype(jnp.float32)
        span //= 2
    return total


def on_device(factors, temporal, maps, kdata, masks):
    width_x = maps.shape[2] // 2
    width_y = maps.shape[1]
    rows_own = factors.shape[2]
    table_x_re, table_x_im = dft_parts(width_x)
    table_y_re, table_y_im = dft_parts(width_y)
    forward_x = jnp.asarray(np.block([[table_x_re, table_x_im], [-table_x_im, table_x_re]]))
    adjoint_x = jnp.asarray(np.block([[table_x_re, -table_x_im], [table_x_im, table_x_re]]))
    table_y_re = jnp.asarray(table_y_re)
    table_y_im = jnp.asarray(table_y_im)
    time_re = temporal[0]
    time_im = temporal[1]
    mixing = jnp.stack(
        [jnp.stack([time_re, -time_im], axis=1), jnp.stack([time_im, time_re], axis=1)], axis=1
    )
    images = jnp.sum(
        mixing[:, :, :, :, None, None] * factors[None, None], axis=(2, 3)
    ).astype(jnp.bfloat16)
    frames_here = images.shape[0]
    width_own = images.shape[3]
    pieces_x = exchange_blocks(images, "frame")
    own_rows = jnp.transpose(pieces_x, (2, 1, 0, 3)).reshape(rows_own, 2 * width_x)
    groups = lax.axis_size("coil")
    sampled = masks[0].astype(jnp.float32)[:, None, :]
    if groups & (groups - 1) == 0:
        full_image = doubling_gather(own_rows, "coil")
    else:
        full_image = gather_blocks(own_rows, "coil").reshape(width_y, 2 * width_x)
    combined = coil_chain(full_image, maps, kdata[0], sampled, forward_x, adjoint_x, table_y_re, table_y_im)
    if groups & (groups - 1) == 0:
        own_share = halving_reduce(combined, "coil")
    else:
        own_share = reduce_blocks(combined.reshape(groups, rows_own, 2 * width_x), "coil")
    outgoing = jnp.transpose(
        own_share.reshape(rows_own, 2, frames_here, width_own), (2, 0, 1, 3)
    ).astype(jnp.bfloat16)
    returned = exchange_blocks(outgoing, "frame").astype(jnp.float32)
    weights = jnp.stack(
        [jnp.stack([time_re.T, time_im.T], axis=2), jnp.stack([-time_im.T, time_re.T], axis=2)], axis=0
    )
    gradient = jnp.sum(
        weights[:, :, :, None, :, None] * returned[None, None], axis=(2, 4)
    )
    return factors - 0.5 * gradient


def solution(mesh):
    placed = (
        P("slab", None, "coil", "frame"),
        P("slab", None, None),
        P("coil", "slab", None),
        P("frame", "coil", "slab", None),
        P("frame", "coil", "slab"),
    )
    return jax.shard_map(
        on_device,
        mesh=mesh,
        in_specs=placed,
        out_specs=P("slab", None, "coil", "frame"),
        check_vma=False,
    )
```

```python
import math

import jax
import ml_dtypes
import numpy as np
import jax.numpy as jnp
from jax import lax
from jax.experimental import pallas as pl
from jax.experimental.pallas import tpu as pltpu
from jax.sharding import PartitionSpec as P


def dft_parts(length):
    index = np.arange(length, dtype=np.int64)
    phase = (index[:, None] * index[None, :]) % length
    angle = np.float32(2.0 * math.pi / length) * phase.astype(np.float32)
    scale = np.float32(1.0 / math.sqrt(length))
    real = (np.cos(angle.astype(np.float64)).astype(np.float32) * scale).astype(ml_dtypes.bfloat16)
    imag = (-np.sin(angle.astype(np.float64)).astype(np.float32) * scale).astype(ml_dtypes.bfloat16)
    return real, imag


def rotate_plus(values, half_width):
    return jnp.concatenate([-values[..., half_width:], values[..., :half_width]], axis=-1)


def rotate_minus(values, half_width):
    return jnp.concatenate([values[..., half_width:], -values[..., :half_width]], axis=-1)


def sens_times(sens, values, half_width):
    sens_re = sens[..., :half_width].astype(jnp.float32)
    sens_im = sens[..., half_width:].astype(jnp.float32)
    value_re = values[..., :half_width].astype(jnp.float32)
    value_im = values[..., half_width:].astype(jnp.float32)
    return jnp.concatenate(
        [sens_re * value_re - sens_im * value_im, sens_re * value_im + sens_im * value_re], axis=-1
    )


def conj_sens_times(sens, values, half_width):
    sens_re = sens[..., :half_width].astype(jnp.float32)
    sens_im = sens[..., half_width:].astype(jnp.float32)
    value_re = values[..., :half_width]
    value_im = values[..., half_width:]
    return jnp.concatenate(
        [sens_re * value_re + sens_im * value_im, sens_re * value_im - sens_im * value_re], axis=-1
    )


def precise(form, first, second):
    return jnp.einsum(form, first, second, precision=lax.Precision.HIGHEST)


PERMUTE_LIMIT = 8


def shifted(count, step):
    return [(source, (source + step) % count) for source in range(count)]


def by_sender(pieces, count, me):
    ring = jnp.stack([pieces[0]] + pieces[1:][::-1])
    doubled = jnp.concatenate([ring, ring], axis=0)
    return lax.dynamic_slice_in_dim(doubled, (count - me) % count, count, 0)


def gather_blocks(value, axis):
    count = lax.axis_size(axis)
    if count > PERMUTE_LIMIT:
        return lax.all_gather(value, axis)
    me = lax.axis_index(axis)
    pieces = [value] + [lax.ppermute(value, axis, shifted(count, step)) for step in range(1, count)]
    return by_sender(pieces, count, me)


def exchange_blocks(blocks, axis):
    count = lax.axis_size(axis)
    if count > PERMUTE_LIMIT:
        return lax.all_to_all(blocks, axis, 0, 0, tiled=True)
    me = lax.axis_index(axis)
    pieces = [lax.dynamic_index_in_dim(blocks, me, 0, keepdims=False)]
    for step in range(1, count):
        outgoing = lax.dynamic_index_in_dim(blocks, (me + step) % count, 0, keepdims=False)
        pieces.append(lax.ppermute(outgoing, axis, shifted(count, step)))
    return by_sender(pieces, count, me)


def reduce_blocks(blocks, axis):
    count = lax.axis_size(axis)
    if count > PERMUTE_LIMIT:
        return lax.psum_scatter(blocks.astype(jnp.bfloat16), axis, scatter_dimension=0).astype(jnp.float32)
    me = lax.axis_index(axis)
    total = lax.dynamic_index_in_dim(blocks, me, 0, keepdims=False)
    for step in range(1, count):
        outgoing = lax.dynamic_index_in_dim(blocks, (me + step) % count, 0, keepdims=False)
        total = total + lax.ppermute(outgoing.astype(jnp.bfloat16), axis, shifted(count, step)).astype(jnp.float32)
    return total


def swap_halves(values, half_width, negate_first):
    low = values[:, :half_width]
    high = values[:, half_width:]
    if negate_first:
        return jnp.concatenate([-high, low], axis=1)
    return jnp.concatenate([high, -low], axis=1)


def coil_term(coil_index, image_ref, sens_ref, measured_ref, sampled_ref, forward_ref, adjoint_ref,
              table_re_ref, table_im_ref):
    half_width = image_ref.shape[1] // 2
    sens = sens_ref[coil_index].astype(jnp.float32)
    sens_re = sens[:, :half_width]
    sens_im = sens[:, half_width:]
    image = image_ref[...].astype(jnp.float32)
    image_re = image[:, :half_width]
    image_im = image[:, half_width:]
    coil = jnp.concatenate(
        [sens_re * image_re - sens_im * image_im, sens_re * image_im + sens_im * image_re], axis=1
    ).astype(jnp.bfloat16)
    half_k = jnp.dot(coil, forward_ref[...], preferred_element_type=jnp.float32).astype(jnp.bfloat16)
    table_re = table_re_ref[...]
    table_im = table_im_ref[...]
    kspace = jnp.dot(table_re, half_k, preferred_element_type=jnp.float32) + jnp.dot(
        table_im, swap_halves(half_k, half_width, True), preferred_element_type=jnp.float32
    )
    residual = (kspace - measured_ref[coil_index].astype(jnp.float32)).astype(jnp.bfloat16)
    sampled = sampled_ref[coil_index].astype(jnp.bfloat16)
    back_half = (
        jnp.dot(table_re * sampled, residual, preferred_element_type=jnp.float32)
        + jnp.dot(table_im * sampled, swap_halves(residual, half_width, False), preferred_element_type=jnp.float32)
    ).astype(jnp.bfloat16)
    coil_back = jnp.dot(back_half, adjoint_ref[...], preferred_element_type=jnp.float32)
    back_re = coil_back[:, :half_width]
    back_im = coil_back[:, half_width:]
    term = jnp.concatenate(
        [sens_re * back_re + sens_im * back_im, sens_re * back_im - sens_im * back_re], axis=1
    )

    return term


def coil_chain_kernel(*refs):
    groups = len(refs) - 12
    pieces = refs[:groups]
    place_ref, sens_ref, measured_ref, sampled_ref, forward_ref, adjoint_ref, table_re_ref, table_im_ref = refs[
        groups:groups + 8
    ]
    own_ref, send_ref = refs[groups + 8:groups + 10]
    image_ref, total_ref = refs[groups + 10:]
    rows = pieces[0].shape[0]
    half_width = image_ref.shape[1] // 2
    me = place_ref[0]
    step = pl.program_id(0)

    @pl.when(step == 0)
    def _():
        for block in range(groups):
            source = (me - block + groups) % groups
            value = pieces[0][...]
            for other in range(1, groups):
                value = jnp.where(source == other, pieces[other][...], value)
            image_ref[block * rows:(block + 1) * rows, :] = value

    term = None
    for coil_index in range(sens_ref.shape[0]):
        one = coil_term(coil_index, image_ref, sens_ref, measured_ref, sampled_ref, forward_ref, adjoint_ref,
                        table_re_ref, table_im_ref)
        term = one if term is None else term + one

    @pl.when(step == 0)
    def _():
        total_ref[...] = term

    @pl.when(step > 0)
    def _():
        total_ref[...] += term

    @pl.when(step == pl.num_programs(0) - 1)
    def _():
        start = pl.multiple_of(me * rows, rows)
        own_ref[...] = total_ref[pl.ds(start, rows), :]
        for shift in range(1, groups):
            start = pl.multiple_of(((me + shift) % groups) * rows, rows)
            send_ref[shift - 1] = total_ref[pl.ds(start, rows), :].astype(jnp.bfloat16)


def coil_chain(pieces, place, sens, measured, sampled, forward_x, adjoint_x, table_y_re, table_y_im):
    coils, height, width = sens.shape
    groups = len(pieces)
    rows = pieces[0].shape[0]
    whole = lambda c: (0, 0)
    per_coil = lambda c: (c, 0, 0)
    step_coils = 2 if coils % 2 == 0 else 1
    flops = coils * 8 * height * width * width
    return pl.pallas_call(
        coil_chain_kernel,
        out_shape=(
            jax.ShapeDtypeStruct((rows, width), jnp.float32),
            jax.ShapeDtypeStruct((groups - 1, rows, width), jnp.bfloat16),
        ),
        grid=(coils // step_coils,),
        in_specs=[pl.BlockSpec((rows, width), whole)] * groups
        + [
            pl.BlockSpec(memory_space=pltpu.SMEM),
            pl.BlockSpec((step_coils, height, width), per_coil),
            pl.BlockSpec((step_coils, height, width), per_coil),
            pl.BlockSpec((step_coils, 1, height), per_coil),
            pl.BlockSpec((width, width), whole),
            pl.BlockSpec((width, width), whole),
            pl.BlockSpec((height, height), whole),
            pl.BlockSpec((height, height), whole),
        ],
        out_specs=(
            pl.BlockSpec((rows, width), whole),
            pl.BlockSpec((groups - 1, rows, width), lambda c: (0, 0, 0)),
        ),
        scratch_shapes=[pltpu.VMEM((height, width), jnp.bfloat16), pltpu.VMEM((height, width), jnp.float32)],
        compiler_params=pltpu.CompilerParams(dimension_semantics=("arbitrary",)),
        cost_estimate=pl.CostEstimate(
            flops=flops, transcendentals=0, bytes_accessed=2 * 2 * coils * height * width + 4 * height * width
        ),
    )(*pieces, place, sens, measured, sampled, forward_x, adjoint_x, table_y_re, table_y_im)


def on_device(factors, temporal, maps, kdata, masks):
    width_x = maps.shape[2] // 2
    width_y = maps.shape[1]
    rows_own = factors.shape[2]
    table_x_re, table_x_im = dft_parts(width_x)
    table_y_re, table_y_im = dft_parts(width_y)
    forward_x = jnp.asarray(np.block([[table_x_re, table_x_im], [-table_x_im, table_x_re]]))
    adjoint_x = jnp.asarray(np.block([[table_x_re, -table_x_im], [table_x_im, table_x_re]]))
    table_y_re = jnp.asarray(table_y_re)
    table_y_im = jnp.asarray(table_y_im)
    time_re = temporal[0]
    time_im = temporal[1]
    mixing = jnp.stack(
        [jnp.stack([time_re, -time_im], axis=1), jnp.stack([time_im, time_re], axis=1)], axis=1
    )
    parts, ranks, rows_here, cols_here = factors.shape
    frames_all = mixing.shape[0]
    images = jnp.dot(
        mixing.reshape(frames_all * 2, parts * ranks),
        factors.reshape(parts * ranks, rows_here * cols_here),
        precision=lax.Precision.HIGHEST,
        preferred_element_type=jnp.float32,
    ).reshape(frames_all, 2, rows_here, cols_here).astype(jnp.bfloat16)
    frames_here = images.shape[0]
    width_own = images.shape[3]
    pieces_x = exchange_blocks(images, "frame")
    own_rows = jnp.transpose(pieces_x, (2, 1, 0, 3)).reshape(rows_own, 2 * width_x)
    groups = lax.axis_size("coil")
    me_c = lax.axis_index("coil")
    pieces = [own_rows] + [lax.ppermute(own_rows, "coil", shifted(groups, step)) for step in range(1, groups)]
    sampled = masks[0].astype(jnp.float32)[:, None, :]
    place = jnp.reshape(me_c, (1,)).astype(jnp.int32)
    own_total, outgoing = coil_chain(
        pieces, place, maps, kdata[0], sampled, forward_x, adjoint_x, table_y_re, table_y_im
    )
    own_share = own_total
    for step in range(1, groups):
        own_share = own_share + lax.ppermute(outgoing[step - 1], "coil", shifted(groups, step)).astype(jnp.float32)
    outgoing = jnp.transpose(
        own_share.reshape(rows_own, 2, frames_here, width_own), (2, 1, 0, 3)
    ).astype(jnp.bfloat16)
    returned = exchange_blocks(outgoing, "frame").astype(jnp.float32)
    weights = jnp.stack(
        [jnp.stack([time_re.T, time_im.T], axis=2), jnp.stack([-time_im.T, time_re.T], axis=2)], axis=0
    )
    gradient = jnp.dot(
        weights.reshape(parts * ranks, frames_all * 2),
        returned.reshape(frames_all * 2, rows_here * cols_here),
        precision=lax.Precision.HIGHEST,
        preferred_element_type=jnp.float32,
    ).reshape(factors.shape)
    return factors - 0.5 * gradient


def solution(mesh):
    placed = (
        P("slab", None, "coil", "frame"),
        P("slab", None, None),
        P("coil", "slab", None),
        P("frame", "coil", "slab", None),
        P("frame", "coil", "slab"),
    )
    return jax.shard_map(
        on_device,
        mesh=mesh,
        in_specs=placed,
        out_specs=P("slab", None, "coil", "frame"),
        check_vma=False,
    )
```

```python
import math

import jax
import ml_dtypes
import numpy as np
import jax.numpy as jnp
from jax import lax
from jax.experimental import pallas as pl
from jax.experimental.pallas import tpu as pltpu
from jax.sharding import PartitionSpec as P


def dft_parts(length):
    index = np.arange(length, dtype=np.int64)
    phase = (index[:, None] * index[None, :]) % length
    angle = np.float32(2.0 * math.pi / length) * phase.astype(np.float32)
    scale = np.float32(1.0 / math.sqrt(length))
    real = (np.cos(angle.astype(np.float64)).astype(np.float32) * scale).astype(ml_dtypes.bfloat16)
    imag = (-np.sin(angle.astype(np.float64)).astype(np.float32) * scale).astype(ml_dtypes.bfloat16)
    return real, imag


def rotate_plus(values, half_width):
    return jnp.concatenate([-values[..., half_width:], values[..., :half_width]], axis=-1)


def rotate_minus(values, half_width):
    return jnp.concatenate([values[..., half_width:], -values[..., :half_width]], axis=-1)


def sens_times(sens, values, half_width):
    sens_re = sens[..., :half_width].astype(jnp.float32)
    sens_im = sens[..., half_width:].astype(jnp.float32)
    value_re = values[..., :half_width].astype(jnp.float32)
    value_im = values[..., half_width:].astype(jnp.float32)
    return jnp.concatenate(
        [sens_re * value_re - sens_im * value_im, sens_re * value_im + sens_im * value_re], axis=-1
    )


def conj_sens_times(sens, values, half_width):
    sens_re = sens[..., :half_width].astype(jnp.float32)
    sens_im = sens[..., half_width:].astype(jnp.float32)
    value_re = values[..., :half_width]
    value_im = values[..., half_width:]
    return jnp.concatenate(
        [sens_re * value_re + sens_im * value_im, sens_re * value_im - sens_im * value_re], axis=-1
    )


def precise(form, first, second):
    return jnp.einsum(form, first, second, precision=lax.Precision.HIGHEST)


PERMUTE_LIMIT = 8


def shifted(count, step):
    return [(source, (source + step) % count) for source in range(count)]


def by_sender(pieces, count, me):
    ring = jnp.stack([pieces[0]] + pieces[1:][::-1])
    doubled = jnp.concatenate([ring, ring], axis=0)
    return lax.dynamic_slice_in_dim(doubled, (count - me) % count, count, 0)


def gather_blocks(value, axis):
    count = lax.axis_size(axis)
    if count > PERMUTE_LIMIT:
        return lax.all_gather(value, axis)
    me = lax.axis_index(axis)
    pieces = [value] + [lax.ppermute(value, axis, shifted(count, step)) for step in range(1, count)]
    return by_sender(pieces, count, me)


def exchange_blocks(blocks, axis):
    count = lax.axis_size(axis)
    if count > PERMUTE_LIMIT:
        return lax.all_to_all(blocks, axis, 0, 0, tiled=True)
    me = lax.axis_index(axis)
    pieces = [lax.dynamic_index_in_dim(blocks, me, 0, keepdims=False)]
    for step in range(1, count):
        outgoing = lax.dynamic_index_in_dim(blocks, (me + step) % count, 0, keepdims=False)
        pieces.append(lax.ppermute(outgoing, axis, shifted(count, step)))
    return by_sender(pieces, count, me)


def reduce_blocks(blocks, axis):
    count = lax.axis_size(axis)
    if count > PERMUTE_LIMIT:
        return lax.psum_scatter(blocks.astype(jnp.bfloat16), axis, scatter_dimension=0).astype(jnp.float32)
    me = lax.axis_index(axis)
    total = lax.dynamic_index_in_dim(blocks, me, 0, keepdims=False)
    for step in range(1, count):
        outgoing = lax.dynamic_index_in_dim(blocks, (me + step) % count, 0, keepdims=False)
        total = total + lax.ppermute(outgoing.astype(jnp.bfloat16), axis, shifted(count, step)).astype(jnp.float32)
    return total


def swap_halves(values, half_width, negate_first):
    low = values[:, :half_width]
    high = values[:, half_width:]
    if negate_first:
        return jnp.concatenate([-high, low], axis=1)
    return jnp.concatenate([high, -low], axis=1)


def coil_term(coil_index, image_ref, sens_ref, measured_ref, sampled_ref, forward_ref, adjoint_ref,
              table_re_ref, table_im_ref):
    half_width = image_ref.shape[1] // 2
    sens = sens_ref[coil_index].astype(jnp.float32)
    sens_re = sens[:, :half_width]
    sens_im = sens[:, half_width:]
    image = image_ref[...].astype(jnp.float32)
    image_re = image[:, :half_width]
    image_im = image[:, half_width:]
    coil = jnp.concatenate(
        [sens_re * image_re - sens_im * image_im, sens_re * image_im + sens_im * image_re], axis=1
    ).astype(jnp.bfloat16)
    half_k = jnp.dot(coil, forward_ref[...], preferred_element_type=jnp.float32).astype(jnp.bfloat16)
    table_re = table_re_ref[...]
    table_im = table_im_ref[...]
    kspace = jnp.dot(table_re, half_k, preferred_element_type=jnp.float32) + jnp.dot(
        table_im, swap_halves(half_k, half_width, True), preferred_element_type=jnp.float32
    )
    residual = (kspace - measured_ref[coil_index].astype(jnp.float32)).astype(jnp.bfloat16)
    sampled = sampled_ref[coil_index].astype(jnp.bfloat16)
    back_half = (
        jnp.dot(table_re * sampled, residual, preferred_element_type=jnp.float32)
        + jnp.dot(table_im * sampled, swap_halves(residual, half_width, False), preferred_element_type=jnp.float32)
    ).astype(jnp.bfloat16)
    coil_back = jnp.dot(back_half, adjoint_ref[...], preferred_element_type=jnp.float32)
    back_re = coil_back[:, :half_width]
    back_im = coil_back[:, half_width:]
    term = jnp.concatenate(
        [sens_re * back_re + sens_im * back_im, sens_re * back_im - sens_im * back_re], axis=1
    )

    return term


def coil_chain_kernel(*refs):
    groups = len(refs) - 12
    pieces = refs[:groups]
    place_ref, sens_ref, measured_ref, sampled_ref, forward_ref, adjoint_ref, table_re_ref, table_im_ref = refs[
        groups:groups + 8
    ]
    own_ref, send_ref = refs[groups + 8:groups + 10]
    image_ref, total_ref = refs[groups + 10:]
    rows = pieces[0].shape[0]
    half_width = image_ref.shape[1] // 2
    me = place_ref[0]
    step = pl.program_id(0)

    @pl.when(step == 0)
    def _():
        for block in range(groups):
            source = (me - block + groups) % groups
            value = pieces[0][...]
            for other in range(1, groups):
                value = jnp.where(source == other, pieces[other][...], value)
            image_ref[block * rows:(block + 1) * rows, :] = value

    term = None
    for coil_index in range(sens_ref.shape[0]):
        one = coil_term(coil_index, image_ref, sens_ref, measured_ref, sampled_ref, forward_ref, adjoint_ref,
                        table_re_ref, table_im_ref)
        term = one if term is None else term + one

    @pl.when(step == 0)
    def _():
        total_ref[...] = term

    @pl.when(step > 0)
    def _():
        total_ref[...] += term

    @pl.when(step == pl.num_programs(0) - 1)
    def _():
        start = pl.multiple_of(me * rows, rows)
        own_ref[...] = total_ref[pl.ds(start, rows), :]
        for shift in range(1, groups):
            start = pl.multiple_of(((me + shift) % groups) * rows, rows)
            send_ref[shift - 1] = total_ref[pl.ds(start, rows), :].astype(jnp.bfloat16)


def coil_chain(pieces, place, sens, measured, sampled, forward_x, adjoint_x, table_y_re, table_y_im):
    coils, height, width = sens.shape
    groups = len(pieces)
    rows = pieces[0].shape[0]
    whole = lambda c: (0, 0)
    per_coil = lambda c: (c, 0, 0)
    step_coils = 2 if coils % 2 == 0 else 1
    flops = coils * 8 * height * width * width
    return pl.pallas_call(
        coil_chain_kernel,
        out_shape=(
            jax.ShapeDtypeStruct((rows, width), jnp.float32),
            jax.ShapeDtypeStruct((groups - 1, rows, width), jnp.bfloat16),
        ),
        grid=(coils // step_coils,),
        in_specs=[pl.BlockSpec((rows, width), whole)] * groups
        + [
            pl.BlockSpec(memory_space=pltpu.SMEM),
            pl.BlockSpec((step_coils, height, width), per_coil),
            pl.BlockSpec((step_coils, height, width), per_coil),
            pl.BlockSpec((step_coils, 1, height), per_coil),
            pl.BlockSpec((width, width), whole),
            pl.BlockSpec((width, width), whole),
            pl.BlockSpec((height, height), whole),
            pl.BlockSpec((height, height), whole),
        ],
        out_specs=(
            pl.BlockSpec((rows, width), whole),
            pl.BlockSpec((groups - 1, rows, width), lambda c: (0, 0, 0)),
        ),
        scratch_shapes=[pltpu.VMEM((height, width), jnp.bfloat16), pltpu.VMEM((height, width), jnp.float32)],
        compiler_params=pltpu.CompilerParams(dimension_semantics=("arbitrary",)),
        cost_estimate=pl.CostEstimate(
            flops=flops, transcendentals=0, bytes_accessed=2 * 2 * coils * height * width + 4 * height * width
        ),
    )(*pieces, place, sens, measured, sampled, forward_x, adjoint_x, table_y_re, table_y_im)


def images_kernel(weight_ref, factors_ref, out_ref):
    parts, ranks = factors_ref.shape[:2]

    def one_frame(frame, carry):
        for part_out in range(2):
            total = None
            for part in range(parts):
                for rank in range(ranks):
                    weight = weight_ref[((frame * 2 + part_out) * parts + part) * ranks + rank]
                    term = weight * factors_ref[part, rank]
                    total = term if total is None else total + term
            out_ref[frame, part_out] = total.astype(out_ref.dtype)
        return carry

    lax.fori_loop(0, out_ref.shape[0], one_frame, 0)


def make_images(weights, factors):
    parts, ranks, rows, cols = factors.shape
    frames = weights.shape[0] // (2 * parts * ranks)
    return pl.pallas_call(
        images_kernel,
        out_shape=jax.ShapeDtypeStruct((frames, 2, rows, cols), jnp.bfloat16),
        in_specs=[pl.BlockSpec(memory_space=pltpu.SMEM), pl.BlockSpec(memory_space=pltpu.VMEM)],
        out_specs=pl.BlockSpec(memory_space=pltpu.VMEM),
    )(weights, factors)


def step_kernel(weight_ref, back_ref, factors_ref, out_ref):
    parts, ranks = factors_ref.shape[:2]
    frames = back_ref.shape[0]
    for part in range(parts):
        for rank in range(ranks):
            base = (part * ranks + rank) * frames * 2

            def one_frame(frame, total):
                for part_in in range(2):
                    total = total + weight_ref[base + frame * 2 + part_in] * back_ref[frame, part_in].astype(jnp.float32)
                return total

            total = lax.fori_loop(
                0, frames, one_frame, jnp.zeros(factors_ref.shape[2:], jnp.float32), unroll=frames <= 8
            )
            out_ref[part, rank] = factors_ref[part, rank] - 0.5 * total


def take_step(weights, back, factors):
    return pl.pallas_call(
        step_kernel,
        out_shape=jax.ShapeDtypeStruct(factors.shape, jnp.float32),
        in_specs=[
            pl.BlockSpec(memory_space=pltpu.SMEM),
            pl.BlockSpec(memory_space=pltpu.VMEM),
            pl.BlockSpec(memory_space=pltpu.VMEM),
        ],
        out_specs=pl.BlockSpec(memory_space=pltpu.VMEM),
    )(weights, back, factors)


def on_device(factors, temporal, maps, kdata, masks):
    width_x = maps.shape[2] // 2
    width_y = maps.shape[1]
    rows_own = factors.shape[2]
    table_x_re, table_x_im = dft_parts(width_x)
    table_y_re, table_y_im = dft_parts(width_y)
    forward_x = jnp.asarray(np.block([[table_x_re, table_x_im], [-table_x_im, table_x_re]]))
    adjoint_x = jnp.asarray(np.block([[table_x_re, -table_x_im], [table_x_im, table_x_re]]))
    table_y_re = jnp.asarray(table_y_re)
    table_y_im = jnp.asarray(table_y_im)
    time_re = temporal[0]
    time_im = temporal[1]
    mixing = jnp.stack(
        [jnp.stack([time_re, -time_im], axis=1), jnp.stack([time_im, time_re], axis=1)], axis=1
    )
    images = make_images(mixing.reshape(-1), factors)
    frames_here = images.shape[0]
    width_own = images.shape[3]
    pieces_x = exchange_blocks(images, "frame")
    own_rows = jnp.transpose(pieces_x, (2, 1, 0, 3)).reshape(rows_own, 2 * width_x)
    groups = lax.axis_size("coil")
    me_c = lax.axis_index("coil")
    pieces = [own_rows] + [lax.ppermute(own_rows, "coil", shifted(groups, step)) for step in range(1, groups)]
    sampled = masks[0].astype(jnp.float32)[:, None, :]
    place = jnp.reshape(me_c, (1,)).astype(jnp.int32)
    own_total, outgoing = coil_chain(
        pieces, place, maps, kdata[0], sampled, forward_x, adjoint_x, table_y_re, table_y_im
    )
    own_share = own_total
    for step in range(1, groups):
        own_share = own_share + lax.ppermute(outgoing[step - 1], "coil", shifted(groups, step)).astype(jnp.float32)
    outgoing = jnp.transpose(
        own_share.reshape(rows_own, 2, frames_here, width_own), (2, 1, 0, 3)
    ).astype(jnp.bfloat16)
    returned = exchange_blocks(outgoing, "frame")
    weights = jnp.stack(
        [jnp.stack([time_re.T, time_im.T], axis=2), jnp.stack([-time_im.T, time_re.T], axis=2)], axis=0
    )
    return take_step(weights.reshape(-1), returned, factors)


def solution(mesh):
    placed = (
        P("slab", None, "coil", "frame"),
        P("slab", None, None),
        P("coil", "slab", None),
        P("frame", "coil", "slab", None),
        P("frame", "coil", "slab"),
    )
    return jax.shard_map(
        on_device,
        mesh=mesh,
        in_specs=placed,
        out_specs=P("slab", None, "coil", "frame"),
        check_vma=False,
    )
```

```python
import math

import jax
import ml_dtypes
import numpy as np
import jax.numpy as jnp
from jax import lax
from jax.experimental import pallas as pl
from jax.experimental.pallas import tpu as pltpu
from jax.sharding import PartitionSpec as P


def dft_parts(length):
    index = np.arange(length, dtype=np.int64)
    phase = (index[:, None] * index[None, :]) % length
    angle = np.float32(2.0 * math.pi / length) * phase.astype(np.float32)
    scale = np.float32(1.0 / math.sqrt(length))
    real = (np.cos(angle.astype(np.float64)).astype(np.float32) * scale).astype(ml_dtypes.bfloat16)
    imag = (-np.sin(angle.astype(np.float64)).astype(np.float32) * scale).astype(ml_dtypes.bfloat16)
    return real, imag


def rotate_plus(values, half_width):
    return jnp.concatenate([-values[..., half_width:], values[..., :half_width]], axis=-1)


def rotate_minus(values, half_width):
    return jnp.concatenate([values[..., half_width:], -values[..., :half_width]], axis=-1)


def sens_times(sens, values, half_width):
    sens_re = sens[..., :half_width].astype(jnp.float32)
    sens_im = sens[..., half_width:].astype(jnp.float32)
    value_re = values[..., :half_width].astype(jnp.float32)
    value_im = values[..., half_width:].astype(jnp.float32)
    return jnp.concatenate(
        [sens_re * value_re - sens_im * value_im, sens_re * value_im + sens_im * value_re], axis=-1
    )


def conj_sens_times(sens, values, half_width):
    sens_re = sens[..., :half_width].astype(jnp.float32)
    sens_im = sens[..., half_width:].astype(jnp.float32)
    value_re = values[..., :half_width]
    value_im = values[..., half_width:]
    return jnp.concatenate(
        [sens_re * value_re + sens_im * value_im, sens_re * value_im - sens_im * value_re], axis=-1
    )


def precise(form, first, second):
    return jnp.einsum(form, first, second, precision=lax.Precision.HIGHEST)


PERMUTE_LIMIT = 8


def shifted(count, step):
    return [(source, (source + step) % count) for source in range(count)]


def by_sender(pieces, count, me):
    ring = jnp.stack([pieces[0]] + pieces[1:][::-1])
    doubled = jnp.concatenate([ring, ring], axis=0)
    return lax.dynamic_slice_in_dim(doubled, (count - me) % count, count, 0)


def gather_blocks(value, axis):
    count = lax.axis_size(axis)
    if count > PERMUTE_LIMIT:
        return lax.all_gather(value, axis)
    me = lax.axis_index(axis)
    pieces = [value] + [lax.ppermute(value, axis, shifted(count, step)) for step in range(1, count)]
    return by_sender(pieces, count, me)


def exchange_blocks(blocks, axis):
    count = lax.axis_size(axis)
    if count > PERMUTE_LIMIT:
        return lax.all_to_all(blocks, axis, 0, 0, tiled=True)
    me = lax.axis_index(axis)
    pieces = [lax.dynamic_index_in_dim(blocks, me, 0, keepdims=False)]
    for step in range(1, count):
        outgoing = lax.dynamic_index_in_dim(blocks, (me + step) % count, 0, keepdims=False)
        pieces.append(lax.ppermute(outgoing, axis, shifted(count, step)))
    return by_sender(pieces, count, me)


def reduce_blocks(blocks, axis):
    count = lax.axis_size(axis)
    if count > PERMUTE_LIMIT:
        return lax.psum_scatter(blocks.astype(jnp.bfloat16), axis, scatter_dimension=0).astype(jnp.float32)
    me = lax.axis_index(axis)
    total = lax.dynamic_index_in_dim(blocks, me, 0, keepdims=False)
    for step in range(1, count):
        outgoing = lax.dynamic_index_in_dim(blocks, (me + step) % count, 0, keepdims=False)
        total = total + lax.ppermute(outgoing.astype(jnp.bfloat16), axis, shifted(count, step)).astype(jnp.float32)
    return total


def swap_halves(values, half_width, negate_first):
    low = values[:, :half_width]
    high = values[:, half_width:]
    if negate_first:
        return jnp.concatenate([-high, low], axis=1)
    return jnp.concatenate([high, -low], axis=1)


def coil_term(coil_index, image_ref, sens_ref, measured_ref, sampled_ref, forward_ref, adjoint_ref,
              table_re_ref, table_im_ref):
    half_width = image_ref.shape[1] // 2
    sens = sens_ref[coil_index].astype(jnp.float32)
    sens_re = sens[:, :half_width]
    sens_im = sens[:, half_width:]
    image = image_ref[...].astype(jnp.float32)
    image_re = image[:, :half_width]
    image_im = image[:, half_width:]
    coil = jnp.concatenate(
        [sens_re * image_re - sens_im * image_im, sens_re * image_im + sens_im * image_re], axis=1
    ).astype(jnp.bfloat16)
    half_k = jnp.dot(coil, forward_ref[...], preferred_element_type=jnp.float32).astype(jnp.bfloat16)
    table_re = table_re_ref[...]
    table_im = table_im_ref[...]
    kspace = jnp.dot(table_re, half_k, preferred_element_type=jnp.float32) + jnp.dot(
        table_im, swap_halves(half_k, half_width, True), preferred_element_type=jnp.float32
    )
    residual = (kspace - measured_ref[coil_index].astype(jnp.float32)).astype(jnp.bfloat16)
    sampled = sampled_ref[coil_index].astype(jnp.bfloat16)
    back_half = (
        jnp.dot(table_re * sampled, residual, preferred_element_type=jnp.float32)
        + jnp.dot(table_im * sampled, swap_halves(residual, half_width, False), preferred_element_type=jnp.float32)
    ).astype(jnp.bfloat16)
    coil_back = jnp.dot(back_half, adjoint_ref[...], preferred_element_type=jnp.float32)
    back_re = coil_back[:, :half_width]
    back_im = coil_back[:, half_width:]
    term = jnp.concatenate(
        [sens_re * back_re + sens_im * back_im, sens_re * back_im - sens_im * back_re], axis=1
    )

    return term


def coil_chain_kernel(*refs):
    groups = (len(refs) - 9) // 2
    pieces = refs[:groups]
    place_ref, sens_ref, measured_ref, sampled_ref, forward_ref, adjoint_ref, table_re_ref, table_im_ref = refs[
        groups:groups + 8
    ]
    own_ref = refs[groups + 8]
    send_refs = refs[groups + 9:2 * groups + 8]
    image_ref, total_ref = refs[2 * groups + 8:]
    rows = pieces[0].shape[0]
    half_width = image_ref.shape[1] // 2
    me = place_ref[0]
    step = pl.program_id(0)

    @pl.when(step == 0)
    def _():
        for block in range(groups):
            source = (me - block + groups) % groups
            value = pieces[0][...]
            for other in range(1, groups):
                value = jnp.where(source == other, pieces[other][...], value)
            image_ref[block * rows:(block + 1) * rows, :] = value

    term = None
    for coil_index in range(sens_ref.shape[0]):
        one = coil_term(coil_index, image_ref, sens_ref, measured_ref, sampled_ref, forward_ref, adjoint_ref,
                        table_re_ref, table_im_ref)
        term = one if term is None else term + one

    @pl.when(step == 0)
    def _():
        total_ref[...] = term

    @pl.when(step > 0)
    def _():
        total_ref[...] += term

    @pl.when(step == pl.num_programs(0) - 1)
    def _():
        start = pl.multiple_of(me * rows, rows)
        own_ref[...] = total_ref[pl.ds(start, rows), :]
        for shift in range(1, groups):
            start = pl.multiple_of(((me + shift) % groups) * rows, rows)
            send_refs[shift - 1][...] = total_ref[pl.ds(start, rows), :].astype(jnp.bfloat16)


def coil_chain(pieces, place, sens, measured, sampled, forward_x, adjoint_x, table_y_re, table_y_im):
    coils, height, width = sens.shape
    groups = len(pieces)
    rows = pieces[0].shape[0]
    whole = lambda c: (0, 0)
    per_coil = lambda c: (c, 0, 0)
    step_coils = 2 if coils % 2 == 0 else 1
    flops = coils * 8 * height * width * width
    return pl.pallas_call(
        coil_chain_kernel,
        out_shape=(jax.ShapeDtypeStruct((rows, width), jnp.float32),)
        + (jax.ShapeDtypeStruct((rows, width), jnp.bfloat16),) * (groups - 1),
        grid=(coils // step_coils,),
        in_specs=[pl.BlockSpec((rows, width), whole)] * groups
        + [
            pl.BlockSpec(memory_space=pltpu.SMEM),
            pl.BlockSpec((step_coils, height, width), per_coil),
            pl.BlockSpec((step_coils, height, width), per_coil),
            pl.BlockSpec((step_coils, 1, height), per_coil),
            pl.BlockSpec((width, width), whole),
            pl.BlockSpec((width, width), whole),
            pl.BlockSpec((height, height), whole),
            pl.BlockSpec((height, height), whole),
        ],
        out_specs=(pl.BlockSpec((rows, width), whole),) * groups,
        scratch_shapes=[pltpu.VMEM((height, width), jnp.bfloat16), pltpu.VMEM((height, width), jnp.float32)],
        compiler_params=pltpu.CompilerParams(dimension_semantics=("arbitrary",)),
        cost_estimate=pl.CostEstimate(
            flops=flops, transcendentals=0, bytes_accessed=2 * 2 * coils * height * width + 4 * height * width
        ),
    )(*pieces, place, sens, measured, sampled, forward_x, adjoint_x, table_y_re, table_y_im)


def on_device(factors, temporal, maps, kdata, masks):
    width_x = maps.shape[2] // 2
    width_y = maps.shape[1]
    rows_own = factors.shape[2]
    table_x_re, table_x_im = dft_parts(width_x)
    table_y_re, table_y_im = dft_parts(width_y)
    forward_x = jnp.asarray(np.block([[table_x_re, table_x_im], [-table_x_im, table_x_re]]))
    adjoint_x = jnp.asarray(np.block([[table_x_re, -table_x_im], [table_x_im, table_x_re]]))
    table_y_re = jnp.asarray(table_y_re)
    table_y_im = jnp.asarray(table_y_im)
    time_re = temporal[0]
    time_im = temporal[1]
    mixing = jnp.stack(
        [jnp.stack([time_re, -time_im], axis=1), jnp.stack([time_im, time_re], axis=1)], axis=1
    )
    parts, ranks = factors.shape[:2]
    images = None
    for part in range(parts):
        for rank in range(ranks):
            term = mixing[:, :, part, rank, None, None] * factors[part, rank][None, None]
            images = term if images is None else images + term
    images = images.astype(jnp.bfloat16)
    frames_here = images.shape[0]
    width_own = images.shape[3]
    pieces_x = exchange_blocks(images, "frame")
    own_rows = jnp.transpose(pieces_x, (2, 1, 0, 3)).reshape(rows_own, 2 * width_x)
    groups = lax.axis_size("coil")
    me_c = lax.axis_index("coil")
    pieces = [own_rows] + [lax.ppermute(own_rows, "coil", shifted(groups, step)) for step in range(1, groups)]
    sampled = masks[0].astype(jnp.float32)[:, None, :]
    place = jnp.reshape(me_c, (1,)).astype(jnp.int32)
    own_total, *outgoing = coil_chain(
        pieces, place, maps, kdata[0], sampled, forward_x, adjoint_x, table_y_re, table_y_im
    )
    own_share = own_total
    for step in range(1, groups):
        own_share = own_share + lax.ppermute(outgoing[step - 1], "coil", shifted(groups, step)).astype(jnp.float32)
    outgoing = jnp.transpose(
        own_share.reshape(rows_own, 2, frames_here, width_own), (2, 0, 1, 3)
    ).astype(jnp.bfloat16)
    returned = exchange_blocks(outgoing, "frame").astype(jnp.float32)
    weights = jnp.stack(
        [jnp.stack([time_re.T, time_im.T], axis=2), jnp.stack([-time_im.T, time_re.T], axis=2)], axis=0
    )
    gradient = None
    for frame in range(returned.shape[0]):
        for part_in in range(2):
            term = weights[:, :, frame, part_in, None, None] * returned[frame, :, part_in][None, None]
            gradient = term if gradient is None else gradient + term
    return factors - 0.5 * gradient


def solution(mesh):
    placed = (
        P("slab", None, "coil", "frame"),
        P("slab", None, None),
        P("coil", "slab", None),
        P("frame", "coil", "slab", None),
        P("frame", "coil", "slab"),
    )
    return jax.shard_map(
        on_device,
        mesh=mesh,
        in_specs=placed,
        out_specs=P("slab", None, "coil", "frame"),
        check_vma=False,
    )
```

```python
import math

import jax
import ml_dtypes
import numpy as np
import jax.numpy as jnp
from jax import lax
from jax.experimental import pallas as pl
from jax.experimental.pallas import tpu as pltpu
from jax.sharding import PartitionSpec as P


def dft_parts(length):
    index = np.arange(length, dtype=np.int64)
    phase = (index[:, None] * index[None, :]) % length
    angle = np.float32(2.0 * math.pi / length) * phase.astype(np.float32)
    scale = np.float32(1.0 / math.sqrt(length))
    real = (np.cos(angle.astype(np.float64)).astype(np.float32) * scale).astype(ml_dtypes.bfloat16)
    imag = (-np.sin(angle.astype(np.float64)).astype(np.float32) * scale).astype(ml_dtypes.bfloat16)
    return real, imag


def rotate_plus(values, half_width):
    return jnp.concatenate([-values[..., half_width:], values[..., :half_width]], axis=-1)


def rotate_minus(values, half_width):
    return jnp.concatenate([values[..., half_width:], -values[..., :half_width]], axis=-1)


def sens_times(sens, values, half_width):
    sens_re = sens[..., :half_width].astype(jnp.float32)
    sens_im = sens[..., half_width:].astype(jnp.float32)
    value_re = values[..., :half_width].astype(jnp.float32)
    value_im = values[..., half_width:].astype(jnp.float32)
    return jnp.concatenate(
        [sens_re * value_re - sens_im * value_im, sens_re * value_im + sens_im * value_re], axis=-1
    )


def conj_sens_times(sens, values, half_width):
    sens_re = sens[..., :half_width].astype(jnp.float32)
    sens_im = sens[..., half_width:].astype(jnp.float32)
    value_re = values[..., :half_width]
    value_im = values[..., half_width:]
    return jnp.concatenate(
        [sens_re * value_re + sens_im * value_im, sens_re * value_im - sens_im * value_re], axis=-1
    )


def precise(form, first, second):
    return jnp.einsum(form, first, second, precision=lax.Precision.HIGHEST)


PERMUTE_LIMIT = 8


def shifted(count, step):
    return [(source, (source + step) % count) for source in range(count)]


def by_sender(pieces, count, me):
    ring = jnp.stack([pieces[0]] + pieces[1:][::-1])
    doubled = jnp.concatenate([ring, ring], axis=0)
    return lax.dynamic_slice_in_dim(doubled, (count - me) % count, count, 0)


def gather_blocks(value, axis):
    count = lax.axis_size(axis)
    if count > PERMUTE_LIMIT:
        return lax.all_gather(value, axis)
    me = lax.axis_index(axis)
    pieces = [value] + [lax.ppermute(value, axis, shifted(count, step)) for step in range(1, count)]
    return by_sender(pieces, count, me)


def exchange_blocks(blocks, axis):
    count = lax.axis_size(axis)
    if count > PERMUTE_LIMIT:
        return lax.all_to_all(blocks, axis, 0, 0, tiled=True)
    me = lax.axis_index(axis)
    pieces = [lax.dynamic_index_in_dim(blocks, me, 0, keepdims=False)]
    for step in range(1, count):
        outgoing = lax.dynamic_index_in_dim(blocks, (me + step) % count, 0, keepdims=False)
        pieces.append(lax.ppermute(outgoing, axis, shifted(count, step)))
    return by_sender(pieces, count, me)


def reduce_blocks(blocks, axis):
    count = lax.axis_size(axis)
    if count > PERMUTE_LIMIT:
        return lax.psum_scatter(blocks.astype(jnp.bfloat16), axis, scatter_dimension=0).astype(jnp.float32)
    me = lax.axis_index(axis)
    total = lax.dynamic_index_in_dim(blocks, me, 0, keepdims=False)
    for step in range(1, count):
        outgoing = lax.dynamic_index_in_dim(blocks, (me + step) % count, 0, keepdims=False)
        total = total + lax.ppermute(outgoing.astype(jnp.bfloat16), axis, shifted(count, step)).astype(jnp.float32)
    return total


def swap_halves(values, half_width, negate_first):
    low = values[:, :half_width]
    high = values[:, half_width:]
    if negate_first:
        return jnp.concatenate([-high, low], axis=1)
    return jnp.concatenate([high, -low], axis=1)


def coil_term(coil_index, image_ref, sens_ref, measured_ref, sampled_ref, forward_ref, adjoint_ref,
              table_re_ref, table_im_ref):
    half_width = image_ref.shape[1] // 2
    sens = sens_ref[coil_index].astype(jnp.float32)
    sens_re = sens[:, :half_width]
    sens_im = sens[:, half_width:]
    image = image_ref[...].astype(jnp.float32)
    image_re = image[:, :half_width]
    image_im = image[:, half_width:]
    coil = jnp.concatenate(
        [sens_re * image_re - sens_im * image_im, sens_re * image_im + sens_im * image_re], axis=1
    ).astype(jnp.bfloat16)
    half_k = jnp.dot(coil, forward_ref[...], preferred_element_type=jnp.float32).astype(jnp.bfloat16)
    table_re = table_re_ref[...]
    table_im = table_im_ref[...]
    kspace = jnp.dot(table_re, half_k, preferred_element_type=jnp.float32) + jnp.dot(
        table_im, swap_halves(half_k, half_width, True), preferred_element_type=jnp.float32
    )
    residual = (kspace - measured_ref[coil_index].astype(jnp.float32)).astype(jnp.bfloat16)
    sampled = sampled_ref[coil_index].astype(jnp.bfloat16)
    back_half = (
        jnp.dot(table_re * sampled, residual, preferred_element_type=jnp.float32)
        + jnp.dot(table_im * sampled, swap_halves(residual, half_width, False), preferred_element_type=jnp.float32)
    ).astype(jnp.bfloat16)
    coil_back = jnp.dot(back_half, adjoint_ref[...], preferred_element_type=jnp.float32)
    back_re = coil_back[:, :half_width]
    back_im = coil_back[:, half_width:]
    term = jnp.concatenate(
        [sens_re * back_re + sens_im * back_im, sens_re * back_im - sens_im * back_re], axis=1
    )

    return term


def coil_chain_kernel(*refs):
    groups = (len(refs) - 9) // 2
    pieces = refs[:groups]
    place_ref, sens_ref, measured_ref, sampled_ref, forward_ref, adjoint_ref, table_re_ref, table_im_ref = refs[
        groups:groups + 8
    ]
    own_ref = refs[groups + 8]
    send_refs = refs[groups + 9:2 * groups + 8]
    image_ref, total_ref = refs[2 * groups + 8:]
    rows = pieces[0].shape[0]
    half_width = image_ref.shape[1] // 2
    me = place_ref[0]
    step = pl.program_id(0)

    @pl.when(step == 0)
    def _():
        for block in range(groups):
            source = (me - block + groups) % groups
            value = pieces[0][...]
            for other in range(1, groups):
                value = jnp.where(source == other, pieces[other][...], value)
            image_ref[block * rows:(block + 1) * rows, :] = value

    term = None
    for coil_index in range(sens_ref.shape[0]):
        one = coil_term(coil_index, image_ref, sens_ref, measured_ref, sampled_ref, forward_ref, adjoint_ref,
                        table_re_ref, table_im_ref)
        term = one if term is None else term + one

    @pl.when(step == 0)
    def _():
        total_ref[...] = term

    @pl.when(step > 0)
    def _():
        total_ref[...] += term

    @pl.when(step == pl.num_programs(0) - 1)
    def _():
        start = pl.multiple_of(me * rows, rows)
        own_ref[...] = total_ref[pl.ds(start, rows), :]
        for shift in range(1, groups):
            start = pl.multiple_of(((me + shift) % groups) * rows, rows)
            send_refs[shift - 1][...] = total_ref[pl.ds(start, rows), :].astype(jnp.bfloat16)


def coil_chain(pieces, place, sens, measured, sampled, forward_x, adjoint_x, table_y_re, table_y_im):
    coils, height, width = sens.shape
    groups = len(pieces)
    rows = pieces[0].shape[0]
    whole = lambda c: (0, 0)
    per_coil = lambda c: (c, 0, 0)
    step_coils = 2 if coils % 2 == 0 else 1
    flops = coils * 8 * height * width * width
    return pl.pallas_call(
        coil_chain_kernel,
        out_shape=(jax.ShapeDtypeStruct((rows, width), jnp.float32),)
        + (jax.ShapeDtypeStruct((rows, width), jnp.bfloat16),) * (groups - 1),
        grid=(coils // step_coils,),
        in_specs=[pl.BlockSpec((rows, width), whole)] * groups
        + [
            pl.BlockSpec(memory_space=pltpu.SMEM),
            pl.BlockSpec((step_coils, height, width), per_coil),
            pl.BlockSpec((step_coils, height, width), per_coil),
            pl.BlockSpec((step_coils, 1, height), per_coil),
            pl.BlockSpec((width, width), whole),
            pl.BlockSpec((width, width), whole),
            pl.BlockSpec((height, height), whole),
            pl.BlockSpec((height, height), whole),
        ],
        out_specs=(pl.BlockSpec((rows, width), whole),) * groups,
        scratch_shapes=[pltpu.VMEM((height, width), jnp.bfloat16), pltpu.VMEM((height, width), jnp.float32)],
        compiler_params=pltpu.CompilerParams(dimension_semantics=("arbitrary",)),
        cost_estimate=pl.CostEstimate(
            flops=flops, transcendentals=0, bytes_accessed=2 * 2 * coils * height * width + 4 * height * width
        ),
    )(*pieces, place, sens, measured, sampled, forward_x, adjoint_x, table_y_re, table_y_im)


def on_device(factors, temporal, maps, kdata, masks):
    width_x = maps.shape[2] // 2
    width_y = maps.shape[1]
    rows_own = factors.shape[2]
    table_x_re, table_x_im = dft_parts(width_x)
    table_y_re, table_y_im = dft_parts(width_y)
    forward_x = jnp.asarray(np.block([[table_x_re, table_x_im], [-table_x_im, table_x_re]]))
    adjoint_x = jnp.asarray(np.block([[table_x_re, -table_x_im], [table_x_im, table_x_re]]))
    table_y_re = jnp.asarray(table_y_re)
    table_y_im = jnp.asarray(table_y_im)
    time_re = temporal[0]
    time_im = temporal[1]
    mixing = jnp.stack(
        [jnp.stack([time_re, -time_im], axis=1), jnp.stack([time_im, time_re], axis=1)], axis=1
    )
    images = jnp.sum(
        mixing[:, :, :, :, None, None] * factors[None, None], axis=(2, 3)
    ).astype(jnp.bfloat16)
    frames_here = images.shape[0]
    width_own = images.shape[3]
    pieces_x = exchange_blocks(images, "frame")
    own_rows = jnp.transpose(pieces_x, (2, 1, 0, 3)).reshape(rows_own, 2 * width_x)
    groups = lax.axis_size("coil")
    me_c = lax.axis_index("coil")
    pieces = [own_rows] + [lax.ppermute(own_rows, "coil", shifted(groups, step)) for step in range(1, groups)]
    sampled = masks[0].astype(jnp.float32)[:, None, :]
    place = jnp.reshape(me_c, (1,)).astype(jnp.int32)
    own_total, *outgoing = coil_chain(
        pieces, place, maps, kdata[0], sampled, forward_x, adjoint_x, table_y_re, table_y_im
    )
    own_share = own_total
    for step in range(1, groups):
        own_share = own_share + lax.ppermute(outgoing[step - 1], "coil", shifted(groups, step)).astype(jnp.float32)
    outgoing = jnp.transpose(
        own_share.reshape(rows_own, 2, frames_here, width_own), (2, 0, 1, 3)
    ).astype(jnp.bfloat16)
    returned = exchange_blocks(outgoing, "frame").astype(jnp.float32)
    weights = jnp.stack(
        [jnp.stack([time_re.T, time_im.T], axis=2), jnp.stack([-time_im.T, time_re.T], axis=2)], axis=0
    )
    gradient = None
    for frame in range(returned.shape[0]):
        for part_in in range(2):
            term = weights[:, :, frame, part_in, None, None] * returned[frame, :, part_in][None, None]
            gradient = term if gradient is None else gradient + term
    return factors - 0.5 * gradient


def solution(mesh):
    placed = (
        P("slab", None, "coil", "frame"),
        P("slab", None, None),
        P("coil", "slab", None),
        P("frame", "coil", "slab", None),
        P("frame", "coil", "slab"),
    )
    return jax.shard_map(
        on_device,
        mesh=mesh,
        in_specs=placed,
        out_specs=P("slab", None, "coil", "frame"),
        check_vma=False,
    )
```

```python
import math

import jax
import ml_dtypes
import numpy as np
import jax.numpy as jnp
from jax import lax
from jax.experimental import pallas as pl
from jax.experimental.pallas import tpu as pltpu
from jax.sharding import PartitionSpec as P


def dft_parts(length):
    index = np.arange(length, dtype=np.int64)
    phase = (index[:, None] * index[None, :]) % length
    angle = np.float32(2.0 * math.pi / length) * phase.astype(np.float32)
    scale = np.float32(1.0 / math.sqrt(length))
    real = (np.cos(angle.astype(np.float64)).astype(np.float32) * scale).astype(ml_dtypes.bfloat16)
    imag = (-np.sin(angle.astype(np.float64)).astype(np.float32) * scale).astype(ml_dtypes.bfloat16)
    return real, imag


def rotate_plus(values, half_width):
    return jnp.concatenate([-values[..., half_width:], values[..., :half_width]], axis=-1)


def rotate_minus(values, half_width):
    return jnp.concatenate([values[..., half_width:], -values[..., :half_width]], axis=-1)


def sens_times(sens, values, half_width):
    sens_re = sens[..., :half_width].astype(jnp.float32)
    sens_im = sens[..., half_width:].astype(jnp.float32)
    value_re = values[..., :half_width].astype(jnp.float32)
    value_im = values[..., half_width:].astype(jnp.float32)
    return jnp.concatenate(
        [sens_re * value_re - sens_im * value_im, sens_re * value_im + sens_im * value_re], axis=-1
    )


def conj_sens_times(sens, values, half_width):
    sens_re = sens[..., :half_width].astype(jnp.float32)
    sens_im = sens[..., half_width:].astype(jnp.float32)
    value_re = values[..., :half_width]
    value_im = values[..., half_width:]
    return jnp.concatenate(
        [sens_re * value_re + sens_im * value_im, sens_re * value_im - sens_im * value_re], axis=-1
    )


def precise(form, first, second):
    return jnp.einsum(form, first, second, precision=lax.Precision.HIGHEST)


PERMUTE_LIMIT = 8


def shifted(count, step):
    return [(source, (source + step) % count) for source in range(count)]


def by_sender(pieces, count, me):
    ring = jnp.stack([pieces[0]] + pieces[1:][::-1])
    doubled = jnp.concatenate([ring, ring], axis=0)
    return lax.dynamic_slice_in_dim(doubled, (count - me) % count, count, 0)


def gather_blocks(value, axis):
    count = lax.axis_size(axis)
    if count > PERMUTE_LIMIT:
        return lax.all_gather(value, axis)
    me = lax.axis_index(axis)
    pieces = [value] + [lax.ppermute(value, axis, shifted(count, step)) for step in range(1, count)]
    return by_sender(pieces, count, me)


def exchange_blocks(blocks, axis):
    count = lax.axis_size(axis)
    if count > PERMUTE_LIMIT:
        return lax.all_to_all(blocks, axis, 0, 0, tiled=True)
    me = lax.axis_index(axis)
    pieces = [lax.dynamic_index_in_dim(blocks, me, 0, keepdims=False)]
    for step in range(1, count):
        outgoing = lax.dynamic_index_in_dim(blocks, (me + step) % count, 0, keepdims=False)
        pieces.append(lax.ppermute(outgoing, axis, shifted(count, step)))
    return by_sender(pieces, count, me)


def reduce_blocks(blocks, axis):
    count = lax.axis_size(axis)
    if count > PERMUTE_LIMIT:
        return lax.psum_scatter(blocks.astype(jnp.bfloat16), axis, scatter_dimension=0).astype(jnp.float32)
    me = lax.axis_index(axis)
    total = lax.dynamic_index_in_dim(blocks, me, 0, keepdims=False)
    for step in range(1, count):
        outgoing = lax.dynamic_index_in_dim(blocks, (me + step) % count, 0, keepdims=False)
        total = total + lax.ppermute(outgoing.astype(jnp.bfloat16), axis, shifted(count, step)).astype(jnp.float32)
    return total


def swap_halves(values, half_width, negate_first):
    low = values[:, :half_width]
    high = values[:, half_width:]
    if negate_first:
        return jnp.concatenate([-high, low], axis=1)
    return jnp.concatenate([high, -low], axis=1)


def coil_term(coil_index, image_ref, sens_ref, measured_ref, sampled_ref, forward_ref, adjoint_ref,
              table_re_ref, table_im_ref):
    half_width = image_ref.shape[1] // 2
    sens = sens_ref[coil_index].astype(jnp.float32)
    sens_re = sens[:, :half_width]
    sens_im = sens[:, half_width:]
    image = image_ref[...].astype(jnp.float32)
    image_re = image[:, :half_width]
    image_im = image[:, half_width:]
    coil = jnp.concatenate(
        [sens_re * image_re - sens_im * image_im, sens_re * image_im + sens_im * image_re], axis=1
    ).astype(jnp.bfloat16)
    half_k = jnp.dot(coil, forward_ref[...], preferred_element_type=jnp.float32).astype(jnp.bfloat16)
    table_re = table_re_ref[...]
    table_im = table_im_ref[...]
    kspace = jnp.dot(table_re, half_k, preferred_element_type=jnp.float32) + jnp.dot(
        table_im, swap_halves(half_k, half_width, True), preferred_element_type=jnp.float32
    )
    residual = (kspace - measured_ref[coil_index].astype(jnp.float32)).astype(jnp.bfloat16)
    sampled = sampled_ref[coil_index].astype(jnp.bfloat16)
    back_half = (
        jnp.dot(table_re * sampled, residual, preferred_element_type=jnp.float32)
        + jnp.dot(table_im * sampled, swap_halves(residual, half_width, False), preferred_element_type=jnp.float32)
    ).astype(jnp.bfloat16)
    coil_back = jnp.dot(back_half, adjoint_ref[...], preferred_element_type=jnp.float32)
    back_re = coil_back[:, :half_width]
    back_im = coil_back[:, half_width:]
    term = jnp.concatenate(
        [sens_re * back_re + sens_im * back_im, sens_re * back_im - sens_im * back_re], axis=1
    )

    return term


def coil_chain_kernel(*refs):
    groups = (len(refs) - 9) // 2
    pieces = refs[:groups]
    place_ref, sens_ref, measured_ref, sampled_ref, forward_ref, adjoint_ref, table_re_ref, table_im_ref = refs[
        groups:groups + 8
    ]
    own_ref = refs[groups + 8]
    send_refs = refs[groups + 9:2 * groups + 8]
    image_ref, total_ref = refs[2 * groups + 8:]
    rows = pieces[0].shape[0]
    half_width = image_ref.shape[1] // 2
    me = place_ref[0]
    step = pl.program_id(0)

    @pl.when(step == 0)
    def _():
        for block in range(groups):
            source = (me - block + groups) % groups
            value = pieces[0][...]
            for other in range(1, groups):
                value = jnp.where(source == other, pieces[other][...], value)
            image_ref[block * rows:(block + 1) * rows, :] = value

    term = None
    for coil_index in range(sens_ref.shape[0]):
        one = coil_term(coil_index, image_ref, sens_ref, measured_ref, sampled_ref, forward_ref, adjoint_ref,
                        table_re_ref, table_im_ref)
        term = one if term is None else term + one

    @pl.when(step == 0)
    def _():
        total_ref[...] = term

    @pl.when(step > 0)
    def _():
        total_ref[...] += term

    @pl.when(step == pl.num_programs(0) - 1)
    def _():
        start = pl.multiple_of(me * rows, rows)
        own_ref[...] = total_ref[pl.ds(start, rows), :]
        for shift in range(1, groups):
            start = pl.multiple_of(((me + shift) % groups) * rows, rows)
            send_refs[shift - 1][...] = total_ref[pl.ds(start, rows), :].astype(jnp.bfloat16)


def coil_chain(pieces, place, sens, measured, sampled, forward_x, adjoint_x, table_y_re, table_y_im):
    coils, height, width = sens.shape
    groups = len(pieces)
    rows = pieces[0].shape[0]
    whole = lambda c: (0, 0)
    per_coil = lambda c: (c, 0, 0)
    step_coils = 4 if coils % 4 == 0 else (2 if coils % 2 == 0 else 1)
    flops = coils * 8 * height * width * width
    return pl.pallas_call(
        coil_chain_kernel,
        out_shape=(jax.ShapeDtypeStruct((rows, width), jnp.float32),)
        + (jax.ShapeDtypeStruct((rows, width), jnp.bfloat16),) * (groups - 1),
        grid=(coils // step_coils,),
        in_specs=[pl.BlockSpec((rows, width), whole)] * groups
        + [
            pl.BlockSpec(memory_space=pltpu.SMEM),
            pl.BlockSpec((step_coils, height, width), per_coil),
            pl.BlockSpec((step_coils, height, width), per_coil),
            pl.BlockSpec((step_coils, 1, height), per_coil),
            pl.BlockSpec((width, width), whole),
            pl.BlockSpec((width, width), whole),
            pl.BlockSpec((height, height), whole),
            pl.BlockSpec((height, height), whole),
        ],
        out_specs=(pl.BlockSpec((rows, width), whole),) * groups,
        scratch_shapes=[pltpu.VMEM((height, width), jnp.bfloat16), pltpu.VMEM((height, width), jnp.float32)],
        compiler_params=pltpu.CompilerParams(dimension_semantics=("arbitrary",)),
        cost_estimate=pl.CostEstimate(
            flops=flops, transcendentals=0, bytes_accessed=2 * 2 * coils * height * width + 4 * height * width
        ),
    )(*pieces, place, sens, measured, sampled, forward_x, adjoint_x, table_y_re, table_y_im)


def on_device(factors, temporal, maps, kdata, masks):
    width_x = maps.shape[2] // 2
    width_y = maps.shape[1]
    rows_own = factors.shape[2]
    table_x_re, table_x_im = dft_parts(width_x)
    table_y_re, table_y_im = dft_parts(width_y)
    forward_x = jnp.asarray(np.block([[table_x_re, table_x_im], [-table_x_im, table_x_re]]))
    adjoint_x = jnp.asarray(np.block([[table_x_re, -table_x_im], [table_x_im, table_x_re]]))
    table_y_re = jnp.asarray(table_y_re)
    table_y_im = jnp.asarray(table_y_im)
    time_re = temporal[0]
    time_im = temporal[1]
    mixing = jnp.stack(
        [jnp.stack([time_re, -time_im], axis=1), jnp.stack([time_im, time_re], axis=1)], axis=1
    )
    images = jnp.sum(
        mixing[:, :, :, :, None, None] * factors[None, None], axis=(2, 3)
    ).astype(jnp.bfloat16)
    frames_here = images.shape[0]
    width_own = images.shape[3]
    pieces_x = exchange_blocks(images, "frame")
    own_rows = jnp.transpose(pieces_x, (2, 1, 0, 3)).reshape(rows_own, 2 * width_x)
    groups = lax.axis_size("coil")
    me_c = lax.axis_index("coil")
    pieces = [own_rows] + [lax.ppermute(own_rows, "coil", shifted(groups, step)) for step in range(1, groups)]
    sampled = masks[0].astype(jnp.float32)[:, None, :]
    place = jnp.reshape(me_c, (1,)).astype(jnp.int32)
    own_total, *outgoing = coil_chain(
        pieces, place, maps, kdata[0], sampled, forward_x, adjoint_x, table_y_re, table_y_im
    )
    own_share = own_total
    for step in range(1, groups):
        own_share = own_share + lax.ppermute(outgoing[step - 1], "coil", shifted(groups, step)).astype(jnp.float32)
    outgoing = jnp.transpose(
        own_share.reshape(rows_own, 2, frames_here, width_own), (2, 0, 1, 3)
    ).astype(jnp.bfloat16)
    returned = exchange_blocks(outgoing, "frame").astype(jnp.float32)
    weights = jnp.stack(
        [jnp.stack([time_re.T, time_im.T], axis=2), jnp.stack([-time_im.T, time_re.T], axis=2)], axis=0
    )
    gradient = None
    for frame in range(returned.shape[0]):
        for part_in in range(2):
            term = weights[:, :, frame, part_in, None, None] * returned[frame, :, part_in][None, None]
            gradient = term if gradient is None else gradient + term
    return factors - 0.5 * gradient


def solution(mesh):
    placed = (
        P("slab", None, "coil", "frame"),
        P("slab", None, None),
        P("coil", "slab", None),
        P("frame", "coil", "slab", None),
        P("frame", "coil", "slab"),
    )
    return jax.shard_map(
        on_device,
        mesh=mesh,
        in_specs=placed,
        out_specs=P("slab", None, "coil", "frame"),
        check_vma=False,
    )
```

```python
import math

import jax
import ml_dtypes
import numpy as np
import jax.numpy as jnp
from jax import lax
from jax.experimental import pallas as pl
from jax.experimental.pallas import tpu as pltpu
from jax.sharding import PartitionSpec as P


def dft_parts(length):
    index = np.arange(length, dtype=np.int64)
    phase = (index[:, None] * index[None, :]) % length
    angle = np.float32(2.0 * math.pi / length) * phase.astype(np.float32)
    scale = np.float32(1.0 / math.sqrt(length))
    real = (np.cos(angle.astype(np.float64)).astype(np.float32) * scale).astype(ml_dtypes.bfloat16)
    imag = (-np.sin(angle.astype(np.float64)).astype(np.float32) * scale).astype(ml_dtypes.bfloat16)
    return real, imag


def rotate_plus(values, half_width):
    return jnp.concatenate([-values[..., half_width:], values[..., :half_width]], axis=-1)


def rotate_minus(values, half_width):
    return jnp.concatenate([values[..., half_width:], -values[..., :half_width]], axis=-1)


def sens_times(sens, values, half_width):
    sens_re = sens[..., :half_width].astype(jnp.float32)
    sens_im = sens[..., half_width:].astype(jnp.float32)
    value_re = values[..., :half_width].astype(jnp.float32)
    value_im = values[..., half_width:].astype(jnp.float32)
    return jnp.concatenate(
        [sens_re * value_re - sens_im * value_im, sens_re * value_im + sens_im * value_re], axis=-1
    )


def conj_sens_times(sens, values, half_width):
    sens_re = sens[..., :half_width].astype(jnp.float32)
    sens_im = sens[..., half_width:].astype(jnp.float32)
    value_re = values[..., :half_width]
    value_im = values[..., half_width:]
    return jnp.concatenate(
        [sens_re * value_re + sens_im * value_im, sens_re * value_im - sens_im * value_re], axis=-1
    )


def precise(form, first, second):
    return jnp.einsum(form, first, second, precision=lax.Precision.HIGHEST)


PERMUTE_LIMIT = 8


def shifted(count, step):
    return [(source, (source + step) % count) for source in range(count)]


def by_sender(pieces, count, me):
    ring = jnp.stack([pieces[0]] + pieces[1:][::-1])
    doubled = jnp.concatenate([ring, ring], axis=0)
    return lax.dynamic_slice_in_dim(doubled, (count - me) % count, count, 0)


def gather_blocks(value, axis):
    count = lax.axis_size(axis)
    if count > PERMUTE_LIMIT:
        return lax.all_gather(value, axis)
    me = lax.axis_index(axis)
    pieces = [value] + [lax.ppermute(value, axis, shifted(count, step)) for step in range(1, count)]
    return by_sender(pieces, count, me)


def exchange_blocks(blocks, axis):
    count = lax.axis_size(axis)
    if count > PERMUTE_LIMIT:
        return lax.all_to_all(blocks, axis, 0, 0, tiled=True)
    me = lax.axis_index(axis)
    pieces = [lax.dynamic_index_in_dim(blocks, me, 0, keepdims=False)]
    for step in range(1, count):
        outgoing = lax.dynamic_index_in_dim(blocks, (me + step) % count, 0, keepdims=False)
        pieces.append(lax.ppermute(outgoing, axis, shifted(count, step)))
    return by_sender(pieces, count, me)


def reduce_blocks(blocks, axis):
    count = lax.axis_size(axis)
    if count > PERMUTE_LIMIT:
        return lax.psum_scatter(blocks.astype(jnp.bfloat16), axis, scatter_dimension=0).astype(jnp.float32)
    me = lax.axis_index(axis)
    total = lax.dynamic_index_in_dim(blocks, me, 0, keepdims=False)
    for step in range(1, count):
        outgoing = lax.dynamic_index_in_dim(blocks, (me + step) % count, 0, keepdims=False)
        total = total + lax.ppermute(outgoing.astype(jnp.bfloat16), axis, shifted(count, step)).astype(jnp.float32)
    return total


def swap_halves(values, half_width, negate_first):
    low = values[:, :half_width]
    high = values[:, half_width:]
    if negate_first:
        return jnp.concatenate([-high, low], axis=1)
    return jnp.concatenate([high, -low], axis=1)


def coil_terms(image_ref, sens_ref, measured_ref, sampled_ref, forward_ref, adjoint_ref, table_re_ref, table_im_ref):
    coils, height, width = sens_ref.shape
    half_width = width // 2
    sens = sens_ref[...].astype(jnp.float32)
    sens_re = sens[:, :, :half_width]
    sens_im = sens[:, :, half_width:]
    image = image_ref[...].astype(jnp.float32)[None]
    image_re = image[:, :, :half_width]
    image_im = image[:, :, half_width:]
    coil = jnp.concatenate(
        [sens_re * image_re - sens_im * image_im, sens_re * image_im + sens_im * image_re], axis=2
    ).astype(jnp.bfloat16)
    half_k = jnp.dot(
        coil.reshape(coils * height, width), forward_ref[...], preferred_element_type=jnp.float32
    ).astype(jnp.bfloat16)
    table_re = table_re_ref[...]
    table_im = table_im_ref[...]
    backs = []
    for coil_index in range(coils):
        one = half_k[coil_index * height:(coil_index + 1) * height]
        kspace = jnp.dot(table_re, one, preferred_element_type=jnp.float32) + jnp.dot(
            table_im, swap_halves(one, half_width, True), preferred_element_type=jnp.float32
        )
        residual = (kspace - measured_ref[coil_index].astype(jnp.float32)).astype(jnp.bfloat16)
        sampled = sampled_ref[coil_index].astype(jnp.bfloat16)
        backs.append(
            (
                jnp.dot(table_re * sampled, residual, preferred_element_type=jnp.float32)
                + jnp.dot(
                    table_im * sampled, swap_halves(residual, half_width, False), preferred_element_type=jnp.float32
                )
            ).astype(jnp.bfloat16)
        )
    back_half = jnp.concatenate(backs, axis=0)
    coil_back = jnp.dot(back_half, adjoint_ref[...], preferred_element_type=jnp.float32).reshape(
        coils, height, width
    )
    back_re = coil_back[:, :, :half_width]
    back_im = coil_back[:, :, half_width:]
    term = jnp.concatenate(
        [sens_re * back_re + sens_im * back_im, sens_re * back_im - sens_im * back_re], axis=2
    )
    return jnp.sum(term, axis=0)


def coil_chain_kernel(*refs):
    groups = (len(refs) - 9) // 2
    pieces = refs[:groups]
    place_ref, sens_ref, measured_ref, sampled_ref, forward_ref, adjoint_ref, table_re_ref, table_im_ref = refs[
        groups:groups + 8
    ]
    own_ref = refs[groups + 8]
    send_refs = refs[groups + 9:2 * groups + 8]
    image_ref, total_ref = refs[2 * groups + 8:]
    rows = pieces[0].shape[0]
    half_width = image_ref.shape[1] // 2
    me = place_ref[0]
    step = pl.program_id(0)

    @pl.when(step == 0)
    def _():
        for block in range(groups):
            source = (me - block + groups) % groups
            value = pieces[0][...]
            for other in range(1, groups):
                value = jnp.where(source == other, pieces[other][...], value)
            image_ref[block * rows:(block + 1) * rows, :] = value

    term = coil_terms(image_ref, sens_ref, measured_ref, sampled_ref, forward_ref, adjoint_ref,
                      table_re_ref, table_im_ref)

    @pl.when(step == 0)
    def _():
        total_ref[...] = term

    @pl.when(step > 0)
    def _():
        total_ref[...] += term

    @pl.when(step == pl.num_programs(0) - 1)
    def _():
        start = pl.multiple_of(me * rows, rows)
        own_ref[...] = total_ref[pl.ds(start, rows), :]
        for shift in range(1, groups):
            start = pl.multiple_of(((me + shift) % groups) * rows, rows)
            send_refs[shift - 1][...] = total_ref[pl.ds(start, rows), :].astype(jnp.bfloat16)


def coil_chain(pieces, place, sens, measured, sampled, forward_x, adjoint_x, table_y_re, table_y_im):
    coils, height, width = sens.shape
    groups = len(pieces)
    rows = pieces[0].shape[0]
    whole = lambda c: (0, 0)
    per_coil = lambda c: (c, 0, 0)
    step_coils = 2 if coils % 2 == 0 else 1
    flops = coils * 8 * height * width * width
    return pl.pallas_call(
        coil_chain_kernel,
        out_shape=(jax.ShapeDtypeStruct((rows, width), jnp.float32),)
        + (jax.ShapeDtypeStruct((rows, width), jnp.bfloat16),) * (groups - 1),
        grid=(coils // step_coils,),
        in_specs=[pl.BlockSpec((rows, width), whole)] * groups
        + [
            pl.BlockSpec(memory_space=pltpu.SMEM),
            pl.BlockSpec((step_coils, height, width), per_coil),
            pl.BlockSpec((step_coils, height, width), per_coil),
            pl.BlockSpec((step_coils, 1, height), per_coil),
            pl.BlockSpec((width, width), whole),
            pl.BlockSpec((width, width), whole),
            pl.BlockSpec((height, height), whole),
            pl.BlockSpec((height, height), whole),
        ],
        out_specs=(pl.BlockSpec((rows, width), whole),) * groups,
        scratch_shapes=[pltpu.VMEM((height, width), jnp.bfloat16), pltpu.VMEM((height, width), jnp.float32)],
        compiler_params=pltpu.CompilerParams(dimension_semantics=("arbitrary",)),
        cost_estimate=pl.CostEstimate(
            flops=flops, transcendentals=0, bytes_accessed=2 * 2 * coils * height * width + 4 * height * width
        ),
    )(*pieces, place, sens, measured, sampled, forward_x, adjoint_x, table_y_re, table_y_im)


def on_device(factors, temporal, maps, kdata, masks):
    width_x = maps.shape[2] // 2
    width_y = maps.shape[1]
    rows_own = factors.shape[2]
    table_x_re, table_x_im = dft_parts(width_x)
    table_y_re, table_y_im = dft_parts(width_y)
    forward_x = jnp.asarray(np.block([[table_x_re, table_x_im], [-table_x_im, table_x_re]]))
    adjoint_x = jnp.asarray(np.block([[table_x_re, -table_x_im], [table_x_im, table_x_re]]))
    table_y_re = jnp.asarray(table_y_re)
    table_y_im = jnp.asarray(table_y_im)
    time_re = temporal[0]
    time_im = temporal[1]
    mixing = jnp.stack(
        [jnp.stack([time_re, -time_im], axis=1), jnp.stack([time_im, time_re], axis=1)], axis=1
    )
    images = jnp.sum(
        mixing[:, :, :, :, None, None] * factors[None, None], axis=(2, 3)
    ).astype(jnp.bfloat16)
    frames_here = images.shape[0]
    width_own = images.shape[3]
    pieces_x = exchange_blocks(images, "frame")
    own_rows = jnp.transpose(pieces_x, (2, 1, 0, 3)).reshape(rows_own, 2 * width_x)
    groups = lax.axis_size("coil")
    me_c = lax.axis_index("coil")
    pieces = [own_rows] + [lax.ppermute(own_rows, "coil", shifted(groups, step)) for step in range(1, groups)]
    sampled = masks[0].astype(jnp.float32)[:, None, :]
    place = jnp.reshape(me_c, (1,)).astype(jnp.int32)
    own_total, *outgoing = coil_chain(
        pieces, place, maps, kdata[0], sampled, forward_x, adjoint_x, table_y_re, table_y_im
    )
    own_share = own_total
    for step in range(1, groups):
        own_share = own_share + lax.ppermute(outgoing[step - 1], "coil", shifted(groups, step)).astype(jnp.float32)
    outgoing = jnp.transpose(
        own_share.reshape(rows_own, 2, frames_here, width_own), (2, 0, 1, 3)
    ).astype(jnp.bfloat16)
    returned = exchange_blocks(outgoing, "frame").astype(jnp.float32)
    weights = jnp.stack(
        [jnp.stack([time_re.T, time_im.T], axis=2), jnp.stack([-time_im.T, time_re.T], axis=2)], axis=0
    )
    gradient = None
    for frame in range(returned.shape[0]):
        for part_in in range(2):
            term = weights[:, :, frame, part_in, None, None] * returned[frame, :, part_in][None, None]
            gradient = term if gradient is None else gradient + term
    return factors - 0.5 * gradient


def solution(mesh):
    placed = (
        P("slab", None, "coil", "frame"),
        P("slab", None, None),
        P("coil", "slab", None),
        P("frame", "coil", "slab", None),
        P("frame", "coil", "slab"),
    )
    return jax.shard_map(
        on_device,
        mesh=mesh,
        in_specs=placed,
        out_specs=P("slab", None, "coil", "frame"),
        check_vma=False,
    )
```

```python
import math

import jax
import ml_dtypes
import numpy as np
import jax.numpy as jnp
from jax import lax
from jax.experimental import pallas as pl
from jax.experimental.pallas import tpu as pltpu
from jax.sharding import PartitionSpec as P


def dft_parts(length):
    index = np.arange(length, dtype=np.int64)
    phase = (index[:, None] * index[None, :]) % length
    angle = np.float32(2.0 * math.pi / length) * phase.astype(np.float32)
    scale = np.float32(1.0 / math.sqrt(length))
    real = (np.cos(angle.astype(np.float64)).astype(np.float32) * scale).astype(ml_dtypes.bfloat16)
    imag = (-np.sin(angle.astype(np.float64)).astype(np.float32) * scale).astype(ml_dtypes.bfloat16)
    return real, imag


def rotate_plus(values, half_width):
    return jnp.concatenate([-values[..., half_width:], values[..., :half_width]], axis=-1)


def rotate_minus(values, half_width):
    return jnp.concatenate([values[..., half_width:], -values[..., :half_width]], axis=-1)


def sens_times(sens, values, half_width):
    sens_re = sens[..., :half_width].astype(jnp.float32)
    sens_im = sens[..., half_width:].astype(jnp.float32)
    value_re = values[..., :half_width].astype(jnp.float32)
    value_im = values[..., half_width:].astype(jnp.float32)
    return jnp.concatenate(
        [sens_re * value_re - sens_im * value_im, sens_re * value_im + sens_im * value_re], axis=-1
    )


def conj_sens_times(sens, values, half_width):
    sens_re = sens[..., :half_width].astype(jnp.float32)
    sens_im = sens[..., half_width:].astype(jnp.float32)
    value_re = values[..., :half_width]
    value_im = values[..., half_width:]
    return jnp.concatenate(
        [sens_re * value_re + sens_im * value_im, sens_re * value_im - sens_im * value_re], axis=-1
    )


def precise(form, first, second):
    return jnp.einsum(form, first, second, precision=lax.Precision.HIGHEST)


PERMUTE_LIMIT = 8


def shifted(count, step):
    return [(source, (source + step) % count) for source in range(count)]


def by_sender(pieces, count, me):
    ring = jnp.stack([pieces[0]] + pieces[1:][::-1])
    doubled = jnp.concatenate([ring, ring], axis=0)
    return lax.dynamic_slice_in_dim(doubled, (count - me) % count, count, 0)


def gather_blocks(value, axis):
    count = lax.axis_size(axis)
    if count > PERMUTE_LIMIT:
        return lax.all_gather(value, axis)
    me = lax.axis_index(axis)
    pieces = [value] + [lax.ppermute(value, axis, shifted(count, step)) for step in range(1, count)]
    return by_sender(pieces, count, me)


def exchange_blocks(blocks, axis):
    count = lax.axis_size(axis)
    if count > PERMUTE_LIMIT:
        return lax.all_to_all(blocks, axis, 0, 0, tiled=True)
    me = lax.axis_index(axis)
    pieces = [lax.dynamic_index_in_dim(blocks, me, 0, keepdims=False)]
    for step in range(1, count):
        outgoing = lax.dynamic_index_in_dim(blocks, (me + step) % count, 0, keepdims=False)
        pieces.append(lax.ppermute(outgoing, axis, shifted(count, step)))
    return by_sender(pieces, count, me)


def reduce_blocks(blocks, axis):
    count = lax.axis_size(axis)
    if count > PERMUTE_LIMIT:
        return lax.psum_scatter(blocks.astype(jnp.bfloat16), axis, scatter_dimension=0).astype(jnp.float32)
    me = lax.axis_index(axis)
    total = lax.dynamic_index_in_dim(blocks, me, 0, keepdims=False)
    for step in range(1, count):
        outgoing = lax.dynamic_index_in_dim(blocks, (me + step) % count, 0, keepdims=False)
        total = total + lax.ppermute(outgoing.astype(jnp.bfloat16), axis, shifted(count, step)).astype(jnp.float32)
    return total


def swap_halves(values, half_width, negate_first):
    low = values[:, :half_width]
    high = values[:, half_width:]
    if negate_first:
        return jnp.concatenate([-high, low], axis=1)
    return jnp.concatenate([high, -low], axis=1)


def coil_terms(image_ref, sens_ref, measured_ref, sampled_ref, forward_ref, adjoint_ref, table_re_ref, table_im_ref):
    coils, height, width = sens_ref.shape
    half_width = width // 2
    sens = sens_ref[...].astype(jnp.float32)
    sens_re = sens[:, :, :half_width]
    sens_im = sens[:, :, half_width:]
    image = image_ref[...].astype(jnp.float32)[None]
    image_re = image[:, :, :half_width]
    image_im = image[:, :, half_width:]
    coil = jnp.concatenate(
        [sens_re * image_re - sens_im * image_im, sens_re * image_im + sens_im * image_re], axis=2
    ).astype(jnp.bfloat16)
    half_k = jnp.dot(
        coil.reshape(coils * height, width), forward_ref[...], preferred_element_type=jnp.float32
    ).astype(jnp.bfloat16)
    table_re = table_re_ref[...]
    table_im = table_im_ref[...]
    backs = []
    for coil_index in range(coils):
        one = half_k[coil_index * height:(coil_index + 1) * height]
        kspace = jnp.dot(table_re, one, preferred_element_type=jnp.float32) + jnp.dot(
            table_im, swap_halves(one, half_width, True), preferred_element_type=jnp.float32
        )
        residual = (kspace - measured_ref[coil_index].astype(jnp.float32)).astype(jnp.bfloat16)
        sampled = sampled_ref[coil_index].astype(jnp.bfloat16)
        backs.append(
            (
                jnp.dot(table_re * sampled, residual, preferred_element_type=jnp.float32)
                + jnp.dot(
                    table_im * sampled, swap_halves(residual, half_width, False), preferred_element_type=jnp.float32
                )
            ).astype(jnp.bfloat16)
        )
    back_half = jnp.concatenate(backs, axis=0)
    coil_back = jnp.dot(back_half, adjoint_ref[...], preferred_element_type=jnp.float32).reshape(
        coils, height, width
    )
    back_re = coil_back[:, :, :half_width]
    back_im = coil_back[:, :, half_width:]
    term = jnp.concatenate(
        [sens_re * back_re + sens_im * back_im, sens_re * back_im - sens_im * back_re], axis=2
    )
    return jnp.sum(term, axis=0)


def coil_chain_kernel(*refs):
    groups = (len(refs) - 9) // 2
    pieces = refs[:groups]
    place_ref, sens_ref, measured_ref, sampled_ref, forward_ref, adjoint_ref, table_re_ref, table_im_ref = refs[
        groups:groups + 8
    ]
    own_ref = refs[groups + 8]
    send_refs = refs[groups + 9:2 * groups + 8]
    image_ref, total_ref = refs[2 * groups + 8:]
    rows = pieces[0].shape[0]
    half_width = image_ref.shape[1] // 2
    me = place_ref[0]
    step = pl.program_id(0)

    @pl.when(step == 0)
    def _():
        for block in range(groups):
            source = (me - block + groups) % groups
            value = pieces[0][...]
            for other in range(1, groups):
                value = jnp.where(source == other, pieces[other][...], value)
            image_ref[block * rows:(block + 1) * rows, :] = value

    term = coil_terms(image_ref, sens_ref, measured_ref, sampled_ref, forward_ref, adjoint_ref,
                      table_re_ref, table_im_ref)

    @pl.when(step == 0)
    def _():
        total_ref[...] = term

    @pl.when(step > 0)
    def _():
        total_ref[...] += term

    @pl.when(step == pl.num_programs(0) - 1)
    def _():
        start = pl.multiple_of(me * rows, rows)
        own_ref[...] = total_ref[pl.ds(start, rows), :]
        for shift in range(1, groups):
            start = pl.multiple_of(((me + shift) % groups) * rows, rows)
            send_refs[shift - 1][...] = total_ref[pl.ds(start, rows), :].astype(jnp.bfloat16)


def coil_chain(pieces, place, sens, measured, sampled, forward_x, adjoint_x, table_y_re, table_y_im):
    coils, height, width = sens.shape
    groups = len(pieces)
    rows = pieces[0].shape[0]
    whole = lambda c: (0, 0)
    per_coil = lambda c: (c, 0, 0)
    step_coils = 4 if coils % 4 == 0 else (2 if coils % 2 == 0 else 1)
    flops = coils * 8 * height * width * width
    return pl.pallas_call(
        coil_chain_kernel,
        out_shape=(jax.ShapeDtypeStruct((rows, width), jnp.float32),)
        + (jax.ShapeDtypeStruct((rows, width), jnp.bfloat16),) * (groups - 1),
        grid=(coils // step_coils,),
        in_specs=[pl.BlockSpec((rows, width), whole)] * groups
        + [
            pl.BlockSpec(memory_space=pltpu.SMEM),
            pl.BlockSpec((step_coils, height, width), per_coil),
            pl.BlockSpec((step_coils, height, width), per_coil),
            pl.BlockSpec((step_coils, 1, height), per_coil),
            pl.BlockSpec((width, width), whole),
            pl.BlockSpec((width, width), whole),
            pl.BlockSpec((height, height), whole),
            pl.BlockSpec((height, height), whole),
        ],
        out_specs=(pl.BlockSpec((rows, width), whole),) * groups,
        scratch_shapes=[pltpu.VMEM((height, width), jnp.bfloat16), pltpu.VMEM((height, width), jnp.float32)],
        compiler_params=pltpu.CompilerParams(dimension_semantics=("arbitrary",)),
        cost_estimate=pl.CostEstimate(
            flops=flops, transcendentals=0, bytes_accessed=2 * 2 * coils * height * width + 4 * height * width
        ),
    )(*pieces, place, sens, measured, sampled, forward_x, adjoint_x, table_y_re, table_y_im)


def on_device(factors, temporal, maps, kdata, masks):
    width_x = maps.shape[2] // 2
    width_y = maps.shape[1]
    rows_own = factors.shape[2]
    table_x_re, table_x_im = dft_parts(width_x)
    table_y_re, table_y_im = dft_parts(width_y)
    forward_x = jnp.asarray(np.block([[table_x_re, table_x_im], [-table_x_im, table_x_re]]))
    adjoint_x = jnp.asarray(np.block([[table_x_re, -table_x_im], [table_x_im, table_x_re]]))
    table_y_re = jnp.asarray(table_y_re)
    table_y_im = jnp.asarray(table_y_im)
    time_re = temporal[0]
    time_im = temporal[1]
    mixing = jnp.stack(
        [jnp.stack([time_re, -time_im], axis=1), jnp.stack([time_im, time_re], axis=1)], axis=1
    )
    images = jnp.sum(
        mixing[:, :, :, :, None, None] * factors[None, None], axis=(2, 3)
    ).astype(jnp.bfloat16)
    frames_here = images.shape[0]
    width_own = images.shape[3]
    pieces_x = exchange_blocks(images, "frame")
    own_rows = jnp.transpose(pieces_x, (2, 1, 0, 3)).reshape(rows_own, 2 * width_x)
    groups = lax.axis_size("coil")
    me_c = lax.axis_index("coil")
    pieces = [own_rows] + [lax.ppermute(own_rows, "coil", shifted(groups, step)) for step in range(1, groups)]
    sampled = masks[0].astype(jnp.float32)[:, None, :]
    place = jnp.reshape(me_c, (1,)).astype(jnp.int32)
    own_total, *outgoing = coil_chain(
        pieces, place, maps, kdata[0], sampled, forward_x, adjoint_x, table_y_re, table_y_im
    )
    own_share = own_total
    for step in range(1, groups):
        own_share = own_share + lax.ppermute(outgoing[step - 1], "coil", shifted(groups, step)).astype(jnp.float32)
    outgoing = jnp.transpose(
        own_share.reshape(rows_own, 2, frames_here, width_own), (2, 0, 1, 3)
    ).astype(jnp.bfloat16)
    returned = exchange_blocks(outgoing, "frame").astype(jnp.float32)
    weights = jnp.stack(
        [jnp.stack([time_re.T, time_im.T], axis=2), jnp.stack([-time_im.T, time_re.T], axis=2)], axis=0
    )
    gradient = None
    for frame in range(returned.shape[0]):
        for part_in in range(2):
            term = weights[:, :, frame, part_in, None, None] * returned[frame, :, part_in][None, None]
            gradient = term if gradient is None else gradient + term
    return factors - 0.5 * gradient


def solution(mesh):
    placed = (
        P("slab", None, "coil", "frame"),
        P("slab", None, None),
        P("coil", "slab", None),
        P("frame", "coil", "slab", None),
        P("frame", "coil", "slab"),
    )
    return jax.shard_map(
        on_device,
        mesh=mesh,
        in_specs=placed,
        out_specs=P("slab", None, "coil", "frame"),
        check_vma=False,
    )
```

```python
import math

import jax
import ml_dtypes
import numpy as np
import jax.numpy as jnp
from jax import lax
from jax.experimental import pallas as pl
from jax.experimental.pallas import tpu as pltpu
from jax.sharding import PartitionSpec as P


def dft_parts(length):
    index = np.arange(length, dtype=np.int64)
    phase = (index[:, None] * index[None, :]) % length
    angle = np.float32(2.0 * math.pi / length) * phase.astype(np.float32)
    scale = np.float32(1.0 / math.sqrt(length))
    real = (np.cos(angle.astype(np.float64)).astype(np.float32) * scale).astype(ml_dtypes.bfloat16)
    imag = (-np.sin(angle.astype(np.float64)).astype(np.float32) * scale).astype(ml_dtypes.bfloat16)
    return real, imag


def rotate_plus(values, half_width):
    return jnp.concatenate([-values[..., half_width:], values[..., :half_width]], axis=-1)


def rotate_minus(values, half_width):
    return jnp.concatenate([values[..., half_width:], -values[..., :half_width]], axis=-1)


def sens_times(sens, values, half_width):
    sens_re = sens[..., :half_width].astype(jnp.float32)
    sens_im = sens[..., half_width:].astype(jnp.float32)
    value_re = values[..., :half_width].astype(jnp.float32)
    value_im = values[..., half_width:].astype(jnp.float32)
    return jnp.concatenate(
        [sens_re * value_re - sens_im * value_im, sens_re * value_im + sens_im * value_re], axis=-1
    )


def conj_sens_times(sens, values, half_width):
    sens_re = sens[..., :half_width].astype(jnp.float32)
    sens_im = sens[..., half_width:].astype(jnp.float32)
    value_re = values[..., :half_width]
    value_im = values[..., half_width:]
    return jnp.concatenate(
        [sens_re * value_re + sens_im * value_im, sens_re * value_im - sens_im * value_re], axis=-1
    )


def precise(form, first, second):
    return jnp.einsum(form, first, second, precision=lax.Precision.HIGHEST)


PERMUTE_LIMIT = 8


def shifted(count, step):
    return [(source, (source + step) % count) for source in range(count)]


def by_sender(pieces, count, me):
    ring = jnp.stack([pieces[0]] + pieces[1:][::-1])
    doubled = jnp.concatenate([ring, ring], axis=0)
    return lax.dynamic_slice_in_dim(doubled, (count - me) % count, count, 0)


def gather_blocks(value, axis):
    count = lax.axis_size(axis)
    if count > PERMUTE_LIMIT:
        return lax.all_gather(value, axis)
    me = lax.axis_index(axis)
    pieces = [value] + [lax.ppermute(value, axis, shifted(count, step)) for step in range(1, count)]
    return by_sender(pieces, count, me)


def exchange_blocks(blocks, axis):
    count = lax.axis_size(axis)
    if count > PERMUTE_LIMIT:
        return lax.all_to_all(blocks, axis, 0, 0, tiled=True)
    me = lax.axis_index(axis)
    pieces = [lax.dynamic_index_in_dim(blocks, me, 0, keepdims=False)]
    for step in range(1, count):
        outgoing = lax.dynamic_index_in_dim(blocks, (me + step) % count, 0, keepdims=False)
        pieces.append(lax.ppermute(outgoing, axis, shifted(count, step)))
    return by_sender(pieces, count, me)


def reduce_blocks(blocks, axis):
    count = lax.axis_size(axis)
    if count > PERMUTE_LIMIT:
        return lax.psum_scatter(blocks.astype(jnp.bfloat16), axis, scatter_dimension=0).astype(jnp.float32)
    me = lax.axis_index(axis)
    total = lax.dynamic_index_in_dim(blocks, me, 0, keepdims=False)
    for step in range(1, count):
        outgoing = lax.dynamic_index_in_dim(blocks, (me + step) % count, 0, keepdims=False)
        total = total + lax.ppermute(outgoing.astype(jnp.bfloat16), axis, shifted(count, step)).astype(jnp.float32)
    return total


def swap_halves(values, half_width, negate_first):
    low = values[:, :half_width]
    high = values[:, half_width:]
    if negate_first:
        return jnp.concatenate([-high, low], axis=1)
    return jnp.concatenate([high, -low], axis=1)


def coil_terms(image_ref, sens_ref, measured_ref, sampled_ref, forward_ref, adjoint_ref, table_ref):
    coils, height, width = sens_ref.shape
    half_width = width // 2
    sens = sens_ref[...].astype(jnp.float32)
    sens_re = sens[:, :, :half_width]
    sens_im = sens[:, :, half_width:]
    image = image_ref[...].astype(jnp.float32)[None]
    image_re = image[:, :, :half_width]
    image_im = image[:, :, half_width:]
    coil = jnp.concatenate(
        [sens_re * image_re - sens_im * image_im, sens_re * image_im + sens_im * image_re], axis=2
    ).astype(jnp.bfloat16)
    half_k = jnp.dot(coil.reshape(coils * height, width), forward_ref[...], preferred_element_type=jnp.float32)
    table = table_ref[...]
    backs = []
    for coil_index in range(coils):
        one = half_k[coil_index * height:(coil_index + 1) * height].astype(jnp.bfloat16).astype(jnp.float32)
        turned = jnp.concatenate([one[:, :half_width].T, one[:, half_width:].T], axis=0).astype(jnp.bfloat16)
        parts = jnp.dot(turned, table, preferred_element_type=jnp.float32)
        kspace_re = parts[:half_width, :height] - parts[half_width:, height:]
        kspace_im = parts[:half_width, height:] + parts[half_width:, :height]
        sampled = sampled_ref[coil_index]
        residual = jnp.concatenate(
            [
                (sampled * (kspace_re - measured_ref[coil_index, 0].astype(jnp.float32))).astype(jnp.bfloat16),
                (sampled * (kspace_im - measured_ref[coil_index, 1].astype(jnp.float32))).astype(jnp.bfloat16),
            ],
            axis=0,
        )
        parts = jnp.dot(residual, table, preferred_element_type=jnp.float32)
        back_re = (parts[:half_width, :height] + parts[half_width:, height:]).astype(jnp.bfloat16)
        back_im = (parts[half_width:, :height] - parts[:half_width, height:]).astype(jnp.bfloat16)
        backs.append(
            jnp.concatenate([back_re.astype(jnp.float32).T, back_im.astype(jnp.float32).T], axis=1).astype(
                jnp.bfloat16
            )
        )
    back_half = jnp.concatenate(backs, axis=0)
    coil_back = jnp.dot(back_half, adjoint_ref[...], preferred_element_type=jnp.float32).reshape(
        coils, height, width
    )
    back_re = coil_back[:, :, :half_width]
    back_im = coil_back[:, :, half_width:]
    term = jnp.concatenate(
        [sens_re * back_re + sens_im * back_im, sens_re * back_im - sens_im * back_re], axis=2
    )
    return jnp.sum(term, axis=0)


def coil_chain_kernel(*refs):
    groups = (len(refs) - 8) // 2
    pieces = refs[:groups]
    place_ref, sens_ref, measured_ref, sampled_ref, forward_ref, adjoint_ref, table_ref = refs[groups:groups + 7]
    own_ref = refs[groups + 7]
    send_refs = refs[groups + 8:2 * groups + 7]
    image_ref, total_ref = refs[2 * groups + 7:]
    rows = pieces[0].shape[0]
    half_width = image_ref.shape[1] // 2
    me = place_ref[0]
    step = pl.program_id(0)

    @pl.when(step == 0)
    def _():
        for block in range(groups):
            source = (me - block + groups) % groups
            value = pieces[0][...]
            for other in range(1, groups):
                value = jnp.where(source == other, pieces[other][...], value)
            image_ref[block * rows:(block + 1) * rows, :] = value

    term = coil_terms(image_ref, sens_ref, measured_ref, sampled_ref, forward_ref, adjoint_ref, table_ref)

    @pl.when(step == 0)
    def _():
        total_ref[...] = term

    @pl.when(step > 0)
    def _():
        total_ref[...] += term

    @pl.when(step == pl.num_programs(0) - 1)
    def _():
        start = pl.multiple_of(me * rows, rows)
        own_ref[...] = total_ref[pl.ds(start, rows), :]
        for shift in range(1, groups):
            start = pl.multiple_of(((me + shift) % groups) * rows, rows)
            send_refs[shift - 1][...] = total_ref[pl.ds(start, rows), :].astype(jnp.bfloat16)


def coil_chain(pieces, place, sens, measured, sampled, forward_x, adjoint_x, table_y):
    coils, height, width = sens.shape
    groups = len(pieces)
    rows = pieces[0].shape[0]
    whole = lambda c: (0, 0)
    per_coil = lambda c: (c, 0, 0)
    step_coils = 4 if coils % 4 == 0 else (2 if coils % 2 == 0 else 1)
    flops = coils * 8 * height * width * width
    return pl.pallas_call(
        coil_chain_kernel,
        out_shape=(jax.ShapeDtypeStruct((rows, width), jnp.float32),)
        + (jax.ShapeDtypeStruct((rows, width), jnp.bfloat16),) * (groups - 1),
        grid=(coils // step_coils,),
        in_specs=[pl.BlockSpec((rows, width), whole)] * groups
        + [
            pl.BlockSpec(memory_space=pltpu.SMEM),
            pl.BlockSpec((step_coils, height, width), per_coil),
            pl.BlockSpec((step_coils, 2, width // 2, height), lambda c: (c, 0, 0, 0)),
            pl.BlockSpec((step_coils, 1, height), per_coil),
            pl.BlockSpec((width, width), whole),
            pl.BlockSpec((width, width), whole),
            pl.BlockSpec((height, 2 * height), whole),
        ],
        out_specs=(pl.BlockSpec((rows, width), whole),) * groups,
        scratch_shapes=[pltpu.VMEM((height, width), jnp.bfloat16), pltpu.VMEM((height, width), jnp.float32)],
        compiler_params=pltpu.CompilerParams(dimension_semantics=("arbitrary",)),
        cost_estimate=pl.CostEstimate(
            flops=flops, transcendentals=0, bytes_accessed=2 * 2 * coils * height * width + 4 * height * width
        ),
    )(*pieces, place, sens, measured, sampled, forward_x, adjoint_x, table_y)


def on_device(factors, temporal, maps, kdata, masks):
    width_x = maps.shape[2] // 2
    width_y = maps.shape[1]
    rows_own = factors.shape[2]
    table_x_re, table_x_im = dft_parts(width_x)
    table_y_re, table_y_im = dft_parts(width_y)
    forward_x = jnp.asarray(np.block([[table_x_re, table_x_im], [-table_x_im, table_x_re]]))
    adjoint_x = jnp.asarray(np.block([[table_x_re, -table_x_im], [table_x_im, table_x_re]]))
    table_y = jnp.asarray(np.concatenate([table_y_re, table_y_im], axis=1))
    time_re = temporal[0]
    time_im = temporal[1]
    mixing = jnp.stack(
        [jnp.stack([time_re, -time_im], axis=1), jnp.stack([time_im, time_re], axis=1)], axis=1
    )
    images = jnp.sum(
        mixing[:, :, :, :, None, None] * factors[None, None], axis=(2, 3)
    ).astype(jnp.bfloat16)
    frames_here = images.shape[0]
    width_own = images.shape[3]
    pieces_x = exchange_blocks(images, "frame")
    own_rows = jnp.transpose(pieces_x, (2, 1, 0, 3)).reshape(rows_own, 2 * width_x)
    groups = lax.axis_size("coil")
    me_c = lax.axis_index("coil")
    pieces = [own_rows] + [lax.ppermute(own_rows, "coil", shifted(groups, step)) for step in range(1, groups)]
    sampled = masks[0].astype(jnp.float32)[:, None, :]
    place = jnp.reshape(me_c, (1,)).astype(jnp.int32)
    coils_here = kdata.shape[1]
    measured = jnp.transpose(kdata[0].reshape(coils_here, width_y, 2, width_x), (0, 2, 3, 1))
    own_total, *outgoing = coil_chain(
        pieces, place, maps, measured, sampled, forward_x, adjoint_x, table_y
    )
    own_share = own_total
    for step in range(1, groups):
        own_share = own_share + lax.ppermute(outgoing[step - 1], "coil", shifted(groups, step)).astype(jnp.float32)
    outgoing = jnp.transpose(
        own_share.reshape(rows_own, 2, frames_here, width_own), (2, 0, 1, 3)
    ).astype(jnp.bfloat16)
    returned = exchange_blocks(outgoing, "frame").astype(jnp.float32)
    weights = jnp.stack(
        [jnp.stack([time_re.T, time_im.T], axis=2), jnp.stack([-time_im.T, time_re.T], axis=2)], axis=0
    )
    gradient = None
    for frame in range(returned.shape[0]):
        for part_in in range(2):
            term = weights[:, :, frame, part_in, None, None] * returned[frame, :, part_in][None, None]
            gradient = term if gradient is None else gradient + term
    return factors - 0.5 * gradient


def solution(mesh):
    placed = (
        P("slab", None, "coil", "frame"),
        P("slab", None, None),
        P("coil", "slab", None),
        P("frame", "coil", "slab", None),
        P("frame", "coil", "slab"),
    )
    return jax.shard_map(
        on_device,
        mesh=mesh,
        in_specs=placed,
        out_specs=P("slab", None, "coil", "frame"),
        check_vma=False,
    )
```

```python
import math

import jax
import ml_dtypes
import numpy as np
import jax.numpy as jnp
from jax import lax
from jax.experimental import pallas as pl
from jax.experimental.pallas import tpu as pltpu
from jax.sharding import PartitionSpec as P


def dft_parts(length):
    index = np.arange(length, dtype=np.int64)
    phase = (index[:, None] * index[None, :]) % length
    angle = np.float32(2.0 * math.pi / length) * phase.astype(np.float32)
    scale = np.float32(1.0 / math.sqrt(length))
    real = (np.cos(angle.astype(np.float64)).astype(np.float32) * scale).astype(ml_dtypes.bfloat16)
    imag = (-np.sin(angle.astype(np.float64)).astype(np.float32) * scale).astype(ml_dtypes.bfloat16)
    return real, imag


def rotate_plus(values, half_width):
    return jnp.concatenate([-values[..., half_width:], values[..., :half_width]], axis=-1)


def rotate_minus(values, half_width):
    return jnp.concatenate([values[..., half_width:], -values[..., :half_width]], axis=-1)


def sens_times(sens, values, half_width):
    sens_re = sens[..., :half_width].astype(jnp.float32)
    sens_im = sens[..., half_width:].astype(jnp.float32)
    value_re = values[..., :half_width].astype(jnp.float32)
    value_im = values[..., half_width:].astype(jnp.float32)
    return jnp.concatenate(
        [sens_re * value_re - sens_im * value_im, sens_re * value_im + sens_im * value_re], axis=-1
    )


def conj_sens_times(sens, values, half_width):
    sens_re = sens[..., :half_width].astype(jnp.float32)
    sens_im = sens[..., half_width:].astype(jnp.float32)
    value_re = values[..., :half_width]
    value_im = values[..., half_width:]
    return jnp.concatenate(
        [sens_re * value_re + sens_im * value_im, sens_re * value_im - sens_im * value_re], axis=-1
    )


def precise(form, first, second):
    return jnp.einsum(form, first, second, precision=lax.Precision.HIGHEST)


PERMUTE_LIMIT = 8


def shifted(count, step):
    return [(source, (source + step) % count) for source in range(count)]


def by_sender(pieces, count, me):
    ring = jnp.stack([pieces[0]] + pieces[1:][::-1])
    doubled = jnp.concatenate([ring, ring], axis=0)
    return lax.dynamic_slice_in_dim(doubled, (count - me) % count, count, 0)


def gather_blocks(value, axis):
    count = lax.axis_size(axis)
    if count > PERMUTE_LIMIT:
        return lax.all_gather(value, axis)
    me = lax.axis_index(axis)
    pieces = [value] + [lax.ppermute(value, axis, shifted(count, step)) for step in range(1, count)]
    return by_sender(pieces, count, me)


def exchange_blocks(blocks, axis):
    count = lax.axis_size(axis)
    if count > PERMUTE_LIMIT:
        return lax.all_to_all(blocks, axis, 0, 0, tiled=True)
    me = lax.axis_index(axis)
    pieces = [lax.dynamic_index_in_dim(blocks, me, 0, keepdims=False)]
    for step in range(1, count):
        outgoing = lax.dynamic_index_in_dim(blocks, (me + step) % count, 0, keepdims=False)
        pieces.append(lax.ppermute(outgoing, axis, shifted(count, step)))
    return by_sender(pieces, count, me)


def reduce_blocks(blocks, axis):
    count = lax.axis_size(axis)
    if count > PERMUTE_LIMIT:
        return lax.psum_scatter(blocks.astype(jnp.bfloat16), axis, scatter_dimension=0).astype(jnp.float32)
    me = lax.axis_index(axis)
    total = lax.dynamic_index_in_dim(blocks, me, 0, keepdims=False)
    for step in range(1, count):
        outgoing = lax.dynamic_index_in_dim(blocks, (me + step) % count, 0, keepdims=False)
        total = total + lax.ppermute(outgoing.astype(jnp.bfloat16), axis, shifted(count, step)).astype(jnp.float32)
    return total


def swap_halves(values, half_width, negate_first):
    low = values[:, :half_width]
    high = values[:, half_width:]
    if negate_first:
        return jnp.concatenate([-high, low], axis=1)
    return jnp.concatenate([high, -low], axis=1)


def coil_terms(image_ref, sens_ref, measured_ref, sampled_ref, forward_ref, adjoint_ref, table_ref):
    coils, height, width = sens_ref.shape
    half_width = width // 2
    sens = sens_ref[...].astype(jnp.float32)
    sens_re = sens[:, :, :half_width]
    sens_im = sens[:, :, half_width:]
    image = image_ref[...].astype(jnp.float32)[None]
    image_re = image[:, :, :half_width]
    image_im = image[:, :, half_width:]
    coil = jnp.concatenate(
        [sens_re * image_re - sens_im * image_im, sens_re * image_im + sens_im * image_re], axis=2
    ).astype(jnp.bfloat16)
    half_k = jnp.dot(coil.reshape(coils * height, width), forward_ref[...], preferred_element_type=jnp.float32)
    table = table_ref[...]
    backs = []
    for coil_index in range(coils):
        one = half_k[coil_index * height:(coil_index + 1) * height].astype(jnp.bfloat16).astype(jnp.float32)
        turned = jnp.concatenate([one[:, :half_width].T, one[:, half_width:].T], axis=0).astype(jnp.bfloat16)
        parts = jnp.dot(turned, table, preferred_element_type=jnp.float32)
        kspace_re = parts[:half_width, :height] - parts[half_width:, height:]
        kspace_im = parts[:half_width, height:] + parts[half_width:, :height]
        sampled = sampled_ref[coil_index]
        measured = measured_ref[coil_index].astype(jnp.float32)
        residual = jnp.concatenate(
            [
                (sampled * (kspace_re - measured[:, :half_width].T)).astype(jnp.bfloat16),
                (sampled * (kspace_im - measured[:, half_width:].T)).astype(jnp.bfloat16),
            ],
            axis=0,
        )
        parts = jnp.dot(residual, table, preferred_element_type=jnp.float32)
        back_re = (parts[:half_width, :height] + parts[half_width:, height:]).astype(jnp.bfloat16)
        back_im = (parts[half_width:, :height] - parts[:half_width, height:]).astype(jnp.bfloat16)
        backs.append(
            jnp.concatenate([back_re.astype(jnp.float32).T, back_im.astype(jnp.float32).T], axis=1).astype(
                jnp.bfloat16
            )
        )
    back_half = jnp.concatenate(backs, axis=0)
    coil_back = jnp.dot(back_half, adjoint_ref[...], preferred_element_type=jnp.float32).reshape(
        coils, height, width
    )
    back_re = coil_back[:, :, :half_width]
    back_im = coil_back[:, :, half_width:]
    term = jnp.concatenate(
        [sens_re * back_re + sens_im * back_im, sens_re * back_im - sens_im * back_re], axis=2
    )
    return jnp.sum(term, axis=0)


def coil_chain_kernel(*refs):
    groups = (len(refs) - 8) // 2
    pieces = refs[:groups]
    place_ref, sens_ref, measured_ref, sampled_ref, forward_ref, adjoint_ref, table_ref = refs[groups:groups + 7]
    own_ref = refs[groups + 7]
    send_refs = refs[groups + 8:2 * groups + 7]
    image_ref, total_ref = refs[2 * groups + 7:]
    rows = pieces[0].shape[0]
    half_width = image_ref.shape[1] // 2
    me = place_ref[0]
    step = pl.program_id(0)

    @pl.when(step == 0)
    def _():
        for block in range(groups):
            source = (me - block + groups) % groups
            value = pieces[0][...]
            for other in range(1, groups):
                value = jnp.where(source == other, pieces[other][...], value)
            image_ref[block * rows:(block + 1) * rows, :] = value

    term = coil_terms(image_ref, sens_ref, measured_ref, sampled_ref, forward_ref, adjoint_ref, table_ref)

    @pl.when(step == 0)
    def _():
        total_ref[...] = term

    @pl.when(step > 0)
    def _():
        total_ref[...] += term

    @pl.when(step == pl.num_programs(0) - 1)
    def _():
        start = pl.multiple_of(me * rows, rows)
        own_ref[...] = total_ref[pl.ds(start, rows), :]
        for shift in range(1, groups):
            start = pl.multiple_of(((me + shift) % groups) * rows, rows)
            send_refs[shift - 1][...] = total_ref[pl.ds(start, rows), :].astype(jnp.bfloat16)


def coil_chain(pieces, place, sens, measured, sampled, forward_x, adjoint_x, table_y):
    coils, height, width = sens.shape
    groups = len(pieces)
    rows = pieces[0].shape[0]
    whole = lambda c: (0, 0)
    per_coil = lambda c: (c, 0, 0)
    step_coils = 4 if coils % 4 == 0 else (2 if coils % 2 == 0 else 1)
    flops = coils * 8 * height * width * width
    return pl.pallas_call(
        coil_chain_kernel,
        out_shape=(jax.ShapeDtypeStruct((rows, width), jnp.float32),)
        + (jax.ShapeDtypeStruct((rows, width), jnp.bfloat16),) * (groups - 1),
        grid=(coils // step_coils,),
        in_specs=[pl.BlockSpec((rows, width), whole)] * groups
        + [
            pl.BlockSpec(memory_space=pltpu.SMEM),
            pl.BlockSpec((step_coils, height, width), per_coil),
            pl.BlockSpec((step_coils, height, width), per_coil),
            pl.BlockSpec((step_coils, 1, height), per_coil),
            pl.BlockSpec((width, width), whole),
            pl.BlockSpec((width, width), whole),
            pl.BlockSpec((height, 2 * height), whole),
        ],
        out_specs=(pl.BlockSpec((rows, width), whole),) * groups,
        scratch_shapes=[pltpu.VMEM((height, width), jnp.bfloat16), pltpu.VMEM((height, width), jnp.float32)],
        compiler_params=pltpu.CompilerParams(dimension_semantics=("arbitrary",)),
        cost_estimate=pl.CostEstimate(
            flops=flops, transcendentals=0, bytes_accessed=2 * 2 * coils * height * width + 4 * height * width
        ),
    )(*pieces, place, sens, measured, sampled, forward_x, adjoint_x, table_y)


def on_device(factors, temporal, maps, kdata, masks):
    width_x = maps.shape[2] // 2
    width_y = maps.shape[1]
    rows_own = factors.shape[2]
    table_x_re, table_x_im = dft_parts(width_x)
    table_y_re, table_y_im = dft_parts(width_y)
    forward_x = jnp.asarray(np.block([[table_x_re, table_x_im], [-table_x_im, table_x_re]]))
    adjoint_x = jnp.asarray(np.block([[table_x_re, -table_x_im], [table_x_im, table_x_re]]))
    table_y = jnp.asarray(np.concatenate([table_y_re, table_y_im], axis=1))
    time_re = temporal[0]
    time_im = temporal[1]
    mixing = jnp.stack(
        [jnp.stack([time_re, -time_im], axis=1), jnp.stack([time_im, time_re], axis=1)], axis=1
    )
    images = jnp.sum(
        mixing[:, :, :, :, None, None] * factors[None, None], axis=(2, 3)
    ).astype(jnp.bfloat16)
    frames_here = images.shape[0]
    width_own = images.shape[3]
    pieces_x = exchange_blocks(images, "frame")
    own_rows = jnp.transpose(pieces_x, (2, 1, 0, 3)).reshape(rows_own, 2 * width_x)
    groups = lax.axis_size("coil")
    me_c = lax.axis_index("coil")
    pieces = [own_rows] + [lax.ppermute(own_rows, "coil", shifted(groups, step)) for step in range(1, groups)]
    sampled = masks[0].astype(jnp.float32)[:, None, :]
    place = jnp.reshape(me_c, (1,)).astype(jnp.int32)
    measured = kdata[0]
    own_total, *outgoing = coil_chain(
        pieces, place, maps, measured, sampled, forward_x, adjoint_x, table_y
    )
    own_share = own_total
    for step in range(1, groups):
        own_share = own_share + lax.ppermute(outgoing[step - 1], "coil", shifted(groups, step)).astype(jnp.float32)
    outgoing = jnp.transpose(
        own_share.reshape(rows_own, 2, frames_here, width_own), (2, 0, 1, 3)
    ).astype(jnp.bfloat16)
    returned = exchange_blocks(outgoing, "frame").astype(jnp.float32)
    weights = jnp.stack(
        [jnp.stack([time_re.T, time_im.T], axis=2), jnp.stack([-time_im.T, time_re.T], axis=2)], axis=0
    )
    gradient = None
    for frame in range(returned.shape[0]):
        for part_in in range(2):
            term = weights[:, :, frame, part_in, None, None] * returned[frame, :, part_in][None, None]
            gradient = term if gradient is None else gradient + term
    return factors - 0.5 * gradient


def solution(mesh):
    placed = (
        P("slab", None, "coil", "frame"),
        P("slab", None, None),
        P("coil", "slab", None),
        P("frame", "coil", "slab", None),
        P("frame", "coil", "slab"),
    )
    return jax.shard_map(
        on_device,
        mesh=mesh,
        in_specs=placed,
        out_specs=P("slab", None, "coil", "frame"),
        check_vma=False,
    )
```

```python
import math

import jax
import ml_dtypes
import numpy as np
import jax.numpy as jnp
from jax import lax
from jax.experimental import pallas as pl
from jax.experimental.pallas import tpu as pltpu
from jax.sharding import PartitionSpec as P


def dft_parts(length):
    index = np.arange(length, dtype=np.int64)
    phase = (index[:, None] * index[None, :]) % length
    angle = np.float32(2.0 * math.pi / length) * phase.astype(np.float32)
    scale = np.float32(1.0 / math.sqrt(length))
    real = (np.cos(angle.astype(np.float64)).astype(np.float32) * scale).astype(ml_dtypes.bfloat16)
    imag = (-np.sin(angle.astype(np.float64)).astype(np.float32) * scale).astype(ml_dtypes.bfloat16)
    return real, imag


def rotate_plus(values, half_width):
    return jnp.concatenate([-values[..., half_width:], values[..., :half_width]], axis=-1)


def rotate_minus(values, half_width):
    return jnp.concatenate([values[..., half_width:], -values[..., :half_width]], axis=-1)


def sens_times(sens, values, half_width):
    sens_re = sens[..., :half_width].astype(jnp.float32)
    sens_im = sens[..., half_width:].astype(jnp.float32)
    value_re = values[..., :half_width].astype(jnp.float32)
    value_im = values[..., half_width:].astype(jnp.float32)
    return jnp.concatenate(
        [sens_re * value_re - sens_im * value_im, sens_re * value_im + sens_im * value_re], axis=-1
    )


def conj_sens_times(sens, values, half_width):
    sens_re = sens[..., :half_width].astype(jnp.float32)
    sens_im = sens[..., half_width:].astype(jnp.float32)
    value_re = values[..., :half_width]
    value_im = values[..., half_width:]
    return jnp.concatenate(
        [sens_re * value_re + sens_im * value_im, sens_re * value_im - sens_im * value_re], axis=-1
    )


def precise(form, first, second):
    return jnp.einsum(form, first, second, precision=lax.Precision.HIGHEST)


PERMUTE_LIMIT = 8


def shifted(count, step):
    return [(source, (source + step) % count) for source in range(count)]


def by_sender(pieces, count, me):
    ring = jnp.stack([pieces[0]] + pieces[1:][::-1])
    doubled = jnp.concatenate([ring, ring], axis=0)
    return lax.dynamic_slice_in_dim(doubled, (count - me) % count, count, 0)


def gather_blocks(value, axis):
    count = lax.axis_size(axis)
    if count > PERMUTE_LIMIT:
        return lax.all_gather(value, axis)
    me = lax.axis_index(axis)
    pieces = [value] + [lax.ppermute(value, axis, shifted(count, step)) for step in range(1, count)]
    return by_sender(pieces, count, me)


def exchange_blocks(blocks, axis):
    count = lax.axis_size(axis)
    if count > PERMUTE_LIMIT:
        return lax.all_to_all(blocks, axis, 0, 0, tiled=True)
    me = lax.axis_index(axis)
    pieces = [lax.dynamic_index_in_dim(blocks, me, 0, keepdims=False)]
    for step in range(1, count):
        outgoing = lax.dynamic_index_in_dim(blocks, (me + step) % count, 0, keepdims=False)
        pieces.append(lax.ppermute(outgoing, axis, shifted(count, step)))
    return by_sender(pieces, count, me)


def reduce_blocks(blocks, axis):
    count = lax.axis_size(axis)
    if count > PERMUTE_LIMIT:
        return lax.psum_scatter(blocks.astype(jnp.bfloat16), axis, scatter_dimension=0).astype(jnp.float32)
    me = lax.axis_index(axis)
    total = lax.dynamic_index_in_dim(blocks, me, 0, keepdims=False)
    for step in range(1, count):
        outgoing = lax.dynamic_index_in_dim(blocks, (me + step) % count, 0, keepdims=False)
        total = total + lax.ppermute(outgoing.astype(jnp.bfloat16), axis, shifted(count, step)).astype(jnp.float32)
    return total


def swap_halves(values, half_width, negate_first):
    low = values[:, :half_width]
    high = values[:, half_width:]
    if negate_first:
        return jnp.concatenate([-high, low], axis=1)
    return jnp.concatenate([high, -low], axis=1)


def coil_terms(image_ref, sens_ref, measured_ref, sampled_ref, forward_ref, adjoint_ref, table_ref):
    coils, height, width = sens_ref.shape
    half_width = width // 2
    sens = sens_ref[...].astype(jnp.float32)
    sens_re = sens[:, :, :half_width]
    sens_im = sens[:, :, half_width:]
    image = image_ref[...].astype(jnp.float32)[None]
    image_re = image[:, :, :half_width]
    image_im = image[:, :, half_width:]
    coil = jnp.concatenate(
        [sens_re * image_re - sens_im * image_im, sens_re * image_im + sens_im * image_re], axis=2
    ).astype(jnp.bfloat16)
    half_k = jnp.dot(coil.reshape(coils * height, width), forward_ref[...], preferred_element_type=jnp.float32)
    table = table_ref[...]
    backs = []
    for coil_index in range(coils):
        one = half_k[coil_index * height:(coil_index + 1) * height].astype(jnp.bfloat16).astype(jnp.float32)
        turned = jnp.concatenate([one[:, :half_width].T, one[:, half_width:].T], axis=0).astype(jnp.bfloat16)
        parts = jnp.dot(turned, table, preferred_element_type=jnp.float32)
        kspace_re = parts[:half_width, :height] - parts[half_width:, height:]
        kspace_im = parts[:half_width, height:] + parts[half_width:, :height]
        row = pl.program_id(0) * coils + coil_index
        sampled = sampled_ref[pl.ds(row, 1), :].astype(jnp.float32)
        measured = measured_ref[coil_index].astype(jnp.float32)
        residual = jnp.concatenate(
            [
                (sampled * (kspace_re - measured[:, :half_width].T)).astype(jnp.bfloat16),
                (sampled * (kspace_im - measured[:, half_width:].T)).astype(jnp.bfloat16),
            ],
            axis=0,
        )
        parts = jnp.dot(residual, table, preferred_element_type=jnp.float32)
        back_re = (parts[:half_width, :height] + parts[half_width:, height:]).astype(jnp.bfloat16)
        back_im = (parts[half_width:, :height] - parts[:half_width, height:]).astype(jnp.bfloat16)
        backs.append(
            jnp.concatenate([back_re.astype(jnp.float32).T, back_im.astype(jnp.float32).T], axis=1).astype(
                jnp.bfloat16
            )
        )
    back_half = jnp.concatenate(backs, axis=0)
    coil_back = jnp.dot(back_half, adjoint_ref[...], preferred_element_type=jnp.float32).reshape(
        coils, height, width
    )
    back_re = coil_back[:, :, :half_width]
    back_im = coil_back[:, :, half_width:]
    term = jnp.concatenate(
        [sens_re * back_re + sens_im * back_im, sens_re * back_im - sens_im * back_re], axis=2
    )
    return jnp.sum(term, axis=0)


def coil_chain_kernel(*refs):
    groups = (len(refs) - 8) // 2
    pieces = refs[:groups]
    place_ref, sens_ref, measured_ref, sampled_ref, forward_ref, adjoint_ref, table_ref = refs[groups:groups + 7]
    own_ref = refs[groups + 7]
    send_refs = refs[groups + 8:2 * groups + 7]
    image_ref, total_ref = refs[2 * groups + 7:]
    rows = pieces[0].shape[0]
    half_width = image_ref.shape[1] // 2
    me = place_ref[0]
    step = pl.program_id(0)

    @pl.when(step == 0)
    def _():
        for block in range(groups):
            source = (me - block + groups) % groups
            value = pieces[0][...]
            for other in range(1, groups):
                value = jnp.where(source == other, pieces[other][...], value)
            image_ref[block * rows:(block + 1) * rows, :] = value

    term = coil_terms(image_ref, sens_ref, measured_ref, sampled_ref, forward_ref, adjoint_ref, table_ref)

    @pl.when(step == 0)
    def _():
        total_ref[...] = term

    @pl.when(step > 0)
    def _():
        total_ref[...] += term

    @pl.when(step == pl.num_programs(0) - 1)
    def _():
        start = pl.multiple_of(me * rows, rows)
        own_ref[...] = total_ref[pl.ds(start, rows), :]
        for shift in range(1, groups):
            start = pl.multiple_of(((me + shift) % groups) * rows, rows)
            send_refs[shift - 1][...] = total_ref[pl.ds(start, rows), :].astype(jnp.bfloat16)


def coil_chain(pieces, place, sens, measured, sampled, forward_x, adjoint_x, table_y):
    coils, height, width = sens.shape
    groups = len(pieces)
    rows = pieces[0].shape[0]
    whole = lambda c: (0, 0)
    per_coil = lambda c: (c, 0, 0)
    step_coils = 4 if coils % 4 == 0 else (2 if coils % 2 == 0 else 1)
    flops = coils * 8 * height * width * width
    return pl.pallas_call(
        coil_chain_kernel,
        out_shape=(jax.ShapeDtypeStruct((rows, width), jnp.float32),)
        + (jax.ShapeDtypeStruct((rows, width), jnp.bfloat16),) * (groups - 1),
        grid=(coils // step_coils,),
        in_specs=[pl.BlockSpec((rows, width), whole)] * groups
        + [
            pl.BlockSpec(memory_space=pltpu.SMEM),
            pl.BlockSpec((step_coils, height, width), per_coil),
            pl.BlockSpec((step_coils, height, width), per_coil),
            pl.BlockSpec((coils, height), whole),
            pl.BlockSpec((width, width), whole),
            pl.BlockSpec((width, width), whole),
            pl.BlockSpec((height, 2 * height), whole),
        ],
        out_specs=(pl.BlockSpec((rows, width), whole),) * groups,
        scratch_shapes=[pltpu.VMEM((height, width), jnp.bfloat16), pltpu.VMEM((height, width), jnp.float32)],
        compiler_params=pltpu.CompilerParams(dimension_semantics=("arbitrary",)),
        cost_estimate=pl.CostEstimate(
            flops=flops, transcendentals=0, bytes_accessed=2 * 2 * coils * height * width + 4 * height * width
        ),
    )(*pieces, place, sens, measured, sampled, forward_x, adjoint_x, table_y)


def on_device(factors, temporal, maps, kdata, masks):
    width_x = maps.shape[2] // 2
    width_y = maps.shape[1]
    rows_own = factors.shape[2]
    table_x_re, table_x_im = dft_parts(width_x)
    table_y_re, table_y_im = dft_parts(width_y)
    forward_x = jnp.asarray(np.block([[table_x_re, table_x_im], [-table_x_im, table_x_re]]))
    adjoint_x = jnp.asarray(np.block([[table_x_re, -table_x_im], [table_x_im, table_x_re]]))
    table_y = jnp.asarray(np.concatenate([table_y_re, table_y_im], axis=1))
    time_re = temporal[0]
    time_im = temporal[1]
    sign = jnp.asarray(np.array([[1.0, -1.0], [1.0, 1.0]], np.float32))
    mixing = jnp.stack([temporal, temporal[::-1]]) * sign[:, :, None, None]
    images = jnp.sum(
        mixing[:, :, :, :, None, None] * factors[None, :, None], axis=(1, 3)
    )
    images = jnp.transpose(images, (1, 0, 2, 3)).astype(jnp.bfloat16)
    frames_here = images.shape[0]
    width_own = images.shape[3]
    pieces_x = exchange_blocks(images, "frame")
    own_rows = jnp.transpose(pieces_x, (2, 1, 0, 3)).reshape(rows_own, 2 * width_x)
    groups = lax.axis_size("coil")
    me_c = lax.axis_index("coil")
    pieces = [own_rows] + [lax.ppermute(own_rows, "coil", shifted(groups, step)) for step in range(1, groups)]
    sampled = masks[0]
    place = jnp.reshape(me_c, (1,)).astype(jnp.int32)
    measured = kdata[0]
    own_total, *outgoing = coil_chain(
        pieces, place, maps, measured, sampled, forward_x, adjoint_x, table_y
    )
    own_share = own_total
    for step in range(1, groups):
        own_share = own_share + lax.ppermute(outgoing[step - 1], "coil", shifted(groups, step)).astype(jnp.float32)
    outgoing = jnp.transpose(
        own_share.reshape(rows_own, 2, frames_here, width_own), (2, 0, 1, 3)
    ).astype(jnp.bfloat16)
    returned = exchange_blocks(outgoing, "frame").astype(jnp.float32)
    late = lax.optimization_barrier(temporal)
    weights = jnp.stack(
        [jnp.stack([late[0].T, late[1].T], axis=2), jnp.stack([-late[1].T, late[0].T], axis=2)], axis=0
    )
    gradient = None
    for frame in range(returned.shape[0]):
        for part_in in range(2):
            term = weights[:, :, frame, part_in, None, None] * returned[frame, :, part_in][None, None]
            gradient = term if gradient is None else gradient + term
    return factors - 0.5 * gradient


def solution(mesh):
    placed = (
        P("slab", None, "coil", "frame"),
        P("slab", None, None),
        P("coil", "slab", None),
        P("frame", "coil", "slab", None),
        P("frame", "coil", "slab"),
    )
    return jax.shard_map(
        on_device,
        mesh=mesh,
        in_specs=placed,
        out_specs=P("slab", None, "coil", "frame"),
        check_vma=False,
    )
```

```python
import math

import jax
import ml_dtypes
import numpy as np
import jax.numpy as jnp
from jax import lax
from jax.experimental import pallas as pl
from jax.experimental.pallas import tpu as pltpu
from jax.sharding import PartitionSpec as P


def dft_parts(length):
    index = np.arange(length, dtype=np.int64)
    phase = (index[:, None] * index[None, :]) % length
    angle = np.float32(2.0 * math.pi / length) * phase.astype(np.float32)
    scale = np.float32(1.0 / math.sqrt(length))
    real = (np.cos(angle.astype(np.float64)).astype(np.float32) * scale).astype(ml_dtypes.bfloat16)
    imag = (-np.sin(angle.astype(np.float64)).astype(np.float32) * scale).astype(ml_dtypes.bfloat16)
    return real, imag


def rotate_plus(values, half_width):
    return jnp.concatenate([-values[..., half_width:], values[..., :half_width]], axis=-1)


def rotate_minus(values, half_width):
    return jnp.concatenate([values[..., half_width:], -values[..., :half_width]], axis=-1)


def sens_times(sens, values, half_width):
    sens_re = sens[..., :half_width].astype(jnp.float32)
    sens_im = sens[..., half_width:].astype(jnp.float32)
    value_re = values[..., :half_width].astype(jnp.float32)
    value_im = values[..., half_width:].astype(jnp.float32)
    return jnp.concatenate(
        [sens_re * value_re - sens_im * value_im, sens_re * value_im + sens_im * value_re], axis=-1
    )


def conj_sens_times(sens, values, half_width):
    sens_re = sens[..., :half_width].astype(jnp.float32)
    sens_im = sens[..., half_width:].astype(jnp.float32)
    value_re = values[..., :half_width]
    value_im = values[..., half_width:]
    return jnp.concatenate(
        [sens_re * value_re + sens_im * value_im, sens_re * value_im - sens_im * value_re], axis=-1
    )


def precise(form, first, second):
    return jnp.einsum(form, first, second, precision=lax.Precision.HIGHEST)


PERMUTE_LIMIT = 8


def shifted(count, step):
    return [(source, (source + step) % count) for source in range(count)]


def by_sender(pieces, count, me):
    ring = jnp.stack([pieces[0]] + pieces[1:][::-1])
    doubled = jnp.concatenate([ring, ring], axis=0)
    return lax.dynamic_slice_in_dim(doubled, (count - me) % count, count, 0)


def gather_blocks(value, axis):
    count = lax.axis_size(axis)
    if count > PERMUTE_LIMIT:
        return lax.all_gather(value, axis)
    me = lax.axis_index(axis)
    pieces = [value] + [lax.ppermute(value, axis, shifted(count, step)) for step in range(1, count)]
    return by_sender(pieces, count, me)


def exchange_blocks(blocks, axis):
    count = lax.axis_size(axis)
    if count > PERMUTE_LIMIT:
        return lax.all_to_all(blocks, axis, 0, 0, tiled=True)
    me = lax.axis_index(axis)
    pieces = [lax.dynamic_index_in_dim(blocks, me, 0, keepdims=False)]
    for step in range(1, count):
        outgoing = lax.dynamic_index_in_dim(blocks, (me + step) % count, 0, keepdims=False)
        pieces.append(lax.ppermute(outgoing, axis, shifted(count, step)))
    return by_sender(pieces, count, me)


def reduce_blocks(blocks, axis):
    count = lax.axis_size(axis)
    if count > PERMUTE_LIMIT:
        return lax.psum_scatter(blocks.astype(jnp.bfloat16), axis, scatter_dimension=0).astype(jnp.float32)
    me = lax.axis_index(axis)
    total = lax.dynamic_index_in_dim(blocks, me, 0, keepdims=False)
    for step in range(1, count):
        outgoing = lax.dynamic_index_in_dim(blocks, (me + step) % count, 0, keepdims=False)
        total = total + lax.ppermute(outgoing.astype(jnp.bfloat16), axis, shifted(count, step)).astype(jnp.float32)
    return total


def swap_halves(values, half_width, negate_first):
    low = values[:, :half_width]
    high = values[:, half_width:]
    if negate_first:
        return jnp.concatenate([-high, low], axis=1)
    return jnp.concatenate([high, -low], axis=1)


def coil_terms(image_ref, sens_ref, measured_ref, sampled_ref, forward_ref, adjoint_ref, table_ref):
    coils, height, width = sens_ref.shape
    half_width = width // 2
    sens = sens_ref[...].astype(jnp.float32)
    sens_re = sens[:, :, :half_width]
    sens_im = sens[:, :, half_width:]
    image = image_ref[...].astype(jnp.float32)[None]
    image_re = image[:, :, :half_width]
    image_im = image[:, :, half_width:]
    coil = jnp.concatenate(
        [sens_re * image_re - sens_im * image_im, sens_re * image_im + sens_im * image_re], axis=2
    ).astype(jnp.bfloat16)
    half_k = jnp.dot(coil.reshape(coils * height, width), forward_ref[...], preferred_element_type=jnp.float32)
    table = table_ref[...]
    turned = []
    for coil_index in range(coils):
        one = half_k[coil_index * height:(coil_index + 1) * height].astype(jnp.bfloat16).astype(jnp.float32)
        turned.append(jnp.concatenate([one[:, :half_width].T, one[:, half_width:].T], axis=0).astype(jnp.bfloat16))
    all_parts = jnp.dot(jnp.concatenate(turned, axis=0), table, preferred_element_type=jnp.float32)
    residuals = []
    for coil_index in range(coils):
        parts = all_parts[coil_index * width:(coil_index + 1) * width]
        kspace_re = parts[:half_width, :height] - parts[half_width:, height:]
        kspace_im = parts[:half_width, height:] + parts[half_width:, :height]
        row = pl.program_id(0) * coils + coil_index
        sampled = sampled_ref[pl.ds(row, 1), :].astype(jnp.float32)
        measured = measured_ref[coil_index].astype(jnp.float32)
        residuals.append(
            jnp.concatenate(
                [
                    (sampled * (kspace_re - measured[:, :half_width].T)).astype(jnp.bfloat16),
                    (sampled * (kspace_im - measured[:, half_width:].T)).astype(jnp.bfloat16),
                ],
                axis=0,
            )
        )
    all_parts = jnp.dot(jnp.concatenate(residuals, axis=0), table, preferred_element_type=jnp.float32)
    backs = []
    for coil_index in range(coils):
        parts = all_parts[coil_index * width:(coil_index + 1) * width]
        back_re = (parts[:half_width, :height] + parts[half_width:, height:]).astype(jnp.bfloat16)
        back_im = (parts[half_width:, :height] - parts[:half_width, height:]).astype(jnp.bfloat16)
        backs.append(
            jnp.concatenate([back_re.astype(jnp.float32).T, back_im.astype(jnp.float32).T], axis=1).astype(
                jnp.bfloat16
            )
        )
    back_half = jnp.concatenate(backs, axis=0)
    coil_back = jnp.dot(back_half, adjoint_ref[...], preferred_element_type=jnp.float32).reshape(
        coils, height, width
    )
    back_re = coil_back[:, :, :half_width]
    back_im = coil_back[:, :, half_width:]
    term = jnp.concatenate(
        [sens_re * back_re + sens_im * back_im, sens_re * back_im - sens_im * back_re], axis=2
    )
    return jnp.sum(term, axis=0)


def coil_chain_kernel(*refs):
    groups = (len(refs) - 8) // 2
    pieces = refs[:groups]
    place_ref, sens_ref, measured_ref, sampled_ref, forward_ref, adjoint_ref, table_ref = refs[groups:groups + 7]
    own_ref = refs[groups + 7]
    send_refs = refs[groups + 8:2 * groups + 7]
    image_ref, total_ref = refs[2 * groups + 7:]
    rows = pieces[0].shape[0]
    half_width = image_ref.shape[1] // 2
    me = place_ref[0]
    step = pl.program_id(0)

    @pl.when(step == 0)
    def _():
        for block in range(groups):
            source = (me - block + groups) % groups
            value = pieces[0][...]
            for other in range(1, groups):
                value = jnp.where(source == other, pieces[other][...], value)
            image_ref[block * rows:(block + 1) * rows, :] = value

    term = coil_terms(image_ref, sens_ref, measured_ref, sampled_ref, forward_ref, adjoint_ref, table_ref)

    @pl.when(step == 0)
    def _():
        total_ref[...] = term

    @pl.when(step > 0)
    def _():
        total_ref[...] += term

    @pl.when(step == pl.num_programs(0) - 1)
    def _():
        start = pl.multiple_of(me * rows, rows)
        own_ref[...] = total_ref[pl.ds(start, rows), :]
        for shift in range(1, groups):
            start = pl.multiple_of(((me + shift) % groups) * rows, rows)
            send_refs[shift - 1][...] = total_ref[pl.ds(start, rows), :].astype(jnp.bfloat16)


def coil_chain(pieces, place, sens, measured, sampled, forward_x, adjoint_x, table_y):
    coils, height, width = sens.shape
    groups = len(pieces)
    rows = pieces[0].shape[0]
    whole = lambda c: (0, 0)
    per_coil = lambda c: (c, 0, 0)
    step_coils = 4 if coils % 4 == 0 else (2 if coils % 2 == 0 else 1)
    flops = coils * 8 * height * width * width
    return pl.pallas_call(
        coil_chain_kernel,
        out_shape=(jax.ShapeDtypeStruct((rows, width), jnp.float32),)
        + (jax.ShapeDtypeStruct((rows, width), jnp.bfloat16),) * (groups - 1),
        grid=(coils // step_coils,),
        in_specs=[pl.BlockSpec((rows, width), whole)] * groups
        + [
            pl.BlockSpec(memory_space=pltpu.SMEM),
            pl.BlockSpec((step_coils, height, width), per_coil),
            pl.BlockSpec((step_coils, height, width), per_coil),
            pl.BlockSpec((coils, height), whole),
            pl.BlockSpec((width, width), whole),
            pl.BlockSpec((width, width), whole),
            pl.BlockSpec((height, 2 * height), whole),
        ],
        out_specs=(pl.BlockSpec((rows, width), whole),) * groups,
        scratch_shapes=[pltpu.VMEM((height, width), jnp.bfloat16), pltpu.VMEM((height, width), jnp.float32)],
        compiler_params=pltpu.CompilerParams(dimension_semantics=("arbitrary",)),
        cost_estimate=pl.CostEstimate(
            flops=flops, transcendentals=0, bytes_accessed=2 * 2 * coils * height * width + 4 * height * width
        ),
    )(*pieces, place, sens, measured, sampled, forward_x, adjoint_x, table_y)


def on_device(factors, temporal, maps, kdata, masks):
    width_x = maps.shape[2] // 2
    width_y = maps.shape[1]
    rows_own = factors.shape[2]
    table_x_re, table_x_im = dft_parts(width_x)
    table_y_re, table_y_im = dft_parts(width_y)
    forward_x = jnp.asarray(np.block([[table_x_re, table_x_im], [-table_x_im, table_x_re]]))
    adjoint_x = jnp.asarray(np.block([[table_x_re, -table_x_im], [table_x_im, table_x_re]]))
    table_y = jnp.asarray(np.concatenate([table_y_re, table_y_im], axis=1))
    time_re = temporal[0]
    time_im = temporal[1]
    sign = jnp.asarray(np.array([[1.0, -1.0], [1.0, 1.0]], np.float32))
    mixing = jnp.stack([temporal, temporal[::-1]]) * sign[:, :, None, None]
    images = jnp.sum(
        mixing[:, :, :, :, None, None] * factors[None, :, None], axis=(1, 3)
    )
    images = jnp.transpose(images, (1, 0, 2, 3)).astype(jnp.bfloat16)
    frames_here = images.shape[0]
    width_own = images.shape[3]
    pieces_x = exchange_blocks(images, "frame")
    own_rows = jnp.transpose(pieces_x, (2, 1, 0, 3)).reshape(rows_own, 2 * width_x)
    groups = lax.axis_size("coil")
    me_c = lax.axis_index("coil")
    pieces = [own_rows] + [lax.ppermute(own_rows, "coil", shifted(groups, step)) for step in range(1, groups)]
    sampled = masks[0]
    place = jnp.reshape(me_c, (1,)).astype(jnp.int32)
    measured = kdata[0]
    own_total, *outgoing = coil_chain(
        pieces, place, maps, measured, sampled, forward_x, adjoint_x, table_y
    )
    own_share = own_total
    for step in range(1, groups):
        own_share = own_share + lax.ppermute(outgoing[step - 1], "coil", shifted(groups, step)).astype(jnp.float32)
    outgoing = jnp.transpose(
        own_share.reshape(rows_own, 2, frames_here, width_own), (2, 0, 1, 3)
    ).astype(jnp.bfloat16)
    returned = exchange_blocks(outgoing, "frame").astype(jnp.float32)
    late = lax.optimization_barrier(temporal)
    weights = jnp.stack(
        [jnp.stack([late[0].T, late[1].T], axis=2), jnp.stack([-late[1].T, late[0].T], axis=2)], axis=0
    )
    gradient = None
    for frame in range(returned.shape[0]):
        for part_in in range(2):
            term = weights[:, :, frame, part_in, None, None] * returned[frame, :, part_in][None, None]
            gradient = term if gradient is None else gradient + term
    return factors - 0.5 * gradient


def solution(mesh):
    placed = (
        P("slab", None, "coil", "frame"),
        P("slab", None, None),
        P("coil", "slab", None),
        P("frame", "coil", "slab", None),
        P("frame", "coil", "slab"),
    )
    return jax.shard_map(
        on_device,
        mesh=mesh,
        in_specs=placed,
        out_specs=P("slab", None, "coil", "frame"),
        check_vma=False,
    )
```

```python
import math

import jax
import ml_dtypes
import numpy as np
import jax.numpy as jnp
from jax import lax
from jax.experimental import pallas as pl
from jax.experimental.pallas import tpu as pltpu
from jax.sharding import PartitionSpec as P


def dft_parts(length):
    index = np.arange(length, dtype=np.int64)
    phase = (index[:, None] * index[None, :]) % length
    angle = np.float32(2.0 * math.pi / length) * phase.astype(np.float32)
    scale = np.float32(1.0 / math.sqrt(length))
    real = (np.cos(angle.astype(np.float64)).astype(np.float32) * scale).astype(ml_dtypes.bfloat16)
    imag = (-np.sin(angle.astype(np.float64)).astype(np.float32) * scale).astype(ml_dtypes.bfloat16)
    return real, imag


def rotate_plus(values, half_width):
    return jnp.concatenate([-values[..., half_width:], values[..., :half_width]], axis=-1)


def rotate_minus(values, half_width):
    return jnp.concatenate([values[..., half_width:], -values[..., :half_width]], axis=-1)


def sens_times(sens, values, half_width):
    sens_re = sens[..., :half_width].astype(jnp.float32)
    sens_im = sens[..., half_width:].astype(jnp.float32)
    value_re = values[..., :half_width].astype(jnp.float32)
    value_im = values[..., half_width:].astype(jnp.float32)
    return jnp.concatenate(
        [sens_re * value_re - sens_im * value_im, sens_re * value_im + sens_im * value_re], axis=-1
    )


def conj_sens_times(sens, values, half_width):
    sens_re = sens[..., :half_width].astype(jnp.float32)
    sens_im = sens[..., half_width:].astype(jnp.float32)
    value_re = values[..., :half_width]
    value_im = values[..., half_width:]
    return jnp.concatenate(
        [sens_re * value_re + sens_im * value_im, sens_re * value_im - sens_im * value_re], axis=-1
    )


def precise(form, first, second):
    return jnp.einsum(form, first, second, precision=lax.Precision.HIGHEST)


PERMUTE_LIMIT = 8


def shifted(count, step):
    return [(source, (source + step) % count) for source in range(count)]


def by_sender(pieces, count, me):
    ring = jnp.stack([pieces[0]] + pieces[1:][::-1])
    doubled = jnp.concatenate([ring, ring], axis=0)
    return lax.dynamic_slice_in_dim(doubled, (count - me) % count, count, 0)


def gather_blocks(value, axis):
    count = lax.axis_size(axis)
    if count > PERMUTE_LIMIT:
        return lax.all_gather(value, axis)
    me = lax.axis_index(axis)
    pieces = [value] + [lax.ppermute(value, axis, shifted(count, step)) for step in range(1, count)]
    return by_sender(pieces, count, me)


def exchange_blocks(blocks, axis):
    count = lax.axis_size(axis)
    if count > PERMUTE_LIMIT:
        return lax.all_to_all(blocks, axis, 0, 0, tiled=True)
    me = lax.axis_index(axis)
    pieces = [lax.dynamic_index_in_dim(blocks, me, 0, keepdims=False)]
    for step in range(1, count):
        outgoing = lax.dynamic_index_in_dim(blocks, (me + step) % count, 0, keepdims=False)
        pieces.append(lax.ppermute(outgoing, axis, shifted(count, step)))
    return by_sender(pieces, count, me)


def reduce_blocks(blocks, axis):
    count = lax.axis_size(axis)
    if count > PERMUTE_LIMIT:
        return lax.psum_scatter(blocks.astype(jnp.bfloat16), axis, scatter_dimension=0).astype(jnp.float32)
    me = lax.axis_index(axis)
    total = lax.dynamic_index_in_dim(blocks, me, 0, keepdims=False)
    for step in range(1, count):
        outgoing = lax.dynamic_index_in_dim(blocks, (me + step) % count, 0, keepdims=False)
        total = total + lax.ppermute(outgoing.astype(jnp.bfloat16), axis, shifted(count, step)).astype(jnp.float32)
    return total


def swap_halves(values, half_width, negate_first):
    low = values[:, :half_width]
    high = values[:, half_width:]
    if negate_first:
        return jnp.concatenate([-high, low], axis=1)
    return jnp.concatenate([high, -low], axis=1)


def coil_terms(image_ref, sens_ref, measured_ref, sampled_ref, forward_ref, adjoint_ref, table_ref):
    coils, height, width = sens_ref.shape
    half_width = width // 2
    sens = sens_ref[...].astype(jnp.float32)
    sens_re = sens[:, :, :half_width]
    sens_im = sens[:, :, half_width:]
    image = image_ref[...].astype(jnp.float32)[None]
    image_re = image[:, :, :half_width]
    image_im = image[:, :, half_width:]
    coil = jnp.concatenate(
        [sens_re * image_re - sens_im * image_im, sens_re * image_im + sens_im * image_re], axis=2
    ).astype(jnp.bfloat16)
    half_k = jnp.dot(coil.reshape(coils * height, width), forward_ref[...], preferred_element_type=jnp.float32)
    table = table_ref[...]
    backs = []
    for coil_index in range(coils):
        one = half_k[coil_index * height:(coil_index + 1) * height].astype(jnp.bfloat16).astype(jnp.float32)
        turned = jnp.concatenate([one[:, :half_width].T, one[:, half_width:].T], axis=0).astype(jnp.bfloat16)
        parts = jnp.dot(turned, table, preferred_element_type=jnp.float32)
        kspace_re = parts[:half_width, :height] - parts[half_width:, height:]
        kspace_im = parts[:half_width, height:] + parts[half_width:, :height]
        row = pl.program_id(0) * coils + coil_index
        sampled = sampled_ref[pl.ds(row, 1), :].astype(jnp.float32)
        measured = measured_ref[coil_index].astype(jnp.float32)
        residual = jnp.concatenate(
            [
                (sampled * (kspace_re - measured[:, :half_width].T)).astype(jnp.bfloat16),
                (sampled * (kspace_im - measured[:, half_width:].T)).astype(jnp.bfloat16),
            ],
            axis=0,
        )
        parts = jnp.dot(residual, table, preferred_element_type=jnp.float32)
        back_re = (parts[:half_width, :height] + parts[half_width:, height:]).astype(jnp.bfloat16)
        back_im = (parts[half_width:, :height] - parts[:half_width, height:]).astype(jnp.bfloat16)
        backs.append(
            jnp.concatenate([back_re.astype(jnp.float32).T, back_im.astype(jnp.float32).T], axis=1).astype(
                jnp.bfloat16
            )
        )
    back_half = jnp.concatenate(backs, axis=0)
    coil_back = jnp.dot(back_half, adjoint_ref[...], preferred_element_type=jnp.float32).reshape(
        coils, height, width
    )
    back_re = coil_back[:, :, :half_width]
    back_im = coil_back[:, :, half_width:]
    term = jnp.concatenate(
        [sens_re * back_re + sens_im * back_im, sens_re * back_im - sens_im * back_re], axis=2
    )
    return jnp.sum(term, axis=0)


def coil_chain_kernel(*refs):
    groups = (len(refs) - 8) // 2
    pieces = refs[:groups]
    place_ref, sens_ref, measured_ref, sampled_ref, forward_ref, adjoint_ref, table_ref = refs[groups:groups + 7]
    own_ref = refs[groups + 7]
    send_refs = refs[groups + 8:2 * groups + 7]
    image_ref, total_ref = refs[2 * groups + 7:]
    rows = pieces[0].shape[0]
    half_width = image_ref.shape[1] // 2
    me = place_ref[0]
    step = pl.program_id(0)

    @pl.when(step == 0)
    def _():
        for block in range(groups):
            source = (me - block + groups) % groups
            value = pieces[0][...]
            for other in range(1, groups):
                value = jnp.where(source == other, pieces[other][...], value)
            image_ref[block * rows:(block + 1) * rows, :] = value

    term = coil_terms(image_ref, sens_ref, measured_ref, sampled_ref, forward_ref, adjoint_ref, table_ref)

    @pl.when(step == 0)
    def _():
        total_ref[...] = term

    @pl.when(step > 0)
    def _():
        total_ref[...] += term

    @pl.when(step == pl.num_programs(0) - 1)
    def _():
        start = pl.multiple_of(me * rows, rows)
        own_ref[...] = total_ref[pl.ds(start, rows), :]
        for shift in range(1, groups):
            start = pl.multiple_of(((me + shift) % groups) * rows, rows)
            send_refs[shift - 1][...] = total_ref[pl.ds(start, rows), :].astype(jnp.bfloat16)


def coil_chain(pieces, place, sens, measured, sampled, forward_x, adjoint_x, table_y):
    coils, height, width = sens.shape
    groups = len(pieces)
    rows = pieces[0].shape[0]
    whole = lambda c: (0, 0)
    per_coil = lambda c: (c, 0, 0)
    step_coils = 2 if coils % 2 == 0 else 1
    flops = coils * 8 * height * width * width
    return pl.pallas_call(
        coil_chain_kernel,
        out_shape=(jax.ShapeDtypeStruct((rows, width), jnp.float32),)
        + (jax.ShapeDtypeStruct((rows, width), jnp.bfloat16),) * (groups - 1),
        grid=(coils // step_coils,),
        in_specs=[pl.BlockSpec((rows, width), whole)] * groups
        + [
            pl.BlockSpec(memory_space=pltpu.SMEM),
            pl.BlockSpec((step_coils, height, width), per_coil),
            pl.BlockSpec((step_coils, height, width), per_coil),
            pl.BlockSpec((coils, height), whole),
            pl.BlockSpec((width, width), whole),
            pl.BlockSpec((width, width), whole),
            pl.BlockSpec((height, 2 * height), whole),
        ],
        out_specs=(pl.BlockSpec((rows, width), whole),) * groups,
        scratch_shapes=[pltpu.VMEM((height, width), jnp.bfloat16), pltpu.VMEM((height, width), jnp.float32)],
        compiler_params=pltpu.CompilerParams(dimension_semantics=("arbitrary",)),
        cost_estimate=pl.CostEstimate(
            flops=flops, transcendentals=0, bytes_accessed=2 * 2 * coils * height * width + 4 * height * width
        ),
    )(*pieces, place, sens, measured, sampled, forward_x, adjoint_x, table_y)


def on_device(factors, temporal, maps, kdata, masks):
    width_x = maps.shape[2] // 2
    width_y = maps.shape[1]
    rows_own = factors.shape[2]
    table_x_re, table_x_im = dft_parts(width_x)
    table_y_re, table_y_im = dft_parts(width_y)
    forward_x = jnp.asarray(np.block([[table_x_re, table_x_im], [-table_x_im, table_x_re]]))
    adjoint_x = jnp.asarray(np.block([[table_x_re, -table_x_im], [table_x_im, table_x_re]]))
    table_y = jnp.asarray(np.concatenate([table_y_re, table_y_im], axis=1))
    time_re = temporal[0]
    time_im = temporal[1]
    sign = jnp.asarray(np.array([[1.0, -1.0], [1.0, 1.0]], np.float32))
    mixing = jnp.stack([temporal, temporal[::-1]]) * sign[:, :, None, None]
    images = jnp.sum(
        mixing[:, :, :, :, None, None] * factors[None, :, None], axis=(1, 3)
    )
    images = jnp.transpose(images, (1, 0, 2, 3)).astype(jnp.bfloat16)
    frames_here = images.shape[0]
    width_own = images.shape[3]
    pieces_x = exchange_blocks(images, "frame")
    own_rows = jnp.transpose(pieces_x, (2, 1, 0, 3)).reshape(rows_own, 2 * width_x)
    groups = lax.axis_size("coil")
    me_c = lax.axis_index("coil")
    pieces = [own_rows] + [lax.ppermute(own_rows, "coil", shifted(groups, step)) for step in range(1, groups)]
    sampled = masks[0]
    place = jnp.reshape(me_c, (1,)).astype(jnp.int32)
    measured = kdata[0]
    own_total, *outgoing = coil_chain(
        pieces, place, maps, measured, sampled, forward_x, adjoint_x, table_y
    )
    own_share = own_total
    for step in range(1, groups):
        own_share = own_share + lax.ppermute(outgoing[step - 1], "coil", shifted(groups, step)).astype(jnp.float32)
    outgoing = jnp.transpose(
        own_share.reshape(rows_own, 2, frames_here, width_own), (2, 0, 1, 3)
    ).astype(jnp.bfloat16)
    returned = exchange_blocks(outgoing, "frame").astype(jnp.float32)
    late = lax.optimization_barrier(temporal)
    weights = jnp.stack(
        [jnp.stack([late[0].T, late[1].T], axis=2), jnp.stack([-late[1].T, late[0].T], axis=2)], axis=0
    )
    gradient = None
    for frame in range(returned.shape[0]):
        for part_in in range(2):
            term = weights[:, :, frame, part_in, None, None] * returned[frame, :, part_in][None, None]
            gradient = term if gradient is None else gradient + term
    return factors - 0.5 * gradient


def solution(mesh):
    placed = (
        P("slab", None, "coil", "frame"),
        P("slab", None, None),
        P("coil", "slab", None),
        P("frame", "coil", "slab", None),
        P("frame", "coil", "slab"),
    )
    return jax.shard_map(
        on_device,
        mesh=mesh,
        in_specs=placed,
        out_specs=P("slab", None, "coil", "frame"),
        check_vma=False,
    )
```

```python
import math

import jax
import ml_dtypes
import numpy as np
import jax.numpy as jnp
from jax import lax
from jax.experimental import pallas as pl
from jax.experimental.pallas import tpu as pltpu
from jax.sharding import PartitionSpec as P


def dft_parts(length):
    index = np.arange(length, dtype=np.int64)
    phase = (index[:, None] * index[None, :]) % length
    angle = np.float32(2.0 * math.pi / length) * phase.astype(np.float32)
    scale = np.float32(1.0 / math.sqrt(length))
    real = (np.cos(angle.astype(np.float64)).astype(np.float32) * scale).astype(ml_dtypes.bfloat16)
    imag = (-np.sin(angle.astype(np.float64)).astype(np.float32) * scale).astype(ml_dtypes.bfloat16)
    return real, imag


def rotate_plus(values, half_width):
    return jnp.concatenate([-values[..., half_width:], values[..., :half_width]], axis=-1)


def rotate_minus(values, half_width):
    return jnp.concatenate([values[..., half_width:], -values[..., :half_width]], axis=-1)


def sens_times(sens, values, half_width):
    sens_re = sens[..., :half_width].astype(jnp.float32)
    sens_im = sens[..., half_width:].astype(jnp.float32)
    value_re = values[..., :half_width].astype(jnp.float32)
    value_im = values[..., half_width:].astype(jnp.float32)
    return jnp.concatenate(
        [sens_re * value_re - sens_im * value_im, sens_re * value_im + sens_im * value_re], axis=-1
    )


def conj_sens_times(sens, values, half_width):
    sens_re = sens[..., :half_width].astype(jnp.float32)
    sens_im = sens[..., half_width:].astype(jnp.float32)
    value_re = values[..., :half_width]
    value_im = values[..., half_width:]
    return jnp.concatenate(
        [sens_re * value_re + sens_im * value_im, sens_re * value_im - sens_im * value_re], axis=-1
    )


def precise(form, first, second):
    return jnp.einsum(form, first, second, precision=lax.Precision.HIGHEST)


PERMUTE_LIMIT = 8


def shifted(count, step):
    return [(source, (source + step) % count) for source in range(count)]


def by_sender(pieces, count, me):
    ring = jnp.stack([pieces[0]] + pieces[1:][::-1])
    doubled = jnp.concatenate([ring, ring], axis=0)
    return lax.dynamic_slice_in_dim(doubled, (count - me) % count, count, 0)


def gather_blocks(value, axis):
    count = lax.axis_size(axis)
    if count > PERMUTE_LIMIT:
        return lax.all_gather(value, axis)
    me = lax.axis_index(axis)
    pieces = [value] + [lax.ppermute(value, axis, shifted(count, step)) for step in range(1, count)]
    return by_sender(pieces, count, me)


def exchange_blocks(blocks, axis):
    count = lax.axis_size(axis)
    if count > PERMUTE_LIMIT:
        return lax.all_to_all(blocks, axis, 0, 0, tiled=True)
    me = lax.axis_index(axis)
    pieces = [lax.dynamic_index_in_dim(blocks, me, 0, keepdims=False)]
    for step in range(1, count):
        outgoing = lax.dynamic_index_in_dim(blocks, (me + step) % count, 0, keepdims=False)
        pieces.append(lax.ppermute(outgoing, axis, shifted(count, step)))
    return by_sender(pieces, count, me)


def reduce_blocks(blocks, axis):
    count = lax.axis_size(axis)
    if count > PERMUTE_LIMIT:
        return lax.psum_scatter(blocks.astype(jnp.bfloat16), axis, scatter_dimension=0).astype(jnp.float32)
    me = lax.axis_index(axis)
    total = lax.dynamic_index_in_dim(blocks, me, 0, keepdims=False)
    for step in range(1, count):
        outgoing = lax.dynamic_index_in_dim(blocks, (me + step) % count, 0, keepdims=False)
        total = total + lax.ppermute(outgoing.astype(jnp.bfloat16), axis, shifted(count, step)).astype(jnp.float32)
    return total


def swap_halves(values, half_width, negate_first):
    low = values[:, :half_width]
    high = values[:, half_width:]
    if negate_first:
        return jnp.concatenate([-high, low], axis=1)
    return jnp.concatenate([high, -low], axis=1)


def coil_terms(image_ref, sens_ref, measured_ref, sampled_ref, forward_ref, adjoint_ref, table_ref):
    coils, height, width = sens_ref.shape
    half_width = width // 2
    sens = sens_ref[...].astype(jnp.float32)
    sens_re = sens[:, :, :half_width]
    sens_im = sens[:, :, half_width:]
    image = image_ref[...].astype(jnp.float32)[None]
    image_re = image[:, :, :half_width]
    image_im = image[:, :, half_width:]
    coil = jnp.concatenate(
        [sens_re * image_re - sens_im * image_im, sens_re * image_im + sens_im * image_re], axis=2
    ).astype(jnp.bfloat16)
    half_k = jnp.dot(coil.reshape(coils * height, width), forward_ref[...], preferred_element_type=jnp.float32)
    table = table_ref[...]
    backs = []
    for coil_index in range(coils):
        one = half_k[coil_index * height:(coil_index + 1) * height].astype(jnp.bfloat16).astype(jnp.float32)
        turned = jnp.concatenate([one[:, :half_width].T, one[:, half_width:].T], axis=0).astype(jnp.bfloat16)
        parts = jnp.dot(turned, table, preferred_element_type=jnp.float32)
        kspace_re = parts[:half_width, :height] - parts[half_width:, height:]
        kspace_im = parts[:half_width, height:] + parts[half_width:, :height]
        row = pl.program_id(0) * coils + coil_index
        sampled = sampled_ref[pl.ds(row, 1), :].astype(jnp.float32)
        measured = measured_ref[coil_index].astype(jnp.float32)
        residual = jnp.concatenate(
            [
                (sampled * (kspace_re - measured[:, :half_width].T)).astype(jnp.bfloat16),
                (sampled * (kspace_im - measured[:, half_width:].T)).astype(jnp.bfloat16),
            ],
            axis=0,
        )
        parts = jnp.dot(residual, table, preferred_element_type=jnp.float32)
        back_re = (parts[:half_width, :height] + parts[half_width:, height:]).astype(jnp.bfloat16)
        back_im = (parts[half_width:, :height] - parts[:half_width, height:]).astype(jnp.bfloat16)
        backs.append(
            jnp.concatenate([back_re.astype(jnp.float32).T, back_im.astype(jnp.float32).T], axis=1).astype(
                jnp.bfloat16
            )
        )
    back_half = jnp.concatenate(backs, axis=0)
    coil_back = jnp.dot(back_half, adjoint_ref[...], preferred_element_type=jnp.float32).reshape(
        coils, height, width
    )
    back_re = coil_back[:, :, :half_width]
    back_im = coil_back[:, :, half_width:]
    term = jnp.concatenate(
        [sens_re * back_re + sens_im * back_im, sens_re * back_im - sens_im * back_re], axis=2
    )
    return jnp.sum(term, axis=0)


def coil_chain_kernel(*refs):
    groups = (len(refs) - 8) // 2
    pieces = refs[:groups]
    place_ref, sens_ref, measured_ref, sampled_ref, forward_ref, adjoint_ref, table_ref = refs[groups:groups + 7]
    own_ref = refs[groups + 7]
    send_refs = refs[groups + 8:2 * groups + 7]
    image_ref, total_ref = refs[2 * groups + 7:]
    rows = pieces[0].shape[0]
    half_width = image_ref.shape[1] // 2
    me = place_ref[0]
    step = pl.program_id(0)

    @pl.when(step == 0)
    def _():
        for block in range(groups):
            source = (me - block + groups) % groups
            value = pieces[0][...]
            for other in range(1, groups):
                value = jnp.where(source == other, pieces[other][...], value)
            image_ref[block * rows:(block + 1) * rows, :] = value

    term = coil_terms(image_ref, sens_ref, measured_ref, sampled_ref, forward_ref, adjoint_ref, table_ref)

    @pl.when(step == 0)
    def _():
        total_ref[...] = term

    @pl.when(step > 0)
    def _():
        total_ref[...] += term

    @pl.when(step == pl.num_programs(0) - 1)
    def _():
        start = pl.multiple_of(me * rows, rows)
        own_ref[...] = total_ref[pl.ds(start, rows), :]
        for shift in range(1, groups):
            start = pl.multiple_of(((me + shift) % groups) * rows, rows)
            send_refs[shift - 1][...] = total_ref[pl.ds(start, rows), :].astype(jnp.bfloat16)


def coil_chain(pieces, place, sens, measured, sampled, forward_x, adjoint_x, table_y):
    coils, height, width = sens.shape
    groups = len(pieces)
    rows = pieces[0].shape[0]
    whole = lambda c: (0, 0)
    per_coil = lambda c: (c, 0, 0)
    step_coils = 4 if coils % 4 == 0 else (2 if coils % 2 == 0 else 1)
    flops = coils * 8 * height * width * width
    return pl.pallas_call(
        coil_chain_kernel,
        out_shape=(jax.ShapeDtypeStruct((rows, width), jnp.float32),)
        + (jax.ShapeDtypeStruct((rows, width), jnp.bfloat16),) * (groups - 1),
        grid=(coils // step_coils,),
        in_specs=[pl.BlockSpec((rows, width), whole)] * groups
        + [
            pl.BlockSpec(memory_space=pltpu.SMEM),
            pl.BlockSpec((step_coils, height, width), per_coil),
            pl.BlockSpec((step_coils, height, width), per_coil),
            pl.BlockSpec((coils, height), whole),
            pl.BlockSpec((width, width), whole),
            pl.BlockSpec((width, width), whole),
            pl.BlockSpec((height, 2 * height), whole),
        ],
        out_specs=(pl.BlockSpec((rows, width), whole),) * groups,
        scratch_shapes=[pltpu.VMEM((height, width), jnp.bfloat16), pltpu.VMEM((height, width), jnp.float32)],
        compiler_params=pltpu.CompilerParams(dimension_semantics=("arbitrary",)),
        cost_estimate=pl.CostEstimate(
            flops=flops, transcendentals=0, bytes_accessed=2 * 2 * coils * height * width + 4 * height * width
        ),
    )(*pieces, place, sens, measured, sampled, forward_x, adjoint_x, table_y)


def on_device(factors, temporal, maps, kdata, masks):
    width_x = maps.shape[2] // 2
    width_y = maps.shape[1]
    rows_own = factors.shape[2]
    table_x_re, table_x_im = dft_parts(width_x)
    table_y_re, table_y_im = dft_parts(width_y)
    forward_x = jnp.asarray(np.block([[table_x_re, table_x_im], [-table_x_im, table_x_re]]))
    adjoint_x = jnp.asarray(np.block([[table_x_re, -table_x_im], [table_x_im, table_x_re]]))
    table_y = jnp.asarray(np.concatenate([table_y_re, table_y_im], axis=1))
    time_re = temporal[0]
    time_im = temporal[1]
    sign = jnp.asarray(np.array([[1.0, -1.0], [1.0, 1.0]], np.float32))
    mixing = jnp.stack([temporal, temporal[::-1]]) * sign[:, :, None, None]
    images = jnp.sum(
        mixing[:, :, :, :, None, None] * factors[None, :, None], axis=(1, 3)
    )
    images = jnp.transpose(images, (1, 0, 2, 3)).astype(jnp.bfloat16)
    frames_here = images.shape[0]
    width_own = images.shape[3]
    pieces_x = lax.all_to_all(images, "frame", 0, 0, tiled=True)
    own_rows = jnp.transpose(pieces_x, (2, 1, 0, 3)).reshape(rows_own, 2 * width_x)
    groups = lax.axis_size("coil")
    me_c = lax.axis_index("coil")
    pieces = [own_rows] + [lax.ppermute(own_rows, "coil", shifted(groups, step)) for step in range(1, groups)]
    sampled = masks[0]
    place = jnp.reshape(me_c, (1,)).astype(jnp.int32)
    measured = kdata[0]
    own_total, *outgoing = coil_chain(
        pieces, place, maps, measured, sampled, forward_x, adjoint_x, table_y
    )
    own_share = own_total
    for step in range(1, groups):
        own_share = own_share + lax.ppermute(outgoing[step - 1], "coil", shifted(groups, step)).astype(jnp.float32)
    outgoing = jnp.transpose(
        own_share.reshape(rows_own, 2, frames_here, width_own), (2, 0, 1, 3)
    ).astype(jnp.bfloat16)
    returned = exchange_blocks(outgoing, "frame").astype(jnp.float32)
    late = lax.optimization_barrier(temporal)
    weights = jnp.stack(
        [jnp.stack([late[0].T, late[1].T], axis=2), jnp.stack([-late[1].T, late[0].T], axis=2)], axis=0
    )
    gradient = None
    for frame in range(returned.shape[0]):
        for part_in in range(2):
            term = weights[:, :, frame, part_in, None, None] * returned[frame, :, part_in][None, None]
            gradient = term if gradient is None else gradient + term
    return factors - 0.5 * gradient


def solution(mesh):
    placed = (
        P("slab", None, "coil", "frame"),
        P("slab", None, None),
        P("coil", "slab", None),
        P("frame", "coil", "slab", None),
        P("frame", "coil", "slab"),
    )
    return jax.shard_map(
        on_device,
        mesh=mesh,
        in_specs=placed,
        out_specs=P("slab", None, "coil", "frame"),
        check_vma=False,
    )
```

```python
import math

import jax
import ml_dtypes
import numpy as np
import jax.numpy as jnp
from jax import lax
from jax.experimental import pallas as pl
from jax.experimental.pallas import tpu as pltpu
from jax.sharding import PartitionSpec as P


def dft_parts(length):
    index = np.arange(length, dtype=np.int64)
    phase = (index[:, None] * index[None, :]) % length
    angle = np.float32(2.0 * math.pi / length) * phase.astype(np.float32)
    scale = np.float32(1.0 / math.sqrt(length))
    real = (np.cos(angle.astype(np.float64)).astype(np.float32) * scale).astype(ml_dtypes.bfloat16)
    imag = (-np.sin(angle.astype(np.float64)).astype(np.float32) * scale).astype(ml_dtypes.bfloat16)
    return real, imag


def rotate_plus(values, half_width):
    return jnp.concatenate([-values[..., half_width:], values[..., :half_width]], axis=-1)


def rotate_minus(values, half_width):
    return jnp.concatenate([values[..., half_width:], -values[..., :half_width]], axis=-1)


def sens_times(sens, values, half_width):
    sens_re = sens[..., :half_width].astype(jnp.float32)
    sens_im = sens[..., half_width:].astype(jnp.float32)
    value_re = values[..., :half_width].astype(jnp.float32)
    value_im = values[..., half_width:].astype(jnp.float32)
    return jnp.concatenate(
        [sens_re * value_re - sens_im * value_im, sens_re * value_im + sens_im * value_re], axis=-1
    )


def conj_sens_times(sens, values, half_width):
    sens_re = sens[..., :half_width].astype(jnp.float32)
    sens_im = sens[..., half_width:].astype(jnp.float32)
    value_re = values[..., :half_width]
    value_im = values[..., half_width:]
    return jnp.concatenate(
        [sens_re * value_re + sens_im * value_im, sens_re * value_im - sens_im * value_re], axis=-1
    )


def precise(form, first, second):
    return jnp.einsum(form, first, second, precision=lax.Precision.HIGHEST)


PERMUTE_LIMIT = 8


def shifted(count, step):
    return [(source, (source + step) % count) for source in range(count)]


def by_sender(pieces, count, me):
    ring = jnp.stack([pieces[0]] + pieces[1:][::-1])
    doubled = jnp.concatenate([ring, ring], axis=0)
    return lax.dynamic_slice_in_dim(doubled, (count - me) % count, count, 0)


def gather_blocks(value, axis):
    count = lax.axis_size(axis)
    if count > PERMUTE_LIMIT:
        return lax.all_gather(value, axis)
    me = lax.axis_index(axis)
    pieces = [value] + [lax.ppermute(value, axis, shifted(count, step)) for step in range(1, count)]
    return by_sender(pieces, count, me)


def exchange_blocks(blocks, axis):
    count = lax.axis_size(axis)
    if count > PERMUTE_LIMIT:
        return lax.all_to_all(blocks, axis, 0, 0, tiled=True)
    me = lax.axis_index(axis)
    pieces = [lax.dynamic_index_in_dim(blocks, me, 0, keepdims=False)]
    for step in range(1, count):
        outgoing = lax.dynamic_index_in_dim(blocks, (me + step) % count, 0, keepdims=False)
        pieces.append(lax.ppermute(outgoing, axis, shifted(count, step)))
    return by_sender(pieces, count, me)


def reduce_blocks(blocks, axis):
    count = lax.axis_size(axis)
    if count > PERMUTE_LIMIT:
        return lax.psum_scatter(blocks.astype(jnp.bfloat16), axis, scatter_dimension=0).astype(jnp.float32)
    me = lax.axis_index(axis)
    total = lax.dynamic_index_in_dim(blocks, me, 0, keepdims=False)
    for step in range(1, count):
        outgoing = lax.dynamic_index_in_dim(blocks, (me + step) % count, 0, keepdims=False)
        total = total + lax.ppermute(outgoing.astype(jnp.bfloat16), axis, shifted(count, step)).astype(jnp.float32)
    return total


def swap_halves(values, half_width, negate_first):
    low = values[:, :half_width]
    high = values[:, half_width:]
    if negate_first:
        return jnp.concatenate([-high, low], axis=1)
    return jnp.concatenate([high, -low], axis=1)


def coil_terms(image_ref, sens_ref, measured_ref, sampled_ref, forward_ref, adjoint_ref, table_ref):
    coils, height, width = sens_ref.shape
    half_width = width // 2
    sens = sens_ref[...].astype(jnp.float32)
    sens_re = sens[:, :, :half_width]
    sens_im = sens[:, :, half_width:]
    image = image_ref[...].astype(jnp.float32)[None]
    image_re = image[:, :, :half_width]
    image_im = image[:, :, half_width:]
    coil = jnp.concatenate(
        [sens_re * image_re - sens_im * image_im, sens_re * image_im + sens_im * image_re], axis=2
    ).astype(jnp.bfloat16)
    half_k = jnp.dot(coil.reshape(coils * height, width), forward_ref[...], preferred_element_type=jnp.float32)
    table = table_ref[...]
    backs = []
    for coil_index in range(coils):
        one = half_k[coil_index * height:(coil_index + 1) * height].astype(jnp.bfloat16).astype(jnp.float32)
        turned = jnp.concatenate([one[:, :half_width].T, one[:, half_width:].T], axis=0).astype(jnp.bfloat16)
        parts = jnp.dot(turned, table, preferred_element_type=jnp.float32)
        kspace_re = parts[:half_width, :height] - parts[half_width:, height:]
        kspace_im = parts[:half_width, height:] + parts[half_width:, :height]
        row = pl.program_id(0) * coils + coil_index
        sampled = sampled_ref[pl.ds(row, 1), :].astype(jnp.float32)
        measured = measured_ref[coil_index].astype(jnp.float32)
        residual = jnp.concatenate(
            [
                (sampled * (kspace_re - measured[:, :half_width].T)).astype(jnp.bfloat16),
                (sampled * (kspace_im - measured[:, half_width:].T)).astype(jnp.bfloat16),
            ],
            axis=0,
        )
        parts = jnp.dot(residual, table, preferred_element_type=jnp.float32)
        back_re = (parts[:half_width, :height] + parts[half_width:, height:]).astype(jnp.bfloat16)
        back_im = (parts[half_width:, :height] - parts[:half_width, height:]).astype(jnp.bfloat16)
        backs.append(
            jnp.concatenate([back_re.astype(jnp.float32).T, back_im.astype(jnp.float32).T], axis=1).astype(
                jnp.bfloat16
            )
        )
    back_half = jnp.concatenate(backs, axis=0)
    coil_back = jnp.dot(back_half, adjoint_ref[...], preferred_element_type=jnp.float32).reshape(
        coils, height, width
    )
    back_re = coil_back[:, :, :half_width]
    back_im = coil_back[:, :, half_width:]
    term = jnp.concatenate(
        [sens_re * back_re + sens_im * back_im, sens_re * back_im - sens_im * back_re], axis=2
    )
    return jnp.sum(term, axis=0)


def coil_chain_kernel(*refs):
    groups = (len(refs) - 8) // 2
    pieces = refs[:groups]
    place_ref, sens_ref, measured_ref, sampled_ref, forward_ref, adjoint_ref, table_ref = refs[groups:groups + 7]
    own_ref = refs[groups + 7]
    send_refs = refs[groups + 8:2 * groups + 7]
    image_ref, total_ref = refs[2 * groups + 7:]
    rows = pieces[0].shape[0]
    half_width = image_ref.shape[1] // 2
    me = place_ref[0]
    step = pl.program_id(0)

    @pl.when(step == 0)
    def _():
        for block in range(groups):
            source = (me - block + groups) % groups
            value = pieces[0][...]
            for other in range(1, groups):
                value = jnp.where(source == other, pieces[other][...], value)
            image_ref[block * rows:(block + 1) * rows, :] = value

    term = coil_terms(image_ref, sens_ref, measured_ref, sampled_ref, forward_ref, adjoint_ref, table_ref)

    @pl.when(step == 0)
    def _():
        total_ref[...] = term

    @pl.when(step > 0)
    def _():
        total_ref[...] += term

    @pl.when(step == pl.num_programs(0) - 1)
    def _():
        start = pl.multiple_of(me * rows, rows)
        own_ref[...] = total_ref[pl.ds(start, rows), :]
        for shift in range(1, groups):
            start = pl.multiple_of(((me + shift) % groups) * rows, rows)
            send_refs[shift - 1][...] = total_ref[pl.ds(start, rows), :].astype(jnp.bfloat16)


def coil_chain(pieces, place, sens, measured, sampled, forward_x, adjoint_x, table_y):
    coils, height, width = sens.shape
    groups = len(pieces)
    rows = pieces[0].shape[0]
    whole = lambda c: (0, 0)
    per_coil = lambda c: (c, 0, 0)
    step_coils = 8 if coils % 8 == 0 else (4 if coils % 4 == 0 else (2 if coils % 2 == 0 else 1))
    flops = coils * 8 * height * width * width
    return pl.pallas_call(
        coil_chain_kernel,
        out_shape=(jax.ShapeDtypeStruct((rows, width), jnp.float32),)
        + (jax.ShapeDtypeStruct((rows, width), jnp.bfloat16),) * (groups - 1),
        grid=(coils // step_coils,),
        in_specs=[pl.BlockSpec((rows, width), whole)] * groups
        + [
            pl.BlockSpec(memory_space=pltpu.SMEM),
            pl.BlockSpec((step_coils, height, width), per_coil),
            pl.BlockSpec((step_coils, height, width), per_coil),
            pl.BlockSpec((coils, height), whole),
            pl.BlockSpec((width, width), whole),
            pl.BlockSpec((width, width), whole),
            pl.BlockSpec((height, 2 * height), whole),
        ],
        out_specs=(pl.BlockSpec((rows, width), whole),) * groups,
        scratch_shapes=[pltpu.VMEM((height, width), jnp.bfloat16), pltpu.VMEM((height, width), jnp.float32)],
        compiler_params=pltpu.CompilerParams(dimension_semantics=("arbitrary",)),
        cost_estimate=pl.CostEstimate(
            flops=flops, transcendentals=0, bytes_accessed=2 * 2 * coils * height * width + 4 * height * width
        ),
    )(*pieces, place, sens, measured, sampled, forward_x, adjoint_x, table_y)


def on_device(factors, temporal, maps, kdata, masks):
    width_x = maps.shape[2] // 2
    width_y = maps.shape[1]
    rows_own = factors.shape[2]
    table_x_re, table_x_im = dft_parts(width_x)
    table_y_re, table_y_im = dft_parts(width_y)
    forward_x = jnp.asarray(np.block([[table_x_re, table_x_im], [-table_x_im, table_x_re]]))
    adjoint_x = jnp.asarray(np.block([[table_x_re, -table_x_im], [table_x_im, table_x_re]]))
    table_y = jnp.asarray(np.concatenate([table_y_re, table_y_im], axis=1))
    time_re = temporal[0]
    time_im = temporal[1]
    sign = jnp.asarray(np.array([[1.0, -1.0], [1.0, 1.0]], np.float32))
    mixing = jnp.stack([temporal, temporal[::-1]]) * sign[:, :, None, None]
    images = jnp.sum(
        mixing[:, :, :, :, None, None] * factors[None, :, None], axis=(1, 3)
    )
    images = jnp.transpose(images, (1, 0, 2, 3)).astype(jnp.bfloat16)
    frames_here = images.shape[0]
    width_own = images.shape[3]
    pieces_x = exchange_blocks(images, "frame")
    own_rows = jnp.transpose(pieces_x, (2, 1, 0, 3)).reshape(rows_own, 2 * width_x)
    groups = lax.axis_size("coil")
    me_c = lax.axis_index("coil")
    pieces = [own_rows] + [lax.ppermute(own_rows, "coil", shifted(groups, step)) for step in range(1, groups)]
    sampled = masks[0]
    place = jnp.reshape(me_c, (1,)).astype(jnp.int32)
    measured = kdata[0]
    own_total, *outgoing = coil_chain(
        pieces, place, maps, measured, sampled, forward_x, adjoint_x, table_y
    )
    own_share = own_total
    for step in range(1, groups):
        own_share = own_share + lax.ppermute(outgoing[step - 1], "coil", shifted(groups, step)).astype(jnp.float32)
    outgoing = jnp.transpose(
        own_share.reshape(rows_own, 2, frames_here, width_own), (2, 0, 1, 3)
    ).astype(jnp.bfloat16)
    returned = exchange_blocks(outgoing, "frame").astype(jnp.float32)
    late = lax.optimization_barrier(temporal)
    weights = jnp.stack(
        [jnp.stack([late[0].T, late[1].T], axis=2), jnp.stack([-late[1].T, late[0].T], axis=2)], axis=0
    )
    gradient = None
    for frame in range(returned.shape[0]):
        for part_in in range(2):
            term = weights[:, :, frame, part_in, None, None] * returned[frame, :, part_in][None, None]
            gradient = term if gradient is None else gradient + term
    return factors - 0.5 * gradient


def solution(mesh):
    placed = (
        P("slab", None, "coil", "frame"),
        P("slab", None, None),
        P("coil", "slab", None),
        P("frame", "coil", "slab", None),
        P("frame", "coil", "slab"),
    )
    return jax.shard_map(
        on_device,
        mesh=mesh,
        in_specs=placed,
        out_specs=P("slab", None, "coil", "frame"),
        check_vma=False,
    )
```

```python
import math

import jax
import ml_dtypes
import numpy as np
import jax.numpy as jnp
from jax import lax
from jax.experimental import pallas as pl
from jax.experimental.pallas import tpu as pltpu
from jax.sharding import PartitionSpec as P


def dft_parts(length):
    index = np.arange(length, dtype=np.int64)
    phase = (index[:, None] * index[None, :]) % length
    angle = np.float32(2.0 * math.pi / length) * phase.astype(np.float32)
    scale = np.float32(1.0 / math.sqrt(length))
    real = (np.cos(angle.astype(np.float64)).astype(np.float32) * scale).astype(ml_dtypes.bfloat16)
    imag = (-np.sin(angle.astype(np.float64)).astype(np.float32) * scale).astype(ml_dtypes.bfloat16)
    return real, imag


def rotate_plus(values, half_width):
    return jnp.concatenate([-values[..., half_width:], values[..., :half_width]], axis=-1)


def rotate_minus(values, half_width):
    return jnp.concatenate([values[..., half_width:], -values[..., :half_width]], axis=-1)


def sens_times(sens, values, half_width):
    sens_re = sens[..., :half_width].astype(jnp.float32)
    sens_im = sens[..., half_width:].astype(jnp.float32)
    value_re = values[..., :half_width].astype(jnp.float32)
    value_im = values[..., half_width:].astype(jnp.float32)
    return jnp.concatenate(
        [sens_re * value_re - sens_im * value_im, sens_re * value_im + sens_im * value_re], axis=-1
    )


def conj_sens_times(sens, values, half_width):
    sens_re = sens[..., :half_width].astype(jnp.float32)
    sens_im = sens[..., half_width:].astype(jnp.float32)
    value_re = values[..., :half_width]
    value_im = values[..., half_width:]
    return jnp.concatenate(
        [sens_re * value_re + sens_im * value_im, sens_re * value_im - sens_im * value_re], axis=-1
    )


def precise(form, first, second):
    return jnp.einsum(form, first, second, precision=lax.Precision.HIGHEST)


PERMUTE_LIMIT = 8


def shifted(count, step):
    return [(source, (source + step) % count) for source in range(count)]


def by_sender(pieces, count, me):
    ring = jnp.stack([pieces[0]] + pieces[1:][::-1])
    doubled = jnp.concatenate([ring, ring], axis=0)
    return lax.dynamic_slice_in_dim(doubled, (count - me) % count, count, 0)


def gather_blocks(value, axis):
    count = lax.axis_size(axis)
    if count > PERMUTE_LIMIT:
        return lax.all_gather(value, axis)
    me = lax.axis_index(axis)
    pieces = [value] + [lax.ppermute(value, axis, shifted(count, step)) for step in range(1, count)]
    return by_sender(pieces, count, me)


def exchange_blocks(blocks, axis):
    count = lax.axis_size(axis)
    if count > PERMUTE_LIMIT:
        return lax.all_to_all(blocks, axis, 0, 0, tiled=True)
    me = lax.axis_index(axis)
    pieces = [lax.dynamic_index_in_dim(blocks, me, 0, keepdims=False)]
    for step in range(1, count):
        outgoing = lax.dynamic_index_in_dim(blocks, (me + step) % count, 0, keepdims=False)
        pieces.append(lax.ppermute(outgoing, axis, shifted(count, step)))
    return by_sender(pieces, count, me)


def reduce_blocks(blocks, axis):
    count = lax.axis_size(axis)
    if count > PERMUTE_LIMIT:
        return lax.psum_scatter(blocks.astype(jnp.bfloat16), axis, scatter_dimension=0).astype(jnp.float32)
    me = lax.axis_index(axis)
    total = lax.dynamic_index_in_dim(blocks, me, 0, keepdims=False)
    for step in range(1, count):
        outgoing = lax.dynamic_index_in_dim(blocks, (me + step) % count, 0, keepdims=False)
        total = total + lax.ppermute(outgoing.astype(jnp.bfloat16), axis, shifted(count, step)).astype(jnp.float32)
    return total


def swap_halves(values, half_width, negate_first):
    low = values[:, :half_width]
    high = values[:, half_width:]
    if negate_first:
        return jnp.concatenate([-high, low], axis=1)
    return jnp.concatenate([high, -low], axis=1)


def coil_terms(image_ref, sens_ref, measured_ref, sampled_ref, forward_ref, adjoint_ref, table_ref):
    coils, height, width = sens_ref.shape
    half_width = width // 2
    sens = sens_ref[...].astype(jnp.float32)
    sens_re = sens[:, :, :half_width]
    sens_im = sens[:, :, half_width:]
    image = image_ref[...].astype(jnp.float32)[None]
    image_re = image[:, :, :half_width]
    image_im = image[:, :, half_width:]
    coil = jnp.concatenate(
        [sens_re * image_re - sens_im * image_im, sens_re * image_im + sens_im * image_re], axis=2
    ).astype(jnp.bfloat16)
    half_k = jnp.dot(coil.reshape(coils * height, width), forward_ref[...], preferred_element_type=jnp.float32)
    table = table_ref[...]
    backs = []
    for coil_index in range(coils):
        one = half_k[coil_index * height:(coil_index + 1) * height].astype(jnp.bfloat16).astype(jnp.float32)
        turned = jnp.concatenate([one[:, :half_width].T, one[:, half_width:].T], axis=0).astype(jnp.bfloat16)
        parts = jnp.dot(turned, table, preferred_element_type=jnp.float32)
        kspace_re = parts[:half_width, :height] - parts[half_width:, height:]
        kspace_im = parts[:half_width, height:] + parts[half_width:, :height]
        row = pl.program_id(0) * coils + coil_index
        sampled = sampled_ref[pl.ds(row, 1), :].astype(jnp.float32)
        measured = measured_ref[coil_index].astype(jnp.float32)
        residual = jnp.concatenate(
            [
                (sampled * (kspace_re - measured[:, :half_width].T)).astype(jnp.bfloat16),
                (sampled * (kspace_im - measured[:, half_width:].T)).astype(jnp.bfloat16),
            ],
            axis=0,
        )
        parts = jnp.dot(residual, table, preferred_element_type=jnp.float32)
        back_re = (parts[:half_width, :height] + parts[half_width:, height:]).astype(jnp.bfloat16)
        back_im = (parts[half_width:, :height] - parts[:half_width, height:]).astype(jnp.bfloat16)
        backs.append(
            jnp.concatenate([back_re.astype(jnp.float32).T, back_im.astype(jnp.float32).T], axis=1).astype(
                jnp.bfloat16
            )
        )
    back_half = jnp.concatenate(backs, axis=0)
    coil_back = jnp.dot(back_half, adjoint_ref[...], preferred_element_type=jnp.float32).reshape(
        coils, height, width
    )
    back_re = coil_back[:, :, :half_width]
    back_im = coil_back[:, :, half_width:]
    term = jnp.concatenate(
        [sens_re * back_re + sens_im * back_im, sens_re * back_im - sens_im * back_re], axis=2
    )
    return jnp.sum(term, axis=0)


def coil_chain_kernel(*refs):
    groups = (len(refs) - 8) // 2
    pieces = refs[:groups]
    place_ref, sens_ref, measured_ref, sampled_ref, forward_ref, adjoint_ref, table_ref = refs[groups:groups + 7]
    own_ref = refs[groups + 7]
    send_refs = refs[groups + 8:2 * groups + 7]
    image_ref, total_ref = refs[2 * groups + 7:]
    rows = pieces[0].shape[0]
    half_width = image_ref.shape[1] // 2
    me = place_ref[0]
    step = pl.program_id(0)

    @pl.when(step == 0)
    def _():
        for block in range(groups):
            source = (me - block + groups) % groups
            value = pieces[0][...]
            for other in range(1, groups):
                value = jnp.where(source == other, pieces[other][...], value)
            image_ref[block * rows:(block + 1) * rows, :] = value

    term = coil_terms(image_ref, sens_ref, measured_ref, sampled_ref, forward_ref, adjoint_ref, table_ref)

    @pl.when(step == 0)
    def _():
        total_ref[...] = term

    @pl.when(step > 0)
    def _():
        total_ref[...] += term

    @pl.when(step == pl.num_programs(0) - 1)
    def _():
        start = pl.multiple_of(me * rows, rows)
        own_ref[...] = total_ref[pl.ds(start, rows), :]
        for shift in range(1, groups):
            start = pl.multiple_of(((me + shift) % groups) * rows, rows)
            send_refs[shift - 1][...] = total_ref[pl.ds(start, rows), :].astype(jnp.bfloat16)


def coil_chain(pieces, place, sens, measured, sampled, forward_x, adjoint_x, table_y):
    coils, height, width = sens.shape
    groups = len(pieces)
    rows = pieces[0].shape[0]
    whole = lambda c: (0, 0)
    per_coil = lambda c: (c, 0, 0)
    step_coils = 4 if coils % 4 == 0 else (2 if coils % 2 == 0 else 1)
    flops = coils * 8 * height * width * width
    return pl.pallas_call(
        coil_chain_kernel,
        out_shape=(jax.ShapeDtypeStruct((rows, width), jnp.float32),)
        + (jax.ShapeDtypeStruct((rows, width), jnp.bfloat16),) * (groups - 1),
        grid=(coils // step_coils,),
        in_specs=[pl.BlockSpec((rows, width), whole)] * groups
        + [
            pl.BlockSpec(memory_space=pltpu.SMEM),
            pl.BlockSpec((step_coils, height, width), per_coil),
            pl.BlockSpec((step_coils, height, width), per_coil),
            pl.BlockSpec((coils, height), whole),
            pl.BlockSpec((width, width), whole),
            pl.BlockSpec((width, width), whole),
            pl.BlockSpec((height, 2 * height), whole),
        ],
        out_specs=(pl.BlockSpec((rows, width), whole),) * groups,
        scratch_shapes=[pltpu.VMEM((height, width), jnp.bfloat16), pltpu.VMEM((height, width), jnp.float32)],
        compiler_params=pltpu.CompilerParams(dimension_semantics=("arbitrary",)),
        cost_estimate=pl.CostEstimate(
            flops=flops, transcendentals=0, bytes_accessed=2 * 2 * coils * height * width + 4 * height * width
        ),
    )(*pieces, place, sens, measured, sampled, forward_x, adjoint_x, table_y)


def on_device(factors, temporal, maps, kdata, masks):
    width_x = maps.shape[2] // 2
    width_y = maps.shape[1]
    rows_own = factors.shape[2]
    table_x_re, table_x_im = dft_parts(width_x)
    table_y_re, table_y_im = dft_parts(width_y)
    forward_x = jnp.asarray(np.block([[table_x_re, table_x_im], [-table_x_im, table_x_re]]))
    adjoint_x = jnp.asarray(np.block([[table_x_re, -table_x_im], [table_x_im, table_x_re]]))
    table_y = jnp.asarray(np.concatenate([table_y_re, table_y_im], axis=1))
    time_re = temporal[0]
    time_im = temporal[1]
    parts, ranks = factors.shape[:2]
    weights_in = jnp.stack(
        [
            jnp.concatenate([temporal[0], -temporal[1]], axis=-1),
            jnp.concatenate([temporal[1], temporal[0]], axis=-1),
        ]
    )
    images = jnp.sum(
        weights_in[:, :, :, None, None] * factors.reshape((parts * ranks,) + factors.shape[2:])[None, None],
        axis=2,
    )
    images = jnp.transpose(images, (1, 0, 2, 3)).astype(jnp.bfloat16)
    frames_here = images.shape[0]
    width_own = images.shape[3]
    pieces_x = exchange_blocks(images, "frame")
    own_rows = jnp.transpose(pieces_x, (2, 1, 0, 3)).reshape(rows_own, 2 * width_x)
    groups = lax.axis_size("coil")
    me_c = lax.axis_index("coil")
    pieces = [own_rows] + [lax.ppermute(own_rows, "coil", shifted(groups, step)) for step in range(1, groups)]
    sampled = masks[0]
    place = jnp.reshape(me_c, (1,)).astype(jnp.int32)
    measured = kdata[0]
    own_total, *outgoing = coil_chain(
        pieces, place, maps, measured, sampled, forward_x, adjoint_x, table_y
    )
    own_share = own_total
    for step in range(1, groups):
        own_share = own_share + lax.ppermute(outgoing[step - 1], "coil", shifted(groups, step)).astype(jnp.float32)
    outgoing = jnp.transpose(
        own_share.reshape(rows_own, 2, frames_here, width_own), (2, 0, 1, 3)
    ).astype(jnp.bfloat16)
    returned = exchange_blocks(outgoing, "frame").astype(jnp.float32)
    late = lax.optimization_barrier(temporal)
    weights = jnp.stack(
        [jnp.stack([late[0].T, late[1].T], axis=2), jnp.stack([-late[1].T, late[0].T], axis=2)], axis=0
    )
    gradient = None
    for frame in range(returned.shape[0]):
        for part_in in range(2):
            term = weights[:, :, frame, part_in, None, None] * returned[frame, :, part_in][None, None]
            gradient = term if gradient is None else gradient + term
    return factors - 0.5 * gradient


def solution(mesh):
    placed = (
        P("slab", None, "coil", "frame"),
        P("slab", None, None),
        P("coil", "slab", None),
        P("frame", "coil", "slab", None),
        P("frame", "coil", "slab"),
    )
    return jax.shard_map(
        on_device,
        mesh=mesh,
        in_specs=placed,
        out_specs=P("slab", None, "coil", "frame"),
        check_vma=False,
    )
```

```python
import math

import jax
import ml_dtypes
import numpy as np
import jax.numpy as jnp
from jax import lax
from jax.experimental import pallas as pl
from jax.experimental.pallas import tpu as pltpu
from jax.sharding import PartitionSpec as P


def dft_parts(length):
    index = np.arange(length, dtype=np.int64)
    phase = (index[:, None] * index[None, :]) % length
    angle = np.float32(2.0 * math.pi / length) * phase.astype(np.float32)
    scale = np.float32(1.0 / math.sqrt(length))
    real = (np.cos(angle.astype(np.float64)).astype(np.float32) * scale).astype(ml_dtypes.bfloat16)
    imag = (-np.sin(angle.astype(np.float64)).astype(np.float32) * scale).astype(ml_dtypes.bfloat16)
    return real, imag


def rotate_plus(values, half_width):
    return jnp.concatenate([-values[..., half_width:], values[..., :half_width]], axis=-1)


def rotate_minus(values, half_width):
    return jnp.concatenate([values[..., half_width:], -values[..., :half_width]], axis=-1)


def sens_times(sens, values, half_width):
    sens_re = sens[..., :half_width].astype(jnp.float32)
    sens_im = sens[..., half_width:].astype(jnp.float32)
    value_re = values[..., :half_width].astype(jnp.float32)
    value_im = values[..., half_width:].astype(jnp.float32)
    return jnp.concatenate(
        [sens_re * value_re - sens_im * value_im, sens_re * value_im + sens_im * value_re], axis=-1
    )


def conj_sens_times(sens, values, half_width):
    sens_re = sens[..., :half_width].astype(jnp.float32)
    sens_im = sens[..., half_width:].astype(jnp.float32)
    value_re = values[..., :half_width]
    value_im = values[..., half_width:]
    return jnp.concatenate(
        [sens_re * value_re + sens_im * value_im, sens_re * value_im - sens_im * value_re], axis=-1
    )


def precise(form, first, second):
    return jnp.einsum(form, first, second, precision=lax.Precision.HIGHEST)


PERMUTE_LIMIT = 8


def shifted(count, step):
    return [(source, (source + step) % count) for source in range(count)]


def by_sender(pieces, count, me):
    ring = jnp.stack([pieces[0]] + pieces[1:][::-1])
    doubled = jnp.concatenate([ring, ring], axis=0)
    return lax.dynamic_slice_in_dim(doubled, (count - me) % count, count, 0)


def gather_blocks(value, axis):
    count = lax.axis_size(axis)
    if count > PERMUTE_LIMIT:
        return lax.all_gather(value, axis)
    me = lax.axis_index(axis)
    pieces = [value] + [lax.ppermute(value, axis, shifted(count, step)) for step in range(1, count)]
    return by_sender(pieces, count, me)


def exchange_blocks(blocks, axis):
    count = lax.axis_size(axis)
    if count > PERMUTE_LIMIT:
        return lax.all_to_all(blocks, axis, 0, 0, tiled=True)
    me = lax.axis_index(axis)
    pieces = [lax.dynamic_index_in_dim(blocks, me, 0, keepdims=False)]
    for step in range(1, count):
        outgoing = lax.dynamic_index_in_dim(blocks, (me + step) % count, 0, keepdims=False)
        pieces.append(lax.ppermute(outgoing, axis, shifted(count, step)))
    return by_sender(pieces, count, me)


def reduce_blocks(blocks, axis):
    count = lax.axis_size(axis)
    if count > PERMUTE_LIMIT:
        return lax.psum_scatter(blocks.astype(jnp.bfloat16), axis, scatter_dimension=0).astype(jnp.float32)
    me = lax.axis_index(axis)
    total = lax.dynamic_index_in_dim(blocks, me, 0, keepdims=False)
    for step in range(1, count):
        outgoing = lax.dynamic_index_in_dim(blocks, (me + step) % count, 0, keepdims=False)
        total = total + lax.ppermute(outgoing.astype(jnp.bfloat16), axis, shifted(count, step)).astype(jnp.float32)
    return total


def swap_halves(values, half_width, negate_first):
    low = values[:, :half_width]
    high = values[:, half_width:]
    if negate_first:
        return jnp.concatenate([-high, low], axis=1)
    return jnp.concatenate([high, -low], axis=1)


def coil_terms(image_ref, sens_ref, measured_ref, sampled_ref, forward_ref, adjoint_ref, table_ref):
    coils, height, width = sens_ref.shape
    half_width = width // 2
    sens = sens_ref[...].astype(jnp.float32)
    sens_re = sens[:, :, :half_width]
    sens_im = sens[:, :, half_width:]
    image = image_ref[...].astype(jnp.float32)[None]
    image_re = image[:, :, :half_width]
    image_im = image[:, :, half_width:]
    coil = jnp.concatenate(
        [sens_re * image_re - sens_im * image_im, sens_re * image_im + sens_im * image_re], axis=2
    ).astype(jnp.bfloat16)
    half_k = jnp.dot(coil.reshape(coils * height, width), forward_ref[...], preferred_element_type=jnp.float32)
    table = table_ref[...]
    backs = []
    for coil_index in range(coils):
        one = half_k[coil_index * height:(coil_index + 1) * height].astype(jnp.bfloat16).astype(jnp.float32)
        turned = jnp.concatenate([one[:, :half_width].T, one[:, half_width:].T], axis=0).astype(jnp.bfloat16)
        parts = jnp.dot(turned, table, preferred_element_type=jnp.float32)
        kspace_re = parts[:half_width, :height] - parts[half_width:, height:]
        kspace_im = parts[:half_width, height:] + parts[half_width:, :height]
        row = pl.program_id(0) * coils + coil_index
        sampled = sampled_ref[pl.ds(row, 1), :].astype(jnp.float32)
        measured = measured_ref[coil_index].astype(jnp.float32)
        residual = jnp.concatenate(
            [
                (sampled * (kspace_re - measured[:, :half_width].T)).astype(jnp.bfloat16),
                (sampled * (kspace_im - measured[:, half_width:].T)).astype(jnp.bfloat16),
            ],
            axis=0,
        )
        parts = jnp.dot(residual, table, preferred_element_type=jnp.float32)
        back_re = (parts[:half_width, :height] + parts[half_width:, height:]).astype(jnp.bfloat16)
        back_im = (parts[half_width:, :height] - parts[:half_width, height:]).astype(jnp.bfloat16)
        backs.append(
            jnp.concatenate([back_re.astype(jnp.float32).T, back_im.astype(jnp.float32).T], axis=1).astype(
                jnp.bfloat16
            )
        )
    back_half = jnp.concatenate(backs, axis=0)
    coil_back = jnp.dot(back_half, adjoint_ref[...], preferred_element_type=jnp.float32).reshape(
        coils, height, width
    )
    back_re = coil_back[:, :, :half_width]
    back_im = coil_back[:, :, half_width:]
    term = jnp.concatenate(
        [sens_re * back_re + sens_im * back_im, sens_re * back_im - sens_im * back_re], axis=2
    )
    return jnp.sum(term, axis=0)


def coil_chain_kernel(*refs):
    groups = (len(refs) - 8) // 2
    pieces = refs[:groups]
    place_ref, sens_ref, measured_ref, sampled_ref, forward_ref, adjoint_ref, table_ref = refs[groups:groups + 7]
    own_ref = refs[groups + 7]
    send_refs = refs[groups + 8:2 * groups + 7]
    image_ref, total_ref = refs[2 * groups + 7:]
    rows = pieces[0].shape[0]
    half_width = image_ref.shape[1] // 2
    me = place_ref[0]
    step = pl.program_id(0)

    @pl.when(step == 0)
    def _():
        for block in range(groups):
            source = (me - block + groups) % groups
            value = pieces[0][...]
            for other in range(1, groups):
                value = jnp.where(source == other, pieces[other][...], value)
            image_ref[block * rows:(block + 1) * rows, :] = value

    term = coil_terms(image_ref, sens_ref, measured_ref, sampled_ref, forward_ref, adjoint_ref, table_ref)

    @pl.when(step == 0)
    def _():
        total_ref[...] = term

    @pl.when(step > 0)
    def _():
        total_ref[...] += term

    @pl.when(step == pl.num_programs(0) - 1)
    def _():
        start = pl.multiple_of(me * rows, rows)
        own_ref[...] = total_ref[pl.ds(start, rows), :]
        for shift in range(1, groups):
            start = pl.multiple_of(((me + shift) % groups) * rows, rows)
            send_refs[shift - 1][...] = total_ref[pl.ds(start, rows), :].astype(jnp.bfloat16)


def coil_chain(pieces, place, sens, measured, sampled, forward_x, adjoint_x, table_y):
    coils, height, width = sens.shape
    groups = len(pieces)
    rows = pieces[0].shape[0]
    whole = lambda c: (0, 0)
    per_coil = lambda c: (c, 0, 0)
    step_coils = 4 if coils % 4 == 0 else (2 if coils % 2 == 0 else 1)
    flops = coils * 8 * height * width * width
    return pl.pallas_call(
        coil_chain_kernel,
        out_shape=(jax.ShapeDtypeStruct((rows, width), jnp.float32),)
        + (jax.ShapeDtypeStruct((rows, width), jnp.bfloat16),) * (groups - 1),
        grid=(coils // step_coils,),
        in_specs=[pl.BlockSpec(memory_space=pltpu.VMEM)] * groups
        + [
            pl.BlockSpec(memory_space=pltpu.SMEM),
            pl.BlockSpec((step_coils, height, width), per_coil),
            pl.BlockSpec((step_coils, height, width), per_coil),
            pl.BlockSpec((coils, height), whole),
            pl.BlockSpec((width, width), whole),
            pl.BlockSpec((width, width), whole),
            pl.BlockSpec((height, 2 * height), whole),
        ],
        out_specs=(pl.BlockSpec((rows, width), whole),) * groups,
        scratch_shapes=[pltpu.VMEM((height, width), jnp.bfloat16), pltpu.VMEM((height, width), jnp.float32)],
        compiler_params=pltpu.CompilerParams(dimension_semantics=("arbitrary",)),
        cost_estimate=pl.CostEstimate(
            flops=flops, transcendentals=0, bytes_accessed=2 * 2 * coils * height * width + 4 * height * width
        ),
    )(*pieces, place, sens, measured, sampled, forward_x, adjoint_x, table_y)


def on_device(factors, temporal, maps, kdata, masks):
    width_x = maps.shape[2] // 2
    width_y = maps.shape[1]
    rows_own = factors.shape[2]
    table_x_re, table_x_im = dft_parts(width_x)
    table_y_re, table_y_im = dft_parts(width_y)
    forward_x = jnp.asarray(np.block([[table_x_re, table_x_im], [-table_x_im, table_x_re]]))
    adjoint_x = jnp.asarray(np.block([[table_x_re, -table_x_im], [table_x_im, table_x_re]]))
    table_y = jnp.asarray(np.concatenate([table_y_re, table_y_im], axis=1))
    time_re = temporal[0]
    time_im = temporal[1]
    parts, ranks = factors.shape[:2]
    weights_in = jnp.stack(
        [
            jnp.concatenate([temporal[0], -temporal[1]], axis=-1),
            jnp.concatenate([temporal[1], temporal[0]], axis=-1),
        ]
    )
    images = jnp.sum(
        weights_in[:, :, :, None, None] * factors.reshape((parts * ranks,) + factors.shape[2:])[None, None],
        axis=2,
    )
    images = jnp.transpose(images, (1, 0, 2, 3)).astype(jnp.bfloat16)
    frames_here = images.shape[0]
    width_own = images.shape[3]
    pieces_x = exchange_blocks(images, "frame")
    own_rows = jnp.transpose(pieces_x, (2, 1, 0, 3)).reshape(rows_own, 2 * width_x)
    groups = lax.axis_size("coil")
    me_c = lax.axis_index("coil")
    pieces = [own_rows] + [lax.ppermute(own_rows, "coil", shifted(groups, step)) for step in range(1, groups)]
    sampled = masks[0]
    place = jnp.reshape(me_c, (1,)).astype(jnp.int32)
    measured = kdata[0]
    own_total, *outgoing = coil_chain(
        pieces, place, maps, measured, sampled, forward_x, adjoint_x, table_y
    )
    own_share = own_total
    for step in range(1, groups):
        own_share = own_share + lax.ppermute(outgoing[step - 1], "coil", shifted(groups, step)).astype(jnp.float32)
    outgoing = jnp.transpose(
        own_share.reshape(rows_own, 2, frames_here, width_own), (2, 0, 1, 3)
    ).astype(jnp.bfloat16)
    returned = exchange_blocks(outgoing, "frame").astype(jnp.float32)
    late = lax.optimization_barrier(temporal)
    weights = jnp.stack(
        [jnp.stack([late[0].T, late[1].T], axis=2), jnp.stack([-late[1].T, late[0].T], axis=2)], axis=0
    )
    gradient = None
    for frame in range(returned.shape[0]):
        for part_in in range(2):
            term = weights[:, :, frame, part_in, None, None] * returned[frame, :, part_in][None, None]
            gradient = term if gradient is None else gradient + term
    return factors - 0.5 * gradient


def solution(mesh):
    placed = (
        P("slab", None, "coil", "frame"),
        P("slab", None, None),
        P("coil", "slab", None),
        P("frame", "coil", "slab", None),
        P("frame", "coil", "slab"),
    )
    return jax.shard_map(
        on_device,
        mesh=mesh,
        in_specs=placed,
        out_specs=P("slab", None, "coil", "frame"),
        check_vma=False,
    )
```

```python
import math

import jax
import ml_dtypes
import numpy as np
import jax.numpy as jnp
from jax import lax
from jax.experimental import pallas as pl
from jax.experimental.pallas import tpu as pltpu
from jax.sharding import PartitionSpec as P


def dft_parts(length):
    index = np.arange(length, dtype=np.int64)
    phase = (index[:, None] * index[None, :]) % length
    angle = np.float32(2.0 * math.pi / length) * phase.astype(np.float32)
    scale = np.float32(1.0 / math.sqrt(length))
    real = (np.cos(angle.astype(np.float64)).astype(np.float32) * scale).astype(ml_dtypes.bfloat16)
    imag = (-np.sin(angle.astype(np.float64)).astype(np.float32) * scale).astype(ml_dtypes.bfloat16)
    return real, imag


def rotate_plus(values, half_width):
    return jnp.concatenate([-values[..., half_width:], values[..., :half_width]], axis=-1)


def rotate_minus(values, half_width):
    return jnp.concatenate([values[..., half_width:], -values[..., :half_width]], axis=-1)


def sens_times(sens, values, half_width):
    sens_re = sens[..., :half_width].astype(jnp.float32)
    sens_im = sens[..., half_width:].astype(jnp.float32)
    value_re = values[..., :half_width].astype(jnp.float32)
    value_im = values[..., half_width:].astype(jnp.float32)
    return jnp.concatenate(
        [sens_re * value_re - sens_im * value_im, sens_re * value_im + sens_im * value_re], axis=-1
    )


def conj_sens_times(sens, values, half_width):
    sens_re = sens[..., :half_width].astype(jnp.float32)
    sens_im = sens[..., half_width:].astype(jnp.float32)
    value_re = values[..., :half_width]
    value_im = values[..., half_width:]
    return jnp.concatenate(
        [sens_re * value_re + sens_im * value_im, sens_re * value_im - sens_im * value_re], axis=-1
    )


def precise(form, first, second):
    return jnp.einsum(form, first, second, precision=lax.Precision.HIGHEST)


PERMUTE_LIMIT = 8


def shifted(count, step):
    return [(source, (source + step) % count) for source in range(count)]


def by_sender(pieces, count, me):
    ring = jnp.stack([pieces[0]] + pieces[1:][::-1])
    doubled = jnp.concatenate([ring, ring], axis=0)
    return lax.dynamic_slice_in_dim(doubled, (count - me) % count, count, 0)


def gather_blocks(value, axis):
    count = lax.axis_size(axis)
    if count > PERMUTE_LIMIT:
        return lax.all_gather(value, axis)
    me = lax.axis_index(axis)
    pieces = [value] + [lax.ppermute(value, axis, shifted(count, step)) for step in range(1, count)]
    return by_sender(pieces, count, me)


def exchange_blocks(blocks, axis):
    count = lax.axis_size(axis)
    if count > PERMUTE_LIMIT:
        return lax.all_to_all(blocks, axis, 0, 0, tiled=True)
    me = lax.axis_index(axis)
    pieces = [lax.dynamic_index_in_dim(blocks, me, 0, keepdims=False)]
    for step in range(1, count):
        outgoing = lax.dynamic_index_in_dim(blocks, (me + step) % count, 0, keepdims=False)
        pieces.append(lax.ppermute(outgoing, axis, shifted(count, step)))
    return by_sender(pieces, count, me)


def reduce_blocks(blocks, axis):
    count = lax.axis_size(axis)
    if count > PERMUTE_LIMIT:
        return lax.psum_scatter(blocks.astype(jnp.bfloat16), axis, scatter_dimension=0).astype(jnp.float32)
    me = lax.axis_index(axis)
    total = lax.dynamic_index_in_dim(blocks, me, 0, keepdims=False)
    for step in range(1, count):
        outgoing = lax.dynamic_index_in_dim(blocks, (me + step) % count, 0, keepdims=False)
        total = total + lax.ppermute(outgoing.astype(jnp.bfloat16), axis, shifted(count, step)).astype(jnp.float32)
    return total


def swap_halves(values, half_width, negate_first):
    low = values[:, :half_width]
    high = values[:, half_width:]
    if negate_first:
        return jnp.concatenate([-high, low], axis=1)
    return jnp.concatenate([high, -low], axis=1)


def coil_terms(image_ref, sens_ref, measured_ref, sampled_ref, forward_ref, adjoint_ref, table_ref):
    coils, height, width = sens_ref.shape
    half_width = width // 2
    sens = sens_ref[...].astype(jnp.float32)
    sens_re = sens[:, :, :half_width]
    sens_im = sens[:, :, half_width:]
    image = image_ref[...].astype(jnp.float32)[None]
    image_re = image[:, :, :half_width]
    image_im = image[:, :, half_width:]
    coil = jnp.concatenate(
        [sens_re * image_re - sens_im * image_im, sens_re * image_im + sens_im * image_re], axis=2
    ).astype(jnp.bfloat16)
    half_k = jnp.dot(coil.reshape(coils * height, width), forward_ref[...], preferred_element_type=jnp.float32)
    table = table_ref[...]
    backs = []
    for coil_index in range(coils):
        one = half_k[coil_index * height:(coil_index + 1) * height].astype(jnp.bfloat16).astype(jnp.float32)
        turned = jnp.concatenate([one[:, :half_width].T, one[:, half_width:].T], axis=0).astype(jnp.bfloat16)
        parts = jnp.dot(turned, table, preferred_element_type=jnp.float32)
        kspace_re = parts[:half_width, :height] - parts[half_width:, height:]
        kspace_im = parts[:half_width, height:] + parts[half_width:, :height]
        row = pl.program_id(0) * coils + coil_index
        sampled = sampled_ref[pl.ds(row, 1), :].astype(jnp.float32)
        measured = measured_ref[coil_index].astype(jnp.float32)
        residual = jnp.concatenate(
            [
                (sampled * (kspace_re - measured[:, :half_width].T)).astype(jnp.bfloat16),
                (sampled * (kspace_im - measured[:, half_width:].T)).astype(jnp.bfloat16),
            ],
            axis=0,
        )
        parts = jnp.dot(residual, table, preferred_element_type=jnp.float32)
        back_re = (parts[:half_width, :height] + parts[half_width:, height:]).astype(jnp.bfloat16)
        back_im = (parts[half_width:, :height] - parts[:half_width, height:]).astype(jnp.bfloat16)
        backs.append(
            jnp.concatenate([back_re.astype(jnp.float32).T, back_im.astype(jnp.float32).T], axis=1).astype(
                jnp.bfloat16
            )
        )
    back_half = jnp.concatenate(backs, axis=0)
    coil_back = jnp.dot(back_half, adjoint_ref[...], preferred_element_type=jnp.float32).reshape(
        coils, height, width
    )
    back_re = coil_back[:, :, :half_width]
    back_im = coil_back[:, :, half_width:]
    term = jnp.concatenate(
        [sens_re * back_re + sens_im * back_im, sens_re * back_im - sens_im * back_re], axis=2
    )
    return jnp.sum(term, axis=0)


def coil_chain_kernel(*refs):
    groups = (len(refs) - 8) // 2
    pieces = refs[:groups]
    place_ref, sens_ref, measured_ref, sampled_ref, forward_ref, adjoint_ref, table_ref = refs[groups:groups + 7]
    own_ref = refs[groups + 7]
    send_refs = refs[groups + 8:2 * groups + 7]
    image_ref, total_ref = refs[2 * groups + 7:]
    rows = pieces[0].shape[0]
    half_width = image_ref.shape[1] // 2
    me = place_ref[0]
    step = pl.program_id(0)

    @pl.when(step == 0)
    def _():
        for block in range(groups):
            source = (me - block + groups) % groups
            value = pieces[0][...]
            for other in range(1, groups):
                value = jnp.where(source == other, pieces[other][...], value)
            image_ref[block * rows:(block + 1) * rows, :] = value

    term = coil_terms(image_ref, sens_ref, measured_ref, sampled_ref, forward_ref, adjoint_ref, table_ref)

    @pl.when(step == 0)
    def _():
        total_ref[...] = term

    @pl.when(step > 0)
    def _():
        total_ref[...] += term

    @pl.when(step == pl.num_programs(0) - 1)
    def _():
        start = pl.multiple_of(me * rows, rows)
        own_ref[...] = total_ref[pl.ds(start, rows), :]
        for shift in range(1, groups):
            start = pl.multiple_of(((me + shift) % groups) * rows, rows)
            send_refs[shift - 1][...] = total_ref[pl.ds(start, rows), :].astype(jnp.bfloat16)


def coil_chain(pieces, place, sens, measured, sampled, forward_x, adjoint_x, table_y):
    coils, height, width = sens.shape
    groups = len(pieces)
    rows = pieces[0].shape[0]
    whole = lambda c: (0, 0)
    per_coil = lambda c: (c, 0, 0)
    step_coils = 4 if coils % 4 == 0 else (2 if coils % 2 == 0 else 1)
    flops = coils * 8 * height * width * width
    return pl.pallas_call(
        coil_chain_kernel,
        out_shape=(jax.ShapeDtypeStruct((rows, width), jnp.float32),)
        + (jax.ShapeDtypeStruct((rows, width), jnp.bfloat16),) * (groups - 1),
        grid=(coils // step_coils,),
        in_specs=[pl.BlockSpec((rows, width), whole)] * groups
        + [
            pl.BlockSpec(memory_space=pltpu.SMEM),
            pl.BlockSpec((step_coils, height, width), per_coil),
            pl.BlockSpec((step_coils, height, width), per_coil),
            pl.BlockSpec((coils, height), whole),
            pl.BlockSpec((width, width), whole),
            pl.BlockSpec((width, width), whole),
            pl.BlockSpec((height, 2 * height), whole),
        ],
        out_specs=(pl.BlockSpec((rows, width), whole),) * groups,
        scratch_shapes=[pltpu.VMEM((height, width), jnp.bfloat16), pltpu.VMEM((height, width), jnp.float32)],
        compiler_params=pltpu.CompilerParams(dimension_semantics=("arbitrary",)),
        cost_estimate=pl.CostEstimate(
            flops=flops, transcendentals=0, bytes_accessed=2 * 2 * coils * height * width + 4 * height * width
        ),
    )(*pieces, place, sens, measured, sampled, forward_x, adjoint_x, table_y)


def on_device(factors, temporal, maps, kdata, masks):
    width_x = maps.shape[2] // 2
    width_y = maps.shape[1]
    rows_own = factors.shape[2]
    table_x_re, table_x_im = dft_parts(width_x)
    table_y_re, table_y_im = dft_parts(width_y)
    forward_x = jnp.asarray(np.block([[table_x_re, table_x_im], [-table_x_im, table_x_re]]))
    adjoint_x = jnp.asarray(np.block([[table_x_re, -table_x_im], [table_x_im, table_x_re]]))
    table_y = jnp.asarray(np.concatenate([table_y_re, table_y_im], axis=1))
    time_re = temporal[0]
    time_im = temporal[1]
    parts, ranks = factors.shape[:2]
    weights_in = jnp.stack(
        [
            jnp.concatenate([temporal[0], -temporal[1]], axis=-1),
            jnp.concatenate([temporal[1], temporal[0]], axis=-1),
        ]
    )
    images = jnp.sum(
        weights_in[:, :, :, None, None] * factors.reshape((parts * ranks,) + factors.shape[2:])[None, None],
        axis=2,
    )
    images = jnp.transpose(images, (1, 0, 2, 3)).astype(jnp.bfloat16)
    frames_here = images.shape[0]
    width_own = images.shape[3]
    pieces_x = exchange_blocks(images, "frame")
    own_rows = jnp.transpose(pieces_x, (2, 1, 0, 3)).reshape(rows_own, 2 * width_x)
    groups = lax.axis_size("coil")
    me_c = lax.axis_index("coil")
    pieces = [own_rows] + [lax.ppermute(own_rows, "coil", shifted(groups, step)) for step in range(1, groups)]
    sampled = masks[0]
    place = jnp.reshape(me_c, (1,)).astype(jnp.int32)
    measured = kdata[0]
    own_total, *outgoing = coil_chain(
        pieces, place, maps, measured, sampled, forward_x, adjoint_x, table_y
    )
    own_share = own_total
    for step in range(1, groups):
        own_share = own_share + lax.ppermute(outgoing[step - 1], "coil", shifted(groups, step)).astype(jnp.float32)
    outgoing = jnp.transpose(
        own_share.reshape(rows_own, 2, frames_here, width_own), (2, 0, 1, 3)
    ).astype(jnp.bfloat16)
    returned = exchange_blocks(outgoing, "frame").astype(jnp.float32)
    late = lax.optimization_barrier(temporal)
    weights = jnp.stack(
        [jnp.stack([late[0].T, late[1].T], axis=2), jnp.stack([-late[1].T, late[0].T], axis=2)], axis=0
    )
    step_weights = -0.5 * weights
    gradient = None
    for frame in range(returned.shape[0]):
        for part_in in range(2):
            term = step_weights[:, :, frame, part_in, None, None] * returned[frame, :, part_in][None, None]
            gradient = term if gradient is None else gradient + term
    return factors + gradient


def solution(mesh):
    placed = (
        P("slab", None, "coil", "frame"),
        P("slab", None, None),
        P("coil", "slab", None),
        P("frame", "coil", "slab", None),
        P("frame", "coil", "slab"),
    )
    return jax.shard_map(
        on_device,
        mesh=mesh,
        in_specs=placed,
        out_specs=P("slab", None, "coil", "frame"),
        check_vma=False,
    )
```

```python
import math

import jax
import ml_dtypes
import numpy as np
import jax.numpy as jnp
from jax import lax
from jax.experimental import pallas as pl
from jax.experimental.pallas import tpu as pltpu
from jax.sharding import PartitionSpec as P


def dft_parts(length):
    index = np.arange(length, dtype=np.int64)
    phase = (index[:, None] * index[None, :]) % length
    angle = np.float32(2.0 * math.pi / length) * phase.astype(np.float32)
    scale = np.float32(1.0 / math.sqrt(length))
    real = (np.cos(angle.astype(np.float64)).astype(np.float32) * scale).astype(ml_dtypes.bfloat16)
    imag = (-np.sin(angle.astype(np.float64)).astype(np.float32) * scale).astype(ml_dtypes.bfloat16)
    return real, imag


def rotate_plus(values, half_width):
    return jnp.concatenate([-values[..., half_width:], values[..., :half_width]], axis=-1)


def rotate_minus(values, half_width):
    return jnp.concatenate([values[..., half_width:], -values[..., :half_width]], axis=-1)


def sens_times(sens, values, half_width):
    sens_re = sens[..., :half_width].astype(jnp.float32)
    sens_im = sens[..., half_width:].astype(jnp.float32)
    value_re = values[..., :half_width].astype(jnp.float32)
    value_im = values[..., half_width:].astype(jnp.float32)
    return jnp.concatenate(
        [sens_re * value_re - sens_im * value_im, sens_re * value_im + sens_im * value_re], axis=-1
    )


def conj_sens_times(sens, values, half_width):
    sens_re = sens[..., :half_width].astype(jnp.float32)
    sens_im = sens[..., half_width:].astype(jnp.float32)
    value_re = values[..., :half_width]
    value_im = values[..., half_width:]
    return jnp.concatenate(
        [sens_re * value_re + sens_im * value_im, sens_re * value_im - sens_im * value_re], axis=-1
    )


def precise(form, first, second):
    return jnp.einsum(form, first, second, precision=lax.Precision.HIGHEST)


PERMUTE_LIMIT = 8


def shifted(count, step):
    return [(source, (source + step) % count) for source in range(count)]


def by_sender(pieces, count, me):
    ring = jnp.stack([pieces[0]] + pieces[1:][::-1])
    doubled = jnp.concatenate([ring, ring], axis=0)
    return lax.dynamic_slice_in_dim(doubled, (count - me) % count, count, 0)


def gather_blocks(value, axis):
    count = lax.axis_size(axis)
    if count > PERMUTE_LIMIT:
        return lax.all_gather(value, axis)
    me = lax.axis_index(axis)
    pieces = [value] + [lax.ppermute(value, axis, shifted(count, step)) for step in range(1, count)]
    return by_sender(pieces, count, me)


def exchange_blocks(blocks, axis):
    count = lax.axis_size(axis)
    if count > PERMUTE_LIMIT:
        return lax.all_to_all(blocks, axis, 0, 0, tiled=True)
    me = lax.axis_index(axis)
    pieces = [lax.dynamic_index_in_dim(blocks, me, 0, keepdims=False)]
    for step in range(1, count):
        outgoing = lax.dynamic_index_in_dim(blocks, (me + step) % count, 0, keepdims=False)
        pieces.append(lax.ppermute(outgoing, axis, shifted(count, step)))
    return by_sender(pieces, count, me)


def reduce_blocks(blocks, axis):
    count = lax.axis_size(axis)
    if count > PERMUTE_LIMIT:
        return lax.psum_scatter(blocks.astype(jnp.bfloat16), axis, scatter_dimension=0).astype(jnp.float32)
    me = lax.axis_index(axis)
    total = lax.dynamic_index_in_dim(blocks, me, 0, keepdims=False)
    for step in range(1, count):
        outgoing = lax.dynamic_index_in_dim(blocks, (me + step) % count, 0, keepdims=False)
        total = total + lax.ppermute(outgoing.astype(jnp.bfloat16), axis, shifted(count, step)).astype(jnp.float32)
    return total


def swap_halves(values, half_width, negate_first):
    low = values[:, :half_width]
    high = values[:, half_width:]
    if negate_first:
        return jnp.concatenate([-high, low], axis=1)
    return jnp.concatenate([high, -low], axis=1)


def coil_terms(image_ref, sens_ref, measured_ref, sampled_ref, forward_ref, adjoint_ref, table_ref):
    coils, height, width = sens_ref.shape
    half_width = width // 2
    sens = sens_ref[...].astype(jnp.float32)
    sens_re = sens[:, :, :half_width]
    sens_im = sens[:, :, half_width:]
    image = image_ref[...].astype(jnp.float32)[None]
    image_re = image[:, :, :half_width]
    image_im = image[:, :, half_width:]
    coil = jnp.concatenate(
        [sens_re * image_re - sens_im * image_im, sens_re * image_im + sens_im * image_re], axis=2
    ).astype(jnp.bfloat16)
    half_k = jnp.dot(coil.reshape(coils * height, width), forward_ref[...], preferred_element_type=jnp.float32)
    table = table_ref[...]
    backs = []
    for coil_index in range(coils):
        one = half_k[coil_index * height:(coil_index + 1) * height].astype(jnp.bfloat16).astype(jnp.float32)
        turned = jnp.concatenate([one[:, :half_width].T, one[:, half_width:].T], axis=0).astype(jnp.bfloat16)
        parts = jnp.dot(turned, table, preferred_element_type=jnp.float32)
        kspace_re = parts[:half_width, :height] - parts[half_width:, height:]
        kspace_im = parts[:half_width, height:] + parts[half_width:, :height]
        row = pl.program_id(0) * coils + coil_index
        sampled = sampled_ref[pl.ds(row, 1), :].astype(jnp.float32)
        measured = measured_ref[coil_index].astype(jnp.float32)
        residual = jnp.concatenate(
            [
                (sampled * (kspace_re - measured[:, :half_width].T)).astype(jnp.bfloat16),
                (sampled * (kspace_im - measured[:, half_width:].T)).astype(jnp.bfloat16),
            ],
            axis=0,
        )
        parts = jnp.dot(residual, table, preferred_element_type=jnp.float32)
        back_re = (parts[:half_width, :height] + parts[half_width:, height:]).astype(jnp.bfloat16)
        back_im = (parts[half_width:, :height] - parts[:half_width, height:]).astype(jnp.bfloat16)
        backs.append(
            jnp.concatenate([back_re.astype(jnp.float32).T, back_im.astype(jnp.float32).T], axis=1).astype(
                jnp.bfloat16
            )
        )
    back_half = jnp.concatenate(backs, axis=0)
    coil_back = jnp.dot(back_half, adjoint_ref[...], preferred_element_type=jnp.float32).reshape(
        coils, height, width
    )
    back_re = coil_back[:, :, :half_width]
    back_im = coil_back[:, :, half_width:]
    term = jnp.concatenate(
        [sens_re * back_re + sens_im * back_im, sens_re * back_im - sens_im * back_re], axis=2
    )
    return jnp.sum(term, axis=0)


def coil_chain_kernel(*refs):
    groups = (len(refs) - 8) // 2
    pieces = refs[:groups]
    place_ref, sens_ref, measured_ref, sampled_ref, forward_ref, adjoint_ref, table_ref = refs[groups:groups + 7]
    own_ref = refs[groups + 7]
    send_refs = refs[groups + 8:2 * groups + 7]
    image_ref, total_ref = refs[2 * groups + 7:]
    rows = pieces[0].shape[0]
    half_width = image_ref.shape[1] // 2
    me = place_ref[0]
    step = pl.program_id(0)

    @pl.when(step == 0)
    def _():
        for block in range(groups):
            source = (me - block + groups) % groups
            value = pieces[0][...]
            for other in range(1, groups):
                value = jnp.where(source == other, pieces[other][...], value)
            image_ref[block * rows:(block + 1) * rows, :] = value

    term = coil_terms(image_ref, sens_ref, measured_ref, sampled_ref, forward_ref, adjoint_ref, table_ref)

    @pl.when(step == 0)
    def _():
        total_ref[...] = term

    @pl.when(step > 0)
    def _():
        total_ref[...] += term

    @pl.when(step == pl.num_programs(0) - 1)
    def _():
        start = pl.multiple_of(me * rows, rows)
        own_ref[...] = total_ref[pl.ds(start, rows), :]
        for shift in range(1, groups):
            start = pl.multiple_of(((me + shift) % groups) * rows, rows)
            send_refs[shift - 1][...] = total_ref[pl.ds(start, rows), :].astype(jnp.bfloat16)


def coil_chain(pieces, place, sens, measured, sampled, forward_x, adjoint_x, table_y):
    coils, height, width = sens.shape
    groups = len(pieces)
    rows = pieces[0].shape[0]
    whole = lambda c: (0, 0)
    per_coil = lambda c: (c, 0, 0)
    step_coils = 4 if coils % 4 == 0 else (2 if coils % 2 == 0 else 1)
    flops = coils * 8 * height * width * width
    return pl.pallas_call(
        coil_chain_kernel,
        out_shape=(jax.ShapeDtypeStruct((rows, width), jnp.float32),)
        + (jax.ShapeDtypeStruct((rows, width), jnp.bfloat16),) * (groups - 1),
        grid=(coils // step_coils,),
        in_specs=[pl.BlockSpec((rows, width), whole)] * groups
        + [
            pl.BlockSpec(memory_space=pltpu.SMEM),
            pl.BlockSpec((step_coils, height, width), per_coil),
            pl.BlockSpec((step_coils, height, width), per_coil),
            pl.BlockSpec((coils, height), whole),
            pl.BlockSpec((width, width), whole),
            pl.BlockSpec((width, width), whole),
            pl.BlockSpec((height, 2 * height), whole),
        ],
        out_specs=(pl.BlockSpec((rows, width), whole),) * groups,
        scratch_shapes=[pltpu.VMEM((height, width), jnp.bfloat16), pltpu.VMEM((height, width), jnp.float32)],
        compiler_params=pltpu.CompilerParams(dimension_semantics=("arbitrary",)),
        cost_estimate=pl.CostEstimate(
            flops=flops, transcendentals=0, bytes_accessed=2 * 2 * coils * height * width + 4 * height * width
        ),
    )(*pieces, place, sens, measured, sampled, forward_x, adjoint_x, table_y)


def on_device(factors, temporal, maps, kdata, masks):
    width_x = maps.shape[2] // 2
    width_y = maps.shape[1]
    rows_own = factors.shape[2]
    table_x_re, table_x_im = dft_parts(width_x)
    table_y_re, table_y_im = dft_parts(width_y)
    forward_x = jnp.asarray(np.block([[table_x_re, table_x_im], [-table_x_im, table_x_re]]))
    adjoint_x = jnp.asarray(np.block([[table_x_re, -table_x_im], [table_x_im, table_x_re]]))
    table_y = jnp.asarray(np.concatenate([table_y_re, table_y_im], axis=1))
    time_re = temporal[0]
    time_im = temporal[1]
    parts, ranks = factors.shape[:2]
    ranks_all = temporal.shape[2]
    sign = jnp.asarray(np.concatenate([np.ones((1, 1, ranks_all)), -np.ones((1, 1, ranks_all))], axis=2)
                       .astype(np.float32) * np.array([1.0, 0.0], np.float32)[:, None, None]
                       + np.array([0.0, 1.0], np.float32)[:, None, None])
    weights_in = jnp.stack(
        [
            jnp.concatenate([temporal[0], temporal[1]], axis=-1),
            jnp.concatenate([temporal[1], temporal[0]], axis=-1),
        ]
    ) * sign
    images = jnp.sum(
        weights_in[:, :, :, None, None] * factors.reshape((parts * ranks,) + factors.shape[2:])[None, None],
        axis=2,
    )
    images = jnp.transpose(images, (1, 0, 2, 3)).astype(jnp.bfloat16)
    frames_here = images.shape[0]
    width_own = images.shape[3]
    pieces_x = exchange_blocks(images, "frame")
    own_rows = jnp.transpose(pieces_x, (2, 1, 0, 3)).reshape(rows_own, 2 * width_x)
    groups = lax.axis_size("coil")
    me_c = lax.axis_index("coil")
    pieces = [own_rows] + [lax.ppermute(own_rows, "coil", shifted(groups, step)) for step in range(1, groups)]
    sampled = masks[0]
    place = jnp.reshape(me_c, (1,)).astype(jnp.int32)
    measured = kdata[0]
    own_total, *outgoing = coil_chain(
        pieces, place, maps, measured, sampled, forward_x, adjoint_x, table_y
    )
    own_share = own_total
    for step in range(1, groups):
        own_share = own_share + lax.ppermute(outgoing[step - 1], "coil", shifted(groups, step)).astype(jnp.float32)
    outgoing = jnp.transpose(
        own_share.reshape(rows_own, 2, frames_here, width_own), (2, 0, 1, 3)
    ).astype(jnp.bfloat16)
    returned = exchange_blocks(outgoing, "frame").astype(jnp.float32)
    late = lax.optimization_barrier(temporal)
    weights = jnp.stack(
        [jnp.stack([late[0].T, late[1].T], axis=2), jnp.stack([-late[1].T, late[0].T], axis=2)], axis=0
    )
    step_weights = -0.5 * weights
    gradient = None
    for frame in range(returned.shape[0]):
        for part_in in range(2):
            term = step_weights[:, :, frame, part_in, None, None] * returned[frame, :, part_in][None, None]
            gradient = term if gradient is None else gradient + term
    return factors + gradient


def solution(mesh):
    placed = (
        P("slab", None, "coil", "frame"),
        P("slab", None, None),
        P("coil", "slab", None),
        P("frame", "coil", "slab", None),
        P("frame", "coil", "slab"),
    )
    return jax.shard_map(
        on_device,
        mesh=mesh,
        in_specs=placed,
        out_specs=P("slab", None, "coil", "frame"),
        check_vma=False,
    )
```

```python
import math

import jax
import ml_dtypes
import numpy as np
import jax.numpy as jnp
from jax import lax
from jax.experimental import pallas as pl
from jax.experimental.pallas import tpu as pltpu
from jax.sharding import PartitionSpec as P


def dft_parts(length):
    index = np.arange(length, dtype=np.int64)
    phase = (index[:, None] * index[None, :]) % length
    angle = np.float32(2.0 * math.pi / length) * phase.astype(np.float32)
    scale = np.float32(1.0 / math.sqrt(length))
    real = (np.cos(angle.astype(np.float64)).astype(np.float32) * scale).astype(ml_dtypes.bfloat16)
    imag = (-np.sin(angle.astype(np.float64)).astype(np.float32) * scale).astype(ml_dtypes.bfloat16)
    return real, imag


def rotate_plus(values, half_width):
    return jnp.concatenate([-values[..., half_width:], values[..., :half_width]], axis=-1)


def rotate_minus(values, half_width):
    return jnp.concatenate([values[..., half_width:], -values[..., :half_width]], axis=-1)


def sens_times(sens, values, half_width):
    sens_re = sens[..., :half_width].astype(jnp.float32)
    sens_im = sens[..., half_width:].astype(jnp.float32)
    value_re = values[..., :half_width].astype(jnp.float32)
    value_im = values[..., half_width:].astype(jnp.float32)
    return jnp.concatenate(
        [sens_re * value_re - sens_im * value_im, sens_re * value_im + sens_im * value_re], axis=-1
    )


def conj_sens_times(sens, values, half_width):
    sens_re = sens[..., :half_width].astype(jnp.float32)
    sens_im = sens[..., half_width:].astype(jnp.float32)
    value_re = values[..., :half_width]
    value_im = values[..., half_width:]
    return jnp.concatenate(
        [sens_re * value_re + sens_im * value_im, sens_re * value_im - sens_im * value_re], axis=-1
    )


def precise(form, first, second):
    return jnp.einsum(form, first, second, precision=lax.Precision.HIGHEST)


PERMUTE_LIMIT = 8


def shifted(count, step):
    return [(source, (source + step) % count) for source in range(count)]


def by_sender(pieces, count, me):
    ring = jnp.stack([pieces[0]] + pieces[1:][::-1])
    doubled = jnp.concatenate([ring, ring], axis=0)
    return lax.dynamic_slice_in_dim(doubled, (count - me) % count, count, 0)


def gather_blocks(value, axis):
    count = lax.axis_size(axis)
    if count > PERMUTE_LIMIT:
        return lax.all_gather(value, axis)
    me = lax.axis_index(axis)
    pieces = [value] + [lax.ppermute(value, axis, shifted(count, step)) for step in range(1, count)]
    return by_sender(pieces, count, me)


def exchange_blocks(blocks, axis):
    count = lax.axis_size(axis)
    if count > PERMUTE_LIMIT:
        return lax.all_to_all(blocks, axis, 0, 0, tiled=True)
    me = lax.axis_index(axis)
    pieces = [lax.dynamic_index_in_dim(blocks, me, 0, keepdims=False)]
    for step in range(1, count):
        outgoing = lax.dynamic_index_in_dim(blocks, (me + step) % count, 0, keepdims=False)
        pieces.append(lax.ppermute(outgoing, axis, shifted(count, step)))
    return by_sender(pieces, count, me)


def reduce_blocks(blocks, axis):
    count = lax.axis_size(axis)
    if count > PERMUTE_LIMIT:
        return lax.psum_scatter(blocks.astype(jnp.bfloat16), axis, scatter_dimension=0).astype(jnp.float32)
    me = lax.axis_index(axis)
    total = lax.dynamic_index_in_dim(blocks, me, 0, keepdims=False)
    for step in range(1, count):
        outgoing = lax.dynamic_index_in_dim(blocks, (me + step) % count, 0, keepdims=False)
        total = total + lax.ppermute(outgoing.astype(jnp.bfloat16), axis, shifted(count, step)).astype(jnp.float32)
    return total


def swap_halves(values, half_width, negate_first):
    low = values[:, :half_width]
    high = values[:, half_width:]
    if negate_first:
        return jnp.concatenate([-high, low], axis=1)
    return jnp.concatenate([high, -low], axis=1)


def coil_terms(image_ref, sens_ref, measured_ref, sampled_ref, forward_ref, adjoint_ref, table_ref):
    coils, height, width = sens_ref.shape
    half_width = width // 2
    sens = sens_ref[...].astype(jnp.float32)
    sens_re = sens[:, :, :half_width]
    sens_im = sens[:, :, half_width:]
    image = image_ref[...].astype(jnp.float32)[None]
    image_re = image[:, :, :half_width]
    image_im = image[:, :, half_width:]
    coil = jnp.concatenate(
        [sens_re * image_re - sens_im * image_im, sens_re * image_im + sens_im * image_re], axis=2
    ).astype(jnp.bfloat16)
    half_k = jnp.dot(coil.reshape(coils * height, width), forward_ref[...], preferred_element_type=jnp.float32)
    table = table_ref[...]
    backs = []
    for coil_index in range(coils):
        one = half_k[coil_index * height:(coil_index + 1) * height].astype(jnp.bfloat16).astype(jnp.float32)
        turned = jnp.concatenate([one[:, :half_width].T, one[:, half_width:].T], axis=0).astype(jnp.bfloat16)
        parts = jnp.dot(turned, table, preferred_element_type=jnp.float32)
        kspace_re = parts[:half_width, :height] - parts[half_width:, height:]
        kspace_im = parts[:half_width, height:] + parts[half_width:, :height]
        row = pl.program_id(0) * coils + coil_index
        sampled = sampled_ref[pl.ds(row, 1), :].astype(jnp.float32)
        measured = measured_ref[coil_index].astype(jnp.float32)
        residual = jnp.concatenate(
            [
                (sampled * (kspace_re - measured[:, :half_width].T)).astype(jnp.bfloat16),
                (sampled * (kspace_im - measured[:, half_width:].T)).astype(jnp.bfloat16),
            ],
            axis=0,
        )
        parts = jnp.dot(residual, table, preferred_element_type=jnp.float32)
        back_re = (parts[:half_width, :height] + parts[half_width:, height:]).astype(jnp.bfloat16)
        back_im = (parts[half_width:, :height] - parts[:half_width, height:]).astype(jnp.bfloat16)
        backs.append(
            jnp.concatenate([back_re.astype(jnp.float32).T, back_im.astype(jnp.float32).T], axis=1).astype(
                jnp.bfloat16
            )
        )
    back_half = jnp.concatenate(backs, axis=0)
    coil_back = jnp.dot(back_half, adjoint_ref[...], preferred_element_type=jnp.float32).reshape(
        coils, height, width
    )
    back_re = coil_back[:, :, :half_width]
    back_im = coil_back[:, :, half_width:]
    term = jnp.concatenate(
        [sens_re * back_re + sens_im * back_im, sens_re * back_im - sens_im * back_re], axis=2
    )
    return jnp.sum(term, axis=0)


def coil_chain_kernel(*refs):
    groups = (len(refs) - 8) // 2
    pieces = refs[:groups]
    place_ref, sens_ref, measured_ref, sampled_ref, forward_ref, adjoint_ref, table_ref = refs[groups:groups + 7]
    own_ref = refs[groups + 7]
    send_refs = refs[groups + 8:2 * groups + 7]
    image_ref, total_ref = refs[2 * groups + 7:]
    rows = pieces[0].shape[0]
    half_width = image_ref.shape[1] // 2
    me = place_ref[0]
    step = pl.program_id(0)

    @pl.when(step == 0)
    def _():
        for block in range(groups):
            source = (me - block + groups) % groups
            value = pieces[0][...]
            for other in range(1, groups):
                value = jnp.where(source == other, pieces[other][...], value)
            image_ref[block * rows:(block + 1) * rows, :] = value

    term = coil_terms(image_ref, sens_ref, measured_ref, sampled_ref, forward_ref, adjoint_ref, table_ref)

    @pl.when(step == 0)
    def _():
        total_ref[...] = term

    @pl.when(step > 0)
    def _():
        total_ref[...] += term

    @pl.when(step == pl.num_programs(0) - 1)
    def _():
        start = pl.multiple_of(me * rows, rows)
        own_ref[...] = total_ref[pl.ds(start, rows), :]
        for shift in range(1, groups):
            start = pl.multiple_of(((me + shift) % groups) * rows, rows)
            send_refs[shift - 1][...] = total_ref[pl.ds(start, rows), :].astype(jnp.bfloat16)


def coil_chain(pieces, place, sens, measured, sampled, forward_x, adjoint_x, table_y):
    coils, height, width = sens.shape
    groups = len(pieces)
    rows = pieces[0].shape[0]
    whole = lambda c: (0, 0)
    per_coil = lambda c: (c, 0, 0)
    step_coils = 4 if coils % 4 == 0 else (2 if coils % 2 == 0 else 1)
    flops = coils * 8 * height * width * width
    return pl.pallas_call(
        coil_chain_kernel,
        out_shape=(jax.ShapeDtypeStruct((rows, width), jnp.float32),)
        + (jax.ShapeDtypeStruct((rows, width), jnp.bfloat16),) * (groups - 1),
        grid=(coils // step_coils,),
        in_specs=[pl.BlockSpec((rows, width), whole)] * groups
        + [
            pl.BlockSpec(memory_space=pltpu.SMEM),
            pl.BlockSpec((step_coils, height, width), per_coil),
            pl.BlockSpec((step_coils, height, width), per_coil),
            pl.BlockSpec((coils, height), whole),
            pl.BlockSpec((width, width), whole, pipeline_mode=pl.Buffered(1)),
            pl.BlockSpec((width, width), whole, pipeline_mode=pl.Buffered(1)),
            pl.BlockSpec((height, 2 * height), whole, pipeline_mode=pl.Buffered(1)),
        ],
        out_specs=(pl.BlockSpec((rows, width), whole),) * groups,
        scratch_shapes=[pltpu.VMEM((height, width), jnp.bfloat16), pltpu.VMEM((height, width), jnp.float32)],
        compiler_params=pltpu.CompilerParams(dimension_semantics=("arbitrary",)),
        cost_estimate=pl.CostEstimate(
            flops=flops, transcendentals=0, bytes_accessed=2 * 2 * coils * height * width + 4 * height * width
        ),
    )(*pieces, place, sens, measured, sampled, forward_x, adjoint_x, table_y)


def on_device(factors, temporal, maps, kdata, masks):
    width_x = maps.shape[2] // 2
    width_y = maps.shape[1]
    rows_own = factors.shape[2]
    table_x_re, table_x_im = dft_parts(width_x)
    table_y_re, table_y_im = dft_parts(width_y)
    forward_x = jnp.asarray(np.block([[table_x_re, table_x_im], [-table_x_im, table_x_re]]))
    adjoint_x = jnp.asarray(np.block([[table_x_re, -table_x_im], [table_x_im, table_x_re]]))
    table_y = jnp.asarray(np.concatenate([table_y_re, table_y_im], axis=1))
    time_re = temporal[0]
    time_im = temporal[1]
    parts, ranks = factors.shape[:2]
    weights_in = jnp.stack(
        [
            jnp.concatenate([temporal[0], -temporal[1]], axis=-1),
            jnp.concatenate([temporal[1], temporal[0]], axis=-1),
        ]
    )
    images = jnp.sum(
        weights_in[:, :, :, None, None] * factors.reshape((parts * ranks,) + factors.shape[2:])[None, None],
        axis=2,
    )
    images = jnp.transpose(images, (1, 0, 2, 3)).astype(jnp.bfloat16)
    frames_here = images.shape[0]
    width_own = images.shape[3]
    pieces_x = exchange_blocks(images, "frame")
    own_rows = jnp.transpose(pieces_x, (2, 1, 0, 3)).reshape(rows_own, 2 * width_x)
    groups = lax.axis_size("coil")
    me_c = lax.axis_index("coil")
    pieces = [own_rows] + [lax.ppermute(own_rows, "coil", shifted(groups, step)) for step in range(1, groups)]
    sampled = masks[0]
    place = jnp.reshape(me_c, (1,)).astype(jnp.int32)
    measured = kdata[0]
    own_total, *outgoing = coil_chain(
        pieces, place, maps, measured, sampled, forward_x, adjoint_x, table_y
    )
    own_share = own_total
    for step in range(1, groups):
        own_share = own_share + lax.ppermute(outgoing[step - 1], "coil", shifted(groups, step)).astype(jnp.float32)
    outgoing = jnp.transpose(
        own_share.reshape(rows_own, 2, frames_here, width_own), (2, 0, 1, 3)
    ).astype(jnp.bfloat16)
    returned = exchange_blocks(outgoing, "frame").astype(jnp.float32)
    late = lax.optimization_barrier(temporal)
    weights = jnp.stack(
        [jnp.stack([late[0].T, late[1].T], axis=2), jnp.stack([-late[1].T, late[0].T], axis=2)], axis=0
    )
    step_weights = -0.5 * weights
    gradient = None
    for frame in range(returned.shape[0]):
        for part_in in range(2):
            term = step_weights[:, :, frame, part_in, None, None] * returned[frame, :, part_in][None, None]
            gradient = term if gradient is None else gradient + term
    return factors + gradient


def solution(mesh):
    placed = (
        P("slab", None, "coil", "frame"),
        P("slab", None, None),
        P("coil", "slab", None),
        P("frame", "coil", "slab", None),
        P("frame", "coil", "slab"),
    )
    return jax.shard_map(
        on_device,
        mesh=mesh,
        in_specs=placed,
        out_specs=P("slab", None, "coil", "frame"),
        check_vma=False,
    )
```
